128 devices in a mesh: wave: 16 (over y, z_lo, core), pole: 8 (over x, z_hi).
Axes of the slice: x: 4, y: 4, z: 4 (z_hi: 2, z_lo: 2; z = z_hi * 2 + z_lo), core: 2. Of those that a mesh axis runs over, the one named last changes fastest.
Arguments:
- grid: float32 [6, 256, 3072], P(None, None, 'wave'), may hold values from -6 to 6
- legendre: bfloat16 [256, 2, 1536, 1024], P('wave', None, None, 'pole'), may hold values from -0.15625 to 0.15625
- wave_table: int32 [256], replicated, may hold values from 0 to 255, each once
- pole_table: float32 [4, 64], replicated, may hold values from -1.5 to 2.5, as said below
- pole_index: int32 [32], replicated, may hold values from 0 to 63
Outputs:
- next_state: float32 [6, 2, 256, 1024], P(None, None, 'wave', 'pole')
The draws below stay inside these ranges and needn't reach their ends.
Inputs may be any that keep to these rules, and one draw needn't show every extreme that they name: Slot s holds zonal wavenumber wave_table[s], every wavenumber of 0 to 255 once; row s of legendre belongs to it. `pole_table`: shift real parts lie in 1.5 to 2.5, shift imaginary parts in -1.5 to 1.5, weights in -1.2 to 1.2.
All inputs are finite; a program needn't handle non-finite values.
Results may differ from the reference program's by a relative error of at most 0.0003.
Values sent between devices are 32-bit elements; how exact they have to be, the bound alone decides.
No kernel may reach another device: no remote copies, remote signals or barrier semaphores. Data moves between devices by JAX's collectives and lax.ppermute only.
A program may use at most 128 MiB of HBM per device.

```python
import jax
import jax.numpy as jnp
from jax import lax

NLAT = 3072
NHALF = 1536
NDEG_PAR = 1024
M_ALL = 256
NSOLVE = 32
NTABLE = 64
SWEEPS = 8


def draw_pole_table(key, part):
    first, second, third, fourth = jax.random.split(key, 4)
    ushift = jax.random.uniform(first, (NTABLE,), jnp.float32)
    vshift = jax.random.uniform(second, (NTABLE,), jnp.float32)
    shift_re = 1.5 + ushift
    shift_im = 3.0 * vshift - 1.5
    weight_re = jnp.clip(0.3 * jax.random.normal(third, (NTABLE,), jnp.float32), -1.2, 1.2)
    weight_im = jnp.clip(0.3 * jax.random.normal(fourth, (NTABLE,), jnp.float32), -1.2, 1.2)
    return jnp.stack([shift_re, shift_im, weight_re, weight_im]).astype(jnp.float32)


def touch_ends(entries, stream_key, least, high):
    spot = [jax.random.randint(jax.random.fold_in(stream_key, axis), (), 0, length) for axis, length in enumerate(entries.shape)]
    widest = entries.shape.index(max(entries.shape))
    neighbour = spot[:widest] + [(spot[widest] + 1) % entries.shape[widest]] + spot[widest + 1:]
    return entries.at[tuple(spot)].set(least).at[tuple(neighbour)].set(high)


def block_levels(own_key, dims, cuts, least, top_value):
    gain, own = 1.0, jax.random.fold_in(own_key, 6)
    for dim, blocks in cuts:
        heights = jnp.exp(jax.random.uniform(jax.random.fold_in(own, dim), (blocks,), jnp.float32, least / len(cuts), top_value / len(cuts)))
        gain = gain * jnp.repeat(heights, dims[dim] // blocks).reshape([-1 if axis == dim else 1 for axis in range(len(dims))])
    return gain


def bell_draw(key, dims, deviation, most, pieces=(), held_as=jnp.bfloat16):
    level = block_levels(key, dims, pieces, -0.22, 0.18) if pieces else 1.0
    array = jax.random.normal(key, dims, jnp.float32) * deviation * level
    return jnp.minimum(jnp.maximum(array, -most), most).astype(held_as)


def setup_inputs(seed: int = 0) -> dict:
    splits = jax.random.split(jax.random.key(seed), 6)
    return {
        "grid": bell_draw(splits[0], (6, M_ALL, NLAT), 1.0, 6.0, ((2, 16),), jnp.float32),
        "legendre": bell_draw(splits[1], (M_ALL, 2, NHALF, NDEG_PAR), NHALF ** -0.5, 0.15625, ((0, 16), (3, 8))),
        "wave_table": jax.random.permutation(splits[2], M_ALL).astype(jnp.int32),
        "pole_table": draw_pole_table(jax.random.fold_in(splits[5], 71), 0),
        "pole_index": touch_ends(jax.random.randint(splits[4], (NSOLVE,), 0, NTABLE), jax.random.fold_in(splits[4], 1), 0, NTABLE - 1).astype(jnp.int32),
    }


coriolis_step = 1.2
gravity_step = 0.0008

def split_high(values):
    upper_part = values.astype(jnp.bfloat16)
    kept = lax.optimization_barrier(upper_part)
    lower_part = (values - kept.astype(jnp.float32)).astype(jnp.bfloat16)
    return (upper_part, lower_part)

def coefficients(wavenum, start, count):
    index = (start + jnp.arange(count, dtype=jnp.int32)).astype(jnp.float32)
    parity = jnp.arange(2, dtype=jnp.int32).astype(jnp.float32)
    order = (2.0 * index[None, :] + parity[:, None])[:, None, :]
    wave = wavenum[None, :, None]
    degree = wave + order
    product = degree * (degree + 1.0)
    rossby = coriolis_step * wave / jnp.maximum(product, 2.0)
    gravity = gravity_step * jnp.sqrt(product)
    e_lo = jnp.sqrt(order * (2.0 * wave + order) / jnp.maximum(4.0 * degree * degree - 1.0, 1.0))
    after = order + 1.0
    upper_deg = degree + 1.0
    e_hi = jnp.sqrt(after * (2.0 * wave + after) / jnp.maximum(4.0 * upper_deg * upper_deg - 1.0, 1.0))
    return (e_lo, e_hi, rossby, gravity)

def cmul(are, aim, bre, bim):
    return (are * bre - aim * bim, are * bim + aim * bre)

def zero_extend(field):
    return jnp.pad(field, ((0, 0), (0, 0), (0, 0), (0, 0), (1, 1)))

def solve(spectra, coef, shifts, extend):
    e_lo, e_hi, rossby, gravity = coef
    count = spectra.shape[3]
    shift_re = shifts[:, 0][:, None, None, None]
    shift_im = shifts[:, 1][:, None, None, None]
    weight_re = shifts[:, 2][:, None, None, None]
    weight_im = shifts[:, 3][:, None, None, None]
    z0r, z0i = (spectra[0][None], spectra[1][None])
    d0r, d0i = (spectra[2][None], spectra[3][None])
    h0r, h0i = (spectra[4][None], spectra[5][None])
    b_re = shift_re + 0.0 * rossby[None]
    b_im = shift_im + rossby[None]
    b_mag = b_re * b_re + b_im * b_im
    inv_re, inv_im = (b_re / b_mag, -b_im / b_mag)
    det_re, det_im = cmul(b_re, b_im, shift_re, shift_im)
    det_re = det_re + gravity[None] * gravity[None]
    det_mag = det_re * det_re + det_im * det_im
    dinv_re, dinv_im = (det_re / det_mag, -det_im / det_mag)
    grav = gravity[None]
    hb_re, hb_im = cmul(b_re, b_im, h0r, h0i)
    zr, zi, dr, di, hr, hi = (z0r, z0i, d0r, d0i, h0r, h0i)
    for sweep in range(SWEEPS):
        if sweep == 0:
            rzr, rzi, rdr, rdi = (z0r, z0i, d0r, d0i)
        else:
            both = jnp.stack([zr, zi, dr, di], axis=0)
            ext = extend(both)
            lower = jnp.stack([ext[:, :, 1, :, 0:count], ext[:, :, 0, :, 1:count + 1]], axis=2)
            upper = jnp.stack([ext[:, :, 1, :, 1:count + 1], ext[:, :, 0, :, 2:count + 2]], axis=2)
            near = e_lo * lower + e_hi * upper
            rzr = z0r - coriolis_step * near[2]
            rzi = z0i - coriolis_step * near[3]
            rdr = d0r + coriolis_step * near[0]
            rdi = d0i + coriolis_step * near[1]
        zr, zi = cmul(rzr, rzi, inv_re, inv_im)
        nd_re, nd_im = cmul(shift_re, shift_im, rdr, rdi)
        nd_re = nd_re + grav * h0r
        nd_im = nd_im + grav * h0i
        nh_re = hb_re - grav * rdr
        nh_im = hb_im - grav * rdi
        dr, di = cmul(nd_re, nd_im, dinv_re, dinv_im)
        hr, hi = cmul(nh_re, nh_im, dinv_re, dinv_im)
    parts = []
    for field_re, field_im in ((zr, zi), (dr, di), (hr, hi)):
        out_re, out_im = cmul(weight_re, weight_im, field_re, field_im)
        parts.append(lax.optimization_barrier(jnp.sum(out_re, axis=0)))
        parts.append(lax.optimization_barrier(jnp.sum(out_im, axis=0)))
    return jnp.stack(parts, axis=0)

def reference(grid, legendre, wave_table, pole_table, pole_index):
    columns = jnp.take(grid, wave_table, axis=1)
    half = columns.shape[2] // 2
    north = columns[:, :, :half]
    south = columns[:, :, half:]
    parts = jnp.stack([north + south, north - south], axis=1)
    high, low = split_high(parts)
    high_slots = jnp.moveaxis(high, 2, 0)
    low_slots = jnp.moveaxis(low, 2, 0)

    def analyse_one(trio):
        leg_one, high_one, low_one = trio
        leg_wide = leg_one.astype(jnp.float32)
        first = jnp.einsum('plk,cpl->cpk', leg_wide, high_one.astype(jnp.float32), precision=lax.Precision.HIGHEST)
        second = jnp.einsum('plk,cpl->cpk', leg_wide, low_one.astype(jnp.float32), precision=lax.Precision.HIGHEST)
        return first + second
    out = lax.map(analyse_one, (legendre, high_slots, low_slots))
    spectra = jnp.transpose(out, (1, 2, 0, 3))
    coef = coefficients(wave_table.astype(jnp.float32), 0, spectra.shape[3])
    shifts = jnp.transpose(pole_table[:, pole_index])

    def accumulate(total, row):
        return (total + solve(spectra, coef, row[None], zero_extend), None)
    total, unused = lax.scan(accumulate, jnp.zeros(spectra.shape, jnp.float32), shifts)
    return total
```

```python
import jax
import jax.numpy as jnp
from jax import lax
from jax.sharding import PartitionSpec as P

SWEEPS = 8
HALO = 8


coriolis_step = 1.2
gravity_step = 0.0008


def split_high(values):
    upper_part = values.astype(jnp.bfloat16)
    kept = lax.optimization_barrier(upper_part)
    lower_part = (values - kept.astype(jnp.float32)).astype(jnp.bfloat16)
    return (upper_part, lower_part)


def coefficients(wavenum, start, count, total):
    index = (start + jnp.arange(count, dtype=jnp.int32)).astype(jnp.float32)
    parity = jnp.arange(2, dtype=jnp.int32).astype(jnp.float32)
    order = (2.0 * index[None, :] + parity[:, None])[:, None, :]
    inside = (order >= 0.0) & (order < 2.0 * total)
    upper_inside = (order >= 0.0) & (order + 1.0 < 2.0 * total)
    order = jnp.clip(order, 0.0, 2.0 * total - 1.0)
    wave = wavenum[None, :, None]
    degree = wave + order
    product = degree * (degree + 1.0)
    rossby = coriolis_step * wave / jnp.maximum(product, 2.0)
    gravity = gravity_step * jnp.sqrt(product)
    e_lo = jnp.sqrt(order * (2.0 * wave + order) / jnp.maximum(4.0 * degree * degree - 1.0, 1.0))
    after = order + 1.0
    upper_deg = degree + 1.0
    e_hi = jnp.sqrt(
        after * (2.0 * wave + after) / jnp.maximum(4.0 * upper_deg * upper_deg - 1.0, 1.0)
    )
    e_lo = jnp.where(inside, e_lo, 0.0)
    e_hi = jnp.where(upper_inside, e_hi, 0.0)
    return (e_lo, e_hi, rossby, gravity)


def cmul(are, aim, bre, bim):
    return (are * bre - aim * bim, are * bim + aim * bre)


def zero_extend(field):
    return jnp.pad(field, ((0, 0), (0, 0), (0, 0), (0, 0), (1, 1)))


def solve(spectra, coef, shifts, extend):
    e_lo, e_hi, rossby, gravity = coef
    count = spectra.shape[3]
    shift_re = shifts[:, 0][:, None, None, None]
    shift_im = shifts[:, 1][:, None, None, None]
    weight_re = shifts[:, 2][:, None, None, None]
    weight_im = shifts[:, 3][:, None, None, None]
    z0r, z0i = (spectra[0][None], spectra[1][None])
    d0r, d0i = (spectra[2][None], spectra[3][None])
    h0r, h0i = (spectra[4][None], spectra[5][None])
    b_re = shift_re + 0.0 * rossby[None]
    b_im = shift_im + rossby[None]
    b_mag = b_re * b_re + b_im * b_im
    inv_re, inv_im = (b_re / b_mag, -b_im / b_mag)
    det_re, det_im = cmul(b_re, b_im, shift_re, shift_im)
    det_re = det_re + gravity[None] * gravity[None]
    det_mag = det_re * det_re + det_im * det_im
    dinv_re, dinv_im = (det_re / det_mag, -det_im / det_mag)
    grav = gravity[None]
    hb_re, hb_im = cmul(b_re, b_im, h0r, h0i)
    zr, zi, dr, di, hr, hi = (z0r, z0i, d0r, d0i, h0r, h0i)
    for sweep in range(SWEEPS):
        if sweep == 0:
            rzr, rzi, rdr, rdi = (z0r, z0i, d0r, d0i)
        else:
            both = jnp.stack([zr, zi, dr, di], axis=0)
            ext = extend(both)
            lower = jnp.stack([ext[:, :, 1, :, 0:count], ext[:, :, 0, :, 1 : count + 1]], axis=2)
            upper = jnp.stack(
                [ext[:, :, 1, :, 1 : count + 1], ext[:, :, 0, :, 2 : count + 2]], axis=2
            )
            near = e_lo * lower + e_hi * upper
            rzr = z0r - coriolis_step * near[2]
            rzi = z0i - coriolis_step * near[3]
            rdr = d0r + coriolis_step * near[0]
            rdi = d0i + coriolis_step * near[1]
        zr, zi = cmul(rzr, rzi, inv_re, inv_im)
        nd_re, nd_im = cmul(shift_re, shift_im, rdr, rdi)
        nd_re = nd_re + grav * h0r
        nd_im = nd_im + grav * h0i
        nh_re = hb_re - grav * rdr
        nh_im = hb_im - grav * rdi
        dr, di = cmul(nd_re, nd_im, dinv_re, dinv_im)
        hr, hi = cmul(nh_re, nh_im, dinv_re, dinv_im)
    parts = []
    for field_re, field_im in ((zr, zi), (dr, di), (hr, hi)):
        out_re, out_im = cmul(weight_re, weight_im, field_re, field_im)
        parts.append(jnp.sum(out_re, axis=0))
        parts.append(jnp.sum(out_im, axis=0))
    return jnp.stack(parts, axis=0)


def lookup(pole_table, chosen):
    columns = jnp.arange(pole_table.shape[1], dtype=jnp.int32)
    onehot = (chosen[:, None] == columns[None, :]).astype(jnp.float32)
    return jnp.dot(onehot, jnp.transpose(pole_table), precision=lax.Precision.HIGHEST)


def shards(grid, legendre, wave_table, pole_table, pole_index):
    slots = legendre.shape[0]
    local_k = legendre.shape[3]
    lat_rows = grid.shape[2]
    wave_count = lax.axis_size("wave")
    half_count = wave_count // 2
    columns = jnp.take(grid, wave_table, axis=1)
    regrouped = lax.all_to_all(columns[None], "wave", split_axis=2, concat_axis=0, tiled=True)
    north = regrouped[:half_count]
    south = regrouped[half_count:]
    parts = jnp.stack([north + south, north - south], axis=0)
    high, low = split_high(parts)
    leg_blocks = legendre.reshape(slots, 2, half_count, lat_rows, local_k)
    first = jnp.einsum("mpwlk,pwcml->cpmk", leg_blocks, high, preferred_element_type=jnp.float32)
    second = jnp.einsum("mpwlk,pwcml->cpmk", leg_blocks, low, preferred_element_type=jnp.float32)
    spectra = first + second
    own_waves = lax.dynamic_slice_in_dim(wave_table, lax.axis_index("wave") * slots, slots).astype(
        jnp.float32
    )
    pole_count = lax.axis_size("pole")
    pole_pos = lax.axis_index("pole")
    rightward = [(i, i + 1) for i in range(pole_count - 1)]
    leftward = [(i + 1, i) for i in range(pole_count - 1)]
    left_halo = lax.ppermute(spectra[..., local_k - HALO :], "pole", rightward)
    right_halo = lax.ppermute(spectra[..., :HALO], "pole", leftward)
    wide = jnp.concatenate([left_halo, spectra, right_halo], axis=3)
    coef = coefficients(own_waves, pole_pos * local_k - HALO, local_k + 2 * HALO, local_k * pole_count)
    terms = solve(wide, coef, lookup(pole_table, pole_index), zero_extend)
    return terms[..., HALO : HALO + local_k]


def solution(mesh):
    in_specs = (P(None, None, "wave"), P("wave", None, None, "pole"), P(), P(), P())
    out_specs = P(None, None, "wave", "pole")
    return jax.shard_map(shards, mesh=mesh, in_specs=in_specs, out_specs=out_specs, check_vma=False)
```

```python
import jax
import jax.numpy as jnp
from jax import lax
from jax.experimental import pallas as pl
from jax.experimental.pallas import tpu as pltpu
from jax.sharding import PartitionSpec as P

SWEEPS = 8
HALO = 8
RING = 256
CHUNK = 8


coriolis_step = 1.2
gravity_step = 0.0008


def split_high(values):
    upper_part = values.astype(jnp.bfloat16)
    kept = lax.optimization_barrier(upper_part)
    lower_part = (values - kept.astype(jnp.float32)).astype(jnp.bfloat16)
    return (upper_part, lower_part)


def coefficients(wavenum, base, width, total):
    lane = jnp.arange(RING, dtype=jnp.int32)
    index = jnp.where(lane >= RING - HALO, base + lane - RING, base + lane)
    inside = ((lane < width + HALO) | (lane >= RING - HALO)) & (index >= 0) & (index < total)
    index = jnp.clip(index, 0, total - 1).astype(jnp.float32)
    parity = jnp.arange(2, dtype=jnp.int32).astype(jnp.float32)
    order = (2.0 * index[None, :] + parity[:, None])[:, None, :]
    upper_inside = inside[None, None, :] & (order + 1.0 < 2.0 * total)
    wave = wavenum[None, :, None]
    degree = wave + order
    product = degree * (degree + 1.0)
    rossby = coriolis_step * wave / jnp.maximum(product, 2.0)
    gravity = gravity_step * jnp.sqrt(product)
    e_lo = jnp.sqrt(order * (2.0 * wave + order) / jnp.maximum(4.0 * degree * degree - 1.0, 1.0))
    after = order + 1.0
    upper_deg = degree + 1.0
    e_hi = jnp.sqrt(
        after * (2.0 * wave + after) / jnp.maximum(4.0 * upper_deg * upper_deg - 1.0, 1.0)
    )
    e_lo = jnp.where(inside[None, None, :], e_lo, 0.0)
    e_hi = jnp.where(upper_inside, e_hi, 0.0)
    return jnp.stack([e_lo, e_hi, rossby, gravity], axis=0)


def pole_kernel(poles_ref, spec_ref, coef_ref, out_ref):
    npoles = poles_ref.shape[1]
    rows = spec_ref.shape[2]
    lanes = spec_ref.shape[3]
    width = out_ref.shape[3]
    out_ref[...] = jnp.zeros(out_ref.shape, jnp.float32)

    def one_pole(q, carry):
        a_re = poles_ref[0, q]
        a_im = poles_ref[1, q]
        w_re = poles_ref[2, q]
        w_im = poles_ref[3, q]
        for r0 in range(0, rows, CHUNK):
            sl = pl.ds(r0, CHUNK)

            def ld(ref, i, p):
                return ref[i, p, sl, :]

            def near(x):
                n0 = ld(coef_ref, 0, 0) * pltpu.roll(x[1], 1, 1) + ld(coef_ref, 1, 0) * x[1]
                n1 = ld(coef_ref, 0, 1) * x[0] + ld(coef_ref, 1, 1) * pltpu.roll(x[0], lanes - 1, 1)
                return (n0, n1)

            inv, dinv, hb = [], [], []
            for p in range(2):
                grav = ld(coef_ref, 3, p)
                b_im = a_im + ld(coef_ref, 2, p)
                b_mag = a_re * a_re + b_im * b_im
                inv.append((a_re / b_mag, -b_im / b_mag))
                det_re = a_re * a_re - b_im * a_im + grav * grav
                det_im = a_re * a_im + b_im * a_re
                det_mag = det_re * det_re + det_im * det_im
                dinv.append((det_re / det_mag, -det_im / det_mag))
                h0r = ld(spec_ref, 4, p)
                h0i = ld(spec_ref, 5, p)
                hb.append((a_re * h0r - b_im * h0i, a_re * h0i + b_im * h0r))
            zr = zi = dr = di = hr = hi = None
            for sweep in range(SWEEPS):
                if sweep > 0:
                    nzr, nzi, ndr, ndi = near(zr), near(zi), near(dr), near(di)
                zr, zi, dr, di, hr, hi = [], [], [], [], [], []
                for p in range(2):
                    if sweep == 0:
                        rzr, rzi = ld(spec_ref, 0, p), ld(spec_ref, 1, p)
                        rdr, rdi = ld(spec_ref, 2, p), ld(spec_ref, 3, p)
                    else:
                        rzr = ld(spec_ref, 0, p) - coriolis_step * ndr[p]
                        rzi = ld(spec_ref, 1, p) - coriolis_step * ndi[p]
                        rdr = ld(spec_ref, 2, p) + coriolis_step * nzr[p]
                        rdi = ld(spec_ref, 3, p) + coriolis_step * nzi[p]
                    z_re, z_im = cmul(rzr, rzi, inv[p][0], inv[p][1])
                    zr.append(z_re)
                    zi.append(z_im)
                    grav = ld(coef_ref, 3, p)
                    nd_re, nd_im = cmul(a_re, a_im, rdr, rdi)
                    nd_re = nd_re + grav * ld(spec_ref, 4, p)
                    nd_im = nd_im + grav * ld(spec_ref, 5, p)
                    d_re, d_im = cmul(nd_re, nd_im, dinv[p][0], dinv[p][1])
                    dr.append(d_re)
                    di.append(d_im)
                    if sweep == SWEEPS - 1:
                        nh_re = hb[p][0] - grav * rdr
                        nh_im = hb[p][1] - grav * rdi
                        h_re, h_im = cmul(nh_re, nh_im, dinv[p][0], dinv[p][1])
                        hr.append(h_re)
                        hi.append(h_im)
            for field, (f_re, f_im) in enumerate(((zr, zi), (dr, di), (hr, hi))):
                for p in range(2):
                    o_re, o_im = cmul(w_re, w_im, f_re[p], f_im[p])
                    out_ref[2 * field, p, sl, :] += o_re[:, :width]
                    out_ref[2 * field + 1, p, sl, :] += o_im[:, :width]
        return carry

    lax.fori_loop(0, npoles, one_pole, 0)


def solve_poles(poles, wide, coef, width):
    comps, parities, rows, _ = wide.shape
    return pl.pallas_call(
        pole_kernel,
        out_shape=jax.ShapeDtypeStruct((comps, parities, rows, width), jnp.float32),
        in_specs=[
            pl.BlockSpec(memory_space=pltpu.SMEM),
            pl.BlockSpec(memory_space=pltpu.VMEM),
            pl.BlockSpec(memory_space=pltpu.VMEM),
        ],
        out_specs=pl.BlockSpec(memory_space=pltpu.VMEM),
    )(poles, wide, coef)


def cmul(are, aim, bre, bim):
    return (are * bre - aim * bim, are * bim + aim * bre)


def zero_extend(field):
    return jnp.pad(field, ((0, 0), (0, 0), (0, 0), (0, 0), (1, 1)))


def solve(spectra, coef, shifts, extend):
    e_lo, e_hi, rossby, gravity = coef
    count = spectra.shape[3]
    shift_re = shifts[:, 0][:, None, None, None]
    shift_im = shifts[:, 1][:, None, None, None]
    weight_re = shifts[:, 2][:, None, None, None]
    weight_im = shifts[:, 3][:, None, None, None]
    z0r, z0i = (spectra[0][None], spectra[1][None])
    d0r, d0i = (spectra[2][None], spectra[3][None])
    h0r, h0i = (spectra[4][None], spectra[5][None])
    b_re = shift_re + 0.0 * rossby[None]
    b_im = shift_im + rossby[None]
    b_mag = b_re * b_re + b_im * b_im
    inv_re, inv_im = (b_re / b_mag, -b_im / b_mag)
    det_re, det_im = cmul(b_re, b_im, shift_re, shift_im)
    det_re = det_re + gravity[None] * gravity[None]
    det_mag = det_re * det_re + det_im * det_im
    dinv_re, dinv_im = (det_re / det_mag, -det_im / det_mag)
    grav = gravity[None]
    hb_re, hb_im = cmul(b_re, b_im, h0r, h0i)
    zr, zi, dr, di, hr, hi = (z0r, z0i, d0r, d0i, h0r, h0i)
    for sweep in range(SWEEPS):
        if sweep == 0:
            rzr, rzi, rdr, rdi = (z0r, z0i, d0r, d0i)
        else:
            both = jnp.stack([zr, zi, dr, di], axis=0)
            ext = extend(both)
            lower = jnp.stack([ext[:, :, 1, :, 0:count], ext[:, :, 0, :, 1 : count + 1]], axis=2)
            upper = jnp.stack(
                [ext[:, :, 1, :, 1 : count + 1], ext[:, :, 0, :, 2 : count + 2]], axis=2
            )
            near = e_lo * lower + e_hi * upper
            rzr = z0r - coriolis_step * near[2]
            rzi = z0i - coriolis_step * near[3]
            rdr = d0r + coriolis_step * near[0]
            rdi = d0i + coriolis_step * near[1]
        zr, zi = cmul(rzr, rzi, inv_re, inv_im)
        nd_re, nd_im = cmul(shift_re, shift_im, rdr, rdi)
        nd_re = nd_re + grav * h0r
        nd_im = nd_im + grav * h0i
        nh_re = hb_re - grav * rdr
        nh_im = hb_im - grav * rdi
        dr, di = cmul(nd_re, nd_im, dinv_re, dinv_im)
        hr, hi = cmul(nh_re, nh_im, dinv_re, dinv_im)
    parts = []
    for field_re, field_im in ((zr, zi), (dr, di), (hr, hi)):
        out_re, out_im = cmul(weight_re, weight_im, field_re, field_im)
        parts.append(jnp.sum(out_re, axis=0))
        parts.append(jnp.sum(out_im, axis=0))
    return jnp.stack(parts, axis=0)


def lookup(pole_table, chosen):
    columns = jnp.arange(pole_table.shape[1], dtype=jnp.int32)
    onehot = (chosen[:, None] == columns[None, :]).astype(jnp.float32)
    return jnp.dot(onehot, jnp.transpose(pole_table), precision=lax.Precision.HIGHEST)


def shards(grid, legendre, wave_table, pole_table, pole_index):
    slots = legendre.shape[0]
    local_k = legendre.shape[3]
    lat_rows = grid.shape[2]
    wave_count = lax.axis_size("wave")
    half_count = wave_count // 2
    columns = jnp.take(grid, wave_table, axis=1)
    regrouped = lax.all_to_all(columns[None], "wave", split_axis=2, concat_axis=0, tiled=True)
    north = regrouped[:half_count]
    south = regrouped[half_count:]
    parts = jnp.stack([north + south, north - south], axis=0)
    high, low = split_high(parts)
    leg_blocks = legendre.reshape(slots, 2, half_count, lat_rows, local_k)
    first = jnp.einsum("mpwlk,pwcml->cpmk", leg_blocks, high, preferred_element_type=jnp.float32)
    second = jnp.einsum("mpwlk,pwcml->cpmk", leg_blocks, low, preferred_element_type=jnp.float32)
    spectra = first + second
    own_waves = lax.dynamic_slice_in_dim(wave_table, lax.axis_index("wave") * slots, slots).astype(
        jnp.float32
    )
    pole_count = lax.axis_size("pole")
    pole_pos = lax.axis_index("pole")
    rightward = [(i, i + 1) for i in range(pole_count - 1)]
    leftward = [(i + 1, i) for i in range(pole_count - 1)]
    left_halo = lax.ppermute(spectra[..., local_k - HALO :], "pole", rightward)
    right_halo = lax.ppermute(spectra[..., :HALO], "pole", leftward)
    gap = jnp.zeros(spectra.shape[:3] + (RING - local_k - 2 * HALO,), jnp.float32)
    wide = jnp.concatenate([spectra, right_halo, gap, left_halo], axis=3)
    coef = coefficients(own_waves, pole_pos * local_k, local_k, local_k * pole_count)
    poles = jnp.take(pole_table, pole_index, axis=1)
    return solve_poles(poles, wide, coef, local_k)


def solution(mesh):
    in_specs = (P(None, None, "wave"), P("wave", None, None, "pole"), P(), P(), P())
    out_specs = P(None, None, "wave", "pole")
    return jax.shard_map(shards, mesh=mesh, in_specs=in_specs, out_specs=out_specs, check_vma=False)
```

```python
import jax
import jax.numpy as jnp
from jax import lax
from jax.experimental import pallas as pl
from jax.experimental.pallas import tpu as pltpu
from jax.sharding import PartitionSpec as P

SWEEPS = 8
HALO = 8
RING = 256
CHUNK = 8


coriolis_step = 1.2
gravity_step = 0.0008


def split_high(values):
    upper_part = values.astype(jnp.bfloat16)
    kept = lax.optimization_barrier(upper_part)
    lower_part = (values - kept.astype(jnp.float32)).astype(jnp.bfloat16)
    return (upper_part, lower_part)


def coefficients(wavenum, base, width, total):
    lane = jnp.arange(RING, dtype=jnp.int32)
    index = jnp.where(lane >= RING - HALO, base + lane - RING, base + lane)
    inside = ((lane < width + HALO) | (lane >= RING - HALO)) & (index >= 0) & (index < total)
    index = jnp.clip(index, 0, total - 1).astype(jnp.float32)
    parity = jnp.arange(2, dtype=jnp.int32).astype(jnp.float32)
    order = (2.0 * index[None, :] + parity[:, None])[:, None, :]
    upper_inside = inside[None, None, :] & (order + 1.0 < 2.0 * total)
    wave = wavenum[None, :, None]
    degree = wave + order
    product = degree * (degree + 1.0)
    rossby = coriolis_step * wave / jnp.maximum(product, 2.0)
    gravity = gravity_step * jnp.sqrt(product)
    e_lo = jnp.sqrt(order * (2.0 * wave + order) / jnp.maximum(4.0 * degree * degree - 1.0, 1.0))
    after = order + 1.0
    upper_deg = degree + 1.0
    e_hi = jnp.sqrt(
        after * (2.0 * wave + after) / jnp.maximum(4.0 * upper_deg * upper_deg - 1.0, 1.0)
    )
    e_lo = jnp.where(inside[None, None, :], e_lo, 0.0)
    e_hi = jnp.where(upper_inside, e_hi, 0.0)
    return jnp.stack([e_lo, e_hi, rossby, gravity], axis=0)


def pole_kernel(poles_ref, spec_ref, coef_ref, out_ref):
    npoles = poles_ref.shape[1]
    rows = spec_ref.shape[2]
    lanes = spec_ref.shape[3]
    width = out_ref.shape[3]
    out_ref[...] = jnp.zeros(out_ref.shape, jnp.float32)

    def one_pole(q, carry):
        a_re = poles_ref[0, q]
        a_im = poles_ref[1, q]
        w_re = poles_ref[2, q]
        w_im = poles_ref[3, q]
        for r0 in range(0, rows, CHUNK):
            sl = pl.ds(r0, CHUNK)

            def ld(ref, i, p):
                return ref[i, p, sl, :]

            def near(x):
                n0 = ld(coef_ref, 0, 0) * pltpu.roll(x[1], 1, 1) + ld(coef_ref, 1, 0) * x[1]
                n1 = ld(coef_ref, 0, 1) * x[0] + ld(coef_ref, 1, 1) * pltpu.roll(x[0], lanes - 1, 1)
                return (n0, n1)

            inv, dinv, lift, base = [], [], [], []
            for p in range(2):
                grav = ld(coef_ref, 3, p)
                b_im = a_im + ld(coef_ref, 2, p)
                b_rec = 1.0 / (a_re * a_re + b_im * b_im)
                inv.append((a_re * b_rec, -b_im * b_rec))
                det_re = a_re * a_re - b_im * a_im + grav * grav
                det_im = a_re * a_im + b_im * a_re
                det_rec = 1.0 / (det_re * det_re + det_im * det_im)
                dv = (det_re * det_rec, -det_im * det_rec)
                dinv.append(dv)
                lift.append(cmul(a_re, a_im, dv[0], dv[1]))
                base.append(cmul(ld(spec_ref, 6, p), ld(spec_ref, 7, p), dv[0], dv[1]))
            zr = zi = dr = di = None
            for sweep in range(SWEEPS):
                if sweep > 0:
                    nzr, nzi, ndr, ndi = near(zr), near(zi), near(dr), near(di)
                zr, zi, dr, di = [], [], [], []
                hr, hi = [], []
                for p in range(2):
                    if sweep == 0:
                        rzr, rzi = ld(spec_ref, 0, p), ld(spec_ref, 1, p)
                        rdr, rdi = ld(spec_ref, 2, p), ld(spec_ref, 3, p)
                    else:
                        rzr = ld(spec_ref, 0, p) - ndr[p]
                        rzi = ld(spec_ref, 1, p) - ndi[p]
                        rdr = ld(spec_ref, 2, p) + nzr[p]
                        rdi = ld(spec_ref, 3, p) + nzi[p]
                    z_re, z_im = cmul(rzr, rzi, inv[p][0], inv[p][1])
                    zr.append(z_re)
                    zi.append(z_im)
                    d_re, d_im = cmul(lift[p][0], lift[p][1], rdr, rdi)
                    dr.append(d_re + base[p][0])
                    di.append(d_im + base[p][1])
                    if sweep == SWEEPS - 1:
                        grav = ld(coef_ref, 3, p)
                        b_im = a_im + ld(coef_ref, 2, p)
                        h0r = ld(spec_ref, 4, p)
                        h0i = ld(spec_ref, 5, p)
                        nh_re = a_re * h0r - b_im * h0i - grav * rdr
                        nh_im = a_re * h0i + b_im * h0r - grav * rdi
                        h_re, h_im = cmul(nh_re, nh_im, dinv[p][0], dinv[p][1])
                        hr.append(h_re)
                        hi.append(h_im)
            for field, (f_re, f_im) in enumerate(((zr, zi), (dr, di), (hr, hi))):
                for p in range(2):
                    o_re, o_im = cmul(w_re, w_im, f_re[p], f_im[p])
                    out_ref[2 * field, p, sl, :] += o_re[:, :width]
                    out_ref[2 * field + 1, p, sl, :] += o_im[:, :width]
        return carry

    lax.fori_loop(0, npoles, one_pole, 0)


def solve_poles(poles, wide, coef, width):
    _, parities, rows, _ = wide.shape
    return pl.pallas_call(
        pole_kernel,
        out_shape=jax.ShapeDtypeStruct((6, parities, rows, width), jnp.float32),
        in_specs=[
            pl.BlockSpec(memory_space=pltpu.SMEM),
            pl.BlockSpec(memory_space=pltpu.VMEM),
            pl.BlockSpec(memory_space=pltpu.VMEM),
        ],
        out_specs=pl.BlockSpec(memory_space=pltpu.VMEM),
    )(poles, wide, coef)


def cmul(are, aim, bre, bim):
    return (are * bre - aim * bim, are * bim + aim * bre)


def zero_extend(field):
    return jnp.pad(field, ((0, 0), (0, 0), (0, 0), (0, 0), (1, 1)))


def solve(spectra, coef, shifts, extend):
    e_lo, e_hi, rossby, gravity = coef
    count = spectra.shape[3]
    shift_re = shifts[:, 0][:, None, None, None]
    shift_im = shifts[:, 1][:, None, None, None]
    weight_re = shifts[:, 2][:, None, None, None]
    weight_im = shifts[:, 3][:, None, None, None]
    z0r, z0i = (spectra[0][None], spectra[1][None])
    d0r, d0i = (spectra[2][None], spectra[3][None])
    h0r, h0i = (spectra[4][None], spectra[5][None])
    b_re = shift_re + 0.0 * rossby[None]
    b_im = shift_im + rossby[None]
    b_mag = b_re * b_re + b_im * b_im
    inv_re, inv_im = (b_re / b_mag, -b_im / b_mag)
    det_re, det_im = cmul(b_re, b_im, shift_re, shift_im)
    det_re = det_re + gravity[None] * gravity[None]
    det_mag = det_re * det_re + det_im * det_im
    dinv_re, dinv_im = (det_re / det_mag, -det_im / det_mag)
    grav = gravity[None]
    hb_re, hb_im = cmul(b_re, b_im, h0r, h0i)
    zr, zi, dr, di, hr, hi = (z0r, z0i, d0r, d0i, h0r, h0i)
    for sweep in range(SWEEPS):
        if sweep == 0:
            rzr, rzi, rdr, rdi = (z0r, z0i, d0r, d0i)
        else:
            both = jnp.stack([zr, zi, dr, di], axis=0)
            ext = extend(both)
            lower = jnp.stack([ext[:, :, 1, :, 0:count], ext[:, :, 0, :, 1 : count + 1]], axis=2)
            upper = jnp.stack(
                [ext[:, :, 1, :, 1 : count + 1], ext[:, :, 0, :, 2 : count + 2]], axis=2
            )
            near = e_lo * lower + e_hi * upper
            rzr = z0r - coriolis_step * near[2]
            rzi = z0i - coriolis_step * near[3]
            rdr = d0r + coriolis_step * near[0]
            rdi = d0i + coriolis_step * near[1]
        zr, zi = cmul(rzr, rzi, inv_re, inv_im)
        nd_re, nd_im = cmul(shift_re, shift_im, rdr, rdi)
        nd_re = nd_re + grav * h0r
        nd_im = nd_im + grav * h0i
        nh_re = hb_re - grav * rdr
        nh_im = hb_im - grav * rdi
        dr, di = cmul(nd_re, nd_im, dinv_re, dinv_im)
        hr, hi = cmul(nh_re, nh_im, dinv_re, dinv_im)
    parts = []
    for field_re, field_im in ((zr, zi), (dr, di), (hr, hi)):
        out_re, out_im = cmul(weight_re, weight_im, field_re, field_im)
        parts.append(jnp.sum(out_re, axis=0))
        parts.append(jnp.sum(out_im, axis=0))
    return jnp.stack(parts, axis=0)


def lookup(pole_table, chosen):
    columns = jnp.arange(pole_table.shape[1], dtype=jnp.int32)
    onehot = (chosen[:, None] == columns[None, :]).astype(jnp.float32)
    return jnp.dot(onehot, jnp.transpose(pole_table), precision=lax.Precision.HIGHEST)


def shards(grid, legendre, wave_table, pole_table, pole_index):
    slots = legendre.shape[0]
    local_k = legendre.shape[3]
    lat_rows = grid.shape[2]
    wave_count = lax.axis_size("wave")
    half_count = wave_count // 2
    columns = jnp.take(grid, wave_table, axis=1)
    regrouped = lax.all_to_all(columns[None], "wave", split_axis=2, concat_axis=0, tiled=True)
    north = regrouped[:half_count]
    south = regrouped[half_count:]
    parts = jnp.stack([north + south, north - south], axis=0)
    high, low = split_high(parts)
    leg_blocks = legendre.reshape(slots, 2, half_count, lat_rows, local_k)
    both = jnp.concatenate([high, low], axis=2)
    products = jnp.einsum("mpwlk,pwcml->cpmk", leg_blocks, both, preferred_element_type=jnp.float32)
    comps = high.shape[2]
    spectra = products[:comps] + products[comps:]
    own_waves = lax.dynamic_slice_in_dim(wave_table, lax.axis_index("wave") * slots, slots).astype(
        jnp.float32
    )
    pole_count = lax.axis_size("pole")
    pole_pos = lax.axis_index("pole")
    rightward = [(i, i + 1) for i in range(pole_count - 1)]
    leftward = [(i + 1, i) for i in range(pole_count - 1)]
    left_halo = lax.ppermute(spectra[..., local_k - HALO :], "pole", rightward)
    right_halo = lax.ppermute(spectra[..., :HALO], "pole", leftward)
    gap = jnp.zeros(spectra.shape[:3] + (RING - local_k - 2 * HALO,), jnp.float32)
    wide = jnp.concatenate([spectra, right_halo, gap, left_halo], axis=3)
    coef = coefficients(own_waves, pole_pos * local_k, local_k, local_k * pole_count)
    wide = jnp.concatenate([wide, coef[3][None] * wide[4:6]], axis=0)
    coef = jnp.concatenate([coriolis_step * coef[:2], coef[2:]], axis=0)
    poles = jnp.take(pole_table, pole_index, axis=1)
    return solve_poles(poles, wide, coef, local_k)


def solution(mesh):
    in_specs = (P(None, None, "wave"), P("wave", None, None, "pole"), P(), P(), P())
    out_specs = P(None, None, "wave", "pole")
    return jax.shard_map(shards, mesh=mesh, in_specs=in_specs, out_specs=out_specs, check_vma=False)
```

```python
import jax
import jax.numpy as jnp
from jax import lax
from jax.experimental import pallas as pl
from jax.experimental.pallas import tpu as pltpu
from jax.sharding import PartitionSpec as P

SWEEPS = 8
HALO = 8
RING = 256
CHUNK = 8


coriolis_step = 1.2
gravity_step = 0.0008


def split_high(values):
    upper_part = values.astype(jnp.bfloat16)
    kept = lax.optimization_barrier(upper_part)
    lower_part = (values - kept.astype(jnp.float32)).astype(jnp.bfloat16)
    return (upper_part, lower_part)


def coefficients(wavenum, base, width, total):
    lane = jnp.arange(RING, dtype=jnp.int32)
    index = jnp.where(lane >= RING - HALO, base + lane - RING, base + lane)
    inside = ((lane < width + HALO) | (lane >= RING - HALO)) & (index >= 0) & (index < total)
    index = jnp.clip(index, 0, total - 1).astype(jnp.float32)
    parity = jnp.arange(2, dtype=jnp.int32).astype(jnp.float32)
    order = (2.0 * index[None, :] + parity[:, None])[:, None, :]
    upper_inside = inside[None, None, :] & (order + 1.0 < 2.0 * total)
    wave = wavenum[None, :, None]
    degree = wave + order
    product = degree * (degree + 1.0)
    rossby = coriolis_step * wave / jnp.maximum(product, 2.0)
    gravity = gravity_step * jnp.sqrt(product)
    e_lo = jnp.sqrt(order * (2.0 * wave + order) / jnp.maximum(4.0 * degree * degree - 1.0, 1.0))
    after = order + 1.0
    upper_deg = degree + 1.0
    e_hi = jnp.sqrt(
        after * (2.0 * wave + after) / jnp.maximum(4.0 * upper_deg * upper_deg - 1.0, 1.0)
    )
    e_lo = jnp.where(inside[None, None, :], e_lo, 0.0)
    e_hi = jnp.where(upper_inside, e_hi, 0.0)
    return jnp.stack([e_lo, e_hi, rossby, gravity], axis=0)


def pole_kernel(poles_ref, spec_ref, coef_ref, out_ref):
    npoles = poles_ref.shape[1]
    rows = spec_ref.shape[2]
    lanes = spec_ref.shape[3]
    width = out_ref.shape[3]
    out_ref[...] = jnp.zeros(out_ref.shape, jnp.float32)

    def one_pole(q, carry):
        a_re = poles_ref[0, q]
        a_im = poles_ref[1, q]
        w_re = poles_ref[2, q]
        w_im = poles_ref[3, q]
        for r0 in range(0, rows, CHUNK):
            sl = pl.ds(r0, CHUNK)

            def ld(ref, i, p):
                return ref[i, p, sl, :]

            def near(x):
                n0 = ld(coef_ref, 0, 0) * pltpu.roll(x[1], 1, 1) + ld(coef_ref, 1, 0) * x[1]
                n1 = ld(coef_ref, 0, 1) * x[0] + ld(coef_ref, 1, 1) * pltpu.roll(x[0], lanes - 1, 1)
                return (n0, n1)

            inv, dinv, lift, base = [], [], [], []
            for p in range(2):
                grav = ld(coef_ref, 3, p)
                b_im = a_im + ld(coef_ref, 2, p)
                b_rec = 1.0 / (a_re * a_re + b_im * b_im)
                inv.append((a_re * b_rec, -b_im * b_rec))
                det_re = a_re * a_re - b_im * a_im + grav * grav
                det_im = a_re * a_im + b_im * a_re
                det_rec = 1.0 / (det_re * det_re + det_im * det_im)
                dv = (det_re * det_rec, -det_im * det_rec)
                dinv.append(dv)
                lift.append(cmul(a_re, a_im, dv[0], dv[1]))
                base.append(cmul(ld(spec_ref, 6, p), ld(spec_ref, 7, p), dv[0], dv[1]))
            zr = zi = dr = di = None
            for sweep in range(SWEEPS):
                if sweep > 0:
                    nzr, nzi, ndr, ndi = near(zr), near(zi), near(dr), near(di)
                zr, zi, dr, di = [], [], [], []
                hr, hi = [], []
                for p in range(2):
                    if sweep == 0:
                        rzr, rzi = ld(spec_ref, 0, p), ld(spec_ref, 1, p)
                        rdr, rdi = ld(spec_ref, 2, p), ld(spec_ref, 3, p)
                    else:
                        rzr = ld(spec_ref, 0, p) - ndr[p]
                        rzi = ld(spec_ref, 1, p) - ndi[p]
                        rdr = ld(spec_ref, 2, p) + nzr[p]
                        rdi = ld(spec_ref, 3, p) + nzi[p]
                    z_re, z_im = cmul(rzr, rzi, inv[p][0], inv[p][1])
                    zr.append(z_re)
                    zi.append(z_im)
                    d_re, d_im = cmul(lift[p][0], lift[p][1], rdr, rdi)
                    dr.append(d_re + base[p][0])
                    di.append(d_im + base[p][1])
                    if sweep == SWEEPS - 1:
                        grav = ld(coef_ref, 3, p)
                        b_im = a_im + ld(coef_ref, 2, p)
                        h0r = ld(spec_ref, 4, p)
                        h0i = ld(spec_ref, 5, p)
                        nh_re = a_re * h0r - b_im * h0i - grav * rdr
                        nh_im = a_re * h0i + b_im * h0r - grav * rdi
                        h_re, h_im = cmul(nh_re, nh_im, dinv[p][0], dinv[p][1])
                        hr.append(h_re)
                        hi.append(h_im)
            for field, (f_re, f_im) in enumerate(((zr, zi), (dr, di), (hr, hi))):
                for p in range(2):
                    o_re, o_im = cmul(w_re, w_im, f_re[p], f_im[p])
                    out_ref[2 * field, p, sl, :] += o_re[:, :width]
                    out_ref[2 * field + 1, p, sl, :] += o_im[:, :width]
        return carry

    lax.fori_loop(0, npoles, one_pole, 0)


def solve_poles(poles, wide, coef, width):
    _, parities, rows, _ = wide.shape
    return pl.pallas_call(
        pole_kernel,
        out_shape=jax.ShapeDtypeStruct((6, parities, rows, width), jnp.float32),
        in_specs=[
            pl.BlockSpec(memory_space=pltpu.SMEM),
            pl.BlockSpec(memory_space=pltpu.VMEM),
            pl.BlockSpec(memory_space=pltpu.VMEM),
        ],
        out_specs=pl.BlockSpec(memory_space=pltpu.VMEM),
    )(poles, wide, coef)


def cmul(are, aim, bre, bim):
    return (are * bre - aim * bim, are * bim + aim * bre)


def zero_extend(field):
    return jnp.pad(field, ((0, 0), (0, 0), (0, 0), (0, 0), (1, 1)))


def solve(spectra, coef, shifts, extend):
    e_lo, e_hi, rossby, gravity = coef
    count = spectra.shape[3]
    shift_re = shifts[:, 0][:, None, None, None]
    shift_im = shifts[:, 1][:, None, None, None]
    weight_re = shifts[:, 2][:, None, None, None]
    weight_im = shifts[:, 3][:, None, None, None]
    z0r, z0i = (spectra[0][None], spectra[1][None])
    d0r, d0i = (spectra[2][None], spectra[3][None])
    h0r, h0i = (spectra[4][None], spectra[5][None])
    b_re = shift_re + 0.0 * rossby[None]
    b_im = shift_im + rossby[None]
    b_mag = b_re * b_re + b_im * b_im
    inv_re, inv_im = (b_re / b_mag, -b_im / b_mag)
    det_re, det_im = cmul(b_re, b_im, shift_re, shift_im)
    det_re = det_re + gravity[None] * gravity[None]
    det_mag = det_re * det_re + det_im * det_im
    dinv_re, dinv_im = (det_re / det_mag, -det_im / det_mag)
    grav = gravity[None]
    hb_re, hb_im = cmul(b_re, b_im, h0r, h0i)
    zr, zi, dr, di, hr, hi = (z0r, z0i, d0r, d0i, h0r, h0i)
    for sweep in range(SWEEPS):
        if sweep == 0:
            rzr, rzi, rdr, rdi = (z0r, z0i, d0r, d0i)
        else:
            both = jnp.stack([zr, zi, dr, di], axis=0)
            ext = extend(both)
            lower = jnp.stack([ext[:, :, 1, :, 0:count], ext[:, :, 0, :, 1 : count + 1]], axis=2)
            upper = jnp.stack(
                [ext[:, :, 1, :, 1 : count + 1], ext[:, :, 0, :, 2 : count + 2]], axis=2
            )
            near = e_lo * lower + e_hi * upper
            rzr = z0r - coriolis_step * near[2]
            rzi = z0i - coriolis_step * near[3]
            rdr = d0r + coriolis_step * near[0]
            rdi = d0i + coriolis_step * near[1]
        zr, zi = cmul(rzr, rzi, inv_re, inv_im)
        nd_re, nd_im = cmul(shift_re, shift_im, rdr, rdi)
        nd_re = nd_re + grav * h0r
        nd_im = nd_im + grav * h0i
        nh_re = hb_re - grav * rdr
        nh_im = hb_im - grav * rdi
        dr, di = cmul(nd_re, nd_im, dinv_re, dinv_im)
        hr, hi = cmul(nh_re, nh_im, dinv_re, dinv_im)
    parts = []
    for field_re, field_im in ((zr, zi), (dr, di), (hr, hi)):
        out_re, out_im = cmul(weight_re, weight_im, field_re, field_im)
        parts.append(jnp.sum(out_re, axis=0))
        parts.append(jnp.sum(out_im, axis=0))
    return jnp.stack(parts, axis=0)


def lookup(pole_table, chosen):
    columns = jnp.arange(pole_table.shape[1], dtype=jnp.int32)
    onehot = (chosen[:, None] == columns[None, :]).astype(jnp.float32)
    return jnp.dot(onehot, jnp.transpose(pole_table), precision=lax.Precision.HIGHEST)


def shards(grid, legendre, wave_table, pole_table, pole_index):
    slots = legendre.shape[0]
    local_k = legendre.shape[3]
    lat_rows = grid.shape[2]
    wave_count = lax.axis_size("wave")
    half_count = wave_count // 2
    waves = grid.shape[1]
    comps = grid.shape[0]
    onehot = (wave_table[:, None] == jnp.arange(waves, dtype=jnp.int32)[None, :]).astype(jnp.float32)
    columns = jnp.einsum("sm,cml->scl", onehot, grid, precision=lax.Precision.HIGHEST)
    columns = columns.reshape(waves, comps * lat_rows)
    regrouped = lax.all_to_all(columns, "wave", split_axis=0, concat_axis=0, tiled=True)
    regrouped = regrouped.reshape(wave_count, slots, comps, lat_rows)
    north = regrouped[:half_count]
    south = regrouped[half_count:]
    parts = jnp.stack([north + south, north - south], axis=0)
    high, low = split_high(parts)
    leg_blocks = legendre.reshape(slots, 2, half_count, lat_rows, local_k)
    both = jnp.concatenate([high, low], axis=3)
    products = jnp.einsum("mpwlk,pwmcl->cpmk", leg_blocks, both, preferred_element_type=jnp.float32)
    spectra = products[:comps] + products[comps:]
    own_waves = lax.dynamic_slice_in_dim(wave_table, lax.axis_index("wave") * slots, slots).astype(
        jnp.float32
    )
    pole_count = lax.axis_size("pole")
    pole_pos = lax.axis_index("pole")
    rightward = [(i, i + 1) for i in range(pole_count - 1)]
    leftward = [(i + 1, i) for i in range(pole_count - 1)]
    left_halo = lax.ppermute(spectra[..., local_k - HALO :], "pole", rightward)
    right_halo = lax.ppermute(spectra[..., :HALO], "pole", leftward)
    gap = jnp.zeros(spectra.shape[:3] + (RING - local_k - 2 * HALO,), jnp.float32)
    wide = jnp.concatenate([spectra, right_halo, gap, left_halo], axis=3)
    coef = coefficients(own_waves, pole_pos * local_k, local_k, local_k * pole_count)
    wide = jnp.concatenate([wide, coef[3][None] * wide[4:6]], axis=0)
    coef = jnp.concatenate([coriolis_step * coef[:2], coef[2:]], axis=0)
    poles = jnp.take(pole_table, pole_index, axis=1)
    return solve_poles(poles, wide, coef, local_k)


def solution(mesh):
    in_specs = (P(None, None, "wave"), P("wave", None, None, "pole"), P(), P(), P())
    out_specs = P(None, None, "wave", "pole")
    return jax.shard_map(shards, mesh=mesh, in_specs=in_specs, out_specs=out_specs, check_vma=False)
```

```python
import jax
import jax.numpy as jnp
from jax import lax
from jax.experimental import pallas as pl
from jax.experimental.pallas import tpu as pltpu
from jax.sharding import PartitionSpec as P

SWEEPS = 8
HALO = 8
RING = 256
CHUNK = 8
GROUPS = 2


coriolis_step = 1.2
gravity_step = 0.0008


def split_high(values):
    upper_part = values.astype(jnp.bfloat16)
    kept = lax.optimization_barrier(upper_part)
    lower_part = (values - kept.astype(jnp.float32)).astype(jnp.bfloat16)
    return (upper_part, lower_part)


def coefficients(wavenum, base, width, total):
    lane = jnp.arange(RING, dtype=jnp.int32)
    index = jnp.where(lane >= RING - HALO, base + lane - RING, base + lane)
    inside = ((lane < width + HALO) | (lane >= RING - HALO)) & (index >= 0) & (index < total)
    index = jnp.clip(index, 0, total - 1).astype(jnp.float32)
    parity = jnp.arange(2, dtype=jnp.int32).astype(jnp.float32)
    order = (2.0 * index[None, :] + parity[:, None])[:, None, :]
    upper_inside = inside[None, None, :] & (order + 1.0 < 2.0 * total)
    wave = wavenum[None, :, None]
    degree = wave + order
    product = degree * (degree + 1.0)
    rossby = coriolis_step * wave / jnp.maximum(product, 2.0)
    gravity = gravity_step * jnp.sqrt(product)
    e_lo = jnp.sqrt(order * (2.0 * wave + order) / jnp.maximum(4.0 * degree * degree - 1.0, 1.0))
    after = order + 1.0
    upper_deg = degree + 1.0
    e_hi = jnp.sqrt(
        after * (2.0 * wave + after) / jnp.maximum(4.0 * upper_deg * upper_deg - 1.0, 1.0)
    )
    e_lo = jnp.where(inside[None, None, :], e_lo, 0.0)
    e_hi = jnp.where(upper_inside, e_hi, 0.0)
    return jnp.stack([e_lo, e_hi, rossby, gravity], axis=0)


def pole_kernel(poles_ref, spec_ref, coef_ref, out_ref):
    npoles = poles_ref.shape[1]
    rows = spec_ref.shape[2]
    lanes = spec_ref.shape[3]
    width = out_ref.shape[3]
    out_ref[...] = jnp.zeros(out_ref.shape, jnp.float32)

    def one_pole(q, carry):
        a_re = poles_ref[0, q]
        a_im = poles_ref[1, q]
        w_re = poles_ref[2, q]
        w_im = poles_ref[3, q]
        for r0 in range(0, rows, CHUNK):
            sl = pl.ds(r0, CHUNK)

            def ld(ref, i, p):
                return ref[i, p, sl, :]

            def near(x):
                n0 = ld(coef_ref, 0, 0) * pltpu.roll(x[1], 1, 1) + ld(coef_ref, 1, 0) * x[1]
                n1 = ld(coef_ref, 0, 1) * x[0] + ld(coef_ref, 1, 1) * pltpu.roll(x[0], lanes - 1, 1)
                return (n0, n1)

            inv, dinv, lift, base = [], [], [], []
            for p in range(2):
                grav = ld(coef_ref, 3, p)
                b_im = a_im + ld(coef_ref, 2, p)
                b_rec = 1.0 / (a_re * a_re + b_im * b_im)
                inv.append((a_re * b_rec, -b_im * b_rec))
                det_re = a_re * a_re - b_im * a_im + grav * grav
                det_im = a_re * a_im + b_im * a_re
                det_rec = 1.0 / (det_re * det_re + det_im * det_im)
                dv = (det_re * det_rec, -det_im * det_rec)
                dinv.append(dv)
                lift.append(cmul(a_re, a_im, dv[0], dv[1]))
                base.append(cmul(ld(spec_ref, 6, p), ld(spec_ref, 7, p), dv[0], dv[1]))
            zr = zi = dr = di = None
            for sweep in range(SWEEPS):
                if sweep > 0:
                    nzr, nzi, ndr, ndi = near(zr), near(zi), near(dr), near(di)
                zr, zi, dr, di = [], [], [], []
                hr, hi = [], []
                for p in range(2):
                    if sweep == 0:
                        rzr, rzi = ld(spec_ref, 0, p), ld(spec_ref, 1, p)
                        rdr, rdi = ld(spec_ref, 2, p), ld(spec_ref, 3, p)
                    else:
                        rzr = ld(spec_ref, 0, p) - ndr[p]
                        rzi = ld(spec_ref, 1, p) - ndi[p]
                        rdr = ld(spec_ref, 2, p) + nzr[p]
                        rdi = ld(spec_ref, 3, p) + nzi[p]
                    z_re, z_im = cmul(rzr, rzi, inv[p][0], inv[p][1])
                    zr.append(z_re)
                    zi.append(z_im)
                    d_re, d_im = cmul(lift[p][0], lift[p][1], rdr, rdi)
                    dr.append(d_re + base[p][0])
                    di.append(d_im + base[p][1])
                    if sweep == SWEEPS - 1:
                        grav = ld(coef_ref, 3, p)
                        b_im = a_im + ld(coef_ref, 2, p)
                        h0r = ld(spec_ref, 4, p)
                        h0i = ld(spec_ref, 5, p)
                        nh_re = a_re * h0r - b_im * h0i - grav * rdr
                        nh_im = a_re * h0i + b_im * h0r - grav * rdi
                        h_re, h_im = cmul(nh_re, nh_im, dinv[p][0], dinv[p][1])
                        hr.append(h_re)
                        hi.append(h_im)
            for field, (f_re, f_im) in enumerate(((zr, zi), (dr, di), (hr, hi))):
                for p in range(2):
                    o_re, o_im = cmul(w_re, w_im, f_re[p], f_im[p])
                    out_ref[2 * field, p, sl, :] += o_re[:, :width]
                    out_ref[2 * field + 1, p, sl, :] += o_im[:, :width]
        return carry

    lax.fori_loop(0, npoles, one_pole, 0)


def solve_poles(poles, wide, coef, width):
    _, parities, rows, _ = wide.shape
    return pl.pallas_call(
        pole_kernel,
        out_shape=jax.ShapeDtypeStruct((6, parities, rows, width), jnp.float32),
        in_specs=[
            pl.BlockSpec(memory_space=pltpu.SMEM),
            pl.BlockSpec(memory_space=pltpu.VMEM),
            pl.BlockSpec(memory_space=pltpu.VMEM),
        ],
        out_specs=pl.BlockSpec(memory_space=pltpu.VMEM),
    )(poles, wide, coef)


def cmul(are, aim, bre, bim):
    return (are * bre - aim * bim, are * bim + aim * bre)


def zero_extend(field):
    return jnp.pad(field, ((0, 0), (0, 0), (0, 0), (0, 0), (1, 1)))


def solve(spectra, coef, shifts, extend):
    e_lo, e_hi, rossby, gravity = coef
    count = spectra.shape[3]
    shift_re = shifts[:, 0][:, None, None, None]
    shift_im = shifts[:, 1][:, None, None, None]
    weight_re = shifts[:, 2][:, None, None, None]
    weight_im = shifts[:, 3][:, None, None, None]
    z0r, z0i = (spectra[0][None], spectra[1][None])
    d0r, d0i = (spectra[2][None], spectra[3][None])
    h0r, h0i = (spectra[4][None], spectra[5][None])
    b_re = shift_re + 0.0 * rossby[None]
    b_im = shift_im + rossby[None]
    b_mag = b_re * b_re + b_im * b_im
    inv_re, inv_im = (b_re / b_mag, -b_im / b_mag)
    det_re, det_im = cmul(b_re, b_im, shift_re, shift_im)
    det_re = det_re + gravity[None] * gravity[None]
    det_mag = det_re * det_re + det_im * det_im
    dinv_re, dinv_im = (det_re / det_mag, -det_im / det_mag)
    grav = gravity[None]
    hb_re, hb_im = cmul(b_re, b_im, h0r, h0i)
    zr, zi, dr, di, hr, hi = (z0r, z0i, d0r, d0i, h0r, h0i)
    for sweep in range(SWEEPS):
        if sweep == 0:
            rzr, rzi, rdr, rdi = (z0r, z0i, d0r, d0i)
        else:
            both = jnp.stack([zr, zi, dr, di], axis=0)
            ext = extend(both)
            lower = jnp.stack([ext[:, :, 1, :, 0:count], ext[:, :, 0, :, 1 : count + 1]], axis=2)
            upper = jnp.stack(
                [ext[:, :, 1, :, 1 : count + 1], ext[:, :, 0, :, 2 : count + 2]], axis=2
            )
            near = e_lo * lower + e_hi * upper
            rzr = z0r - coriolis_step * near[2]
            rzi = z0i - coriolis_step * near[3]
            rdr = d0r + coriolis_step * near[0]
            rdi = d0i + coriolis_step * near[1]
        zr, zi = cmul(rzr, rzi, inv_re, inv_im)
        nd_re, nd_im = cmul(shift_re, shift_im, rdr, rdi)
        nd_re = nd_re + grav * h0r
        nd_im = nd_im + grav * h0i
        nh_re = hb_re - grav * rdr
        nh_im = hb_im - grav * rdi
        dr, di = cmul(nd_re, nd_im, dinv_re, dinv_im)
        hr, hi = cmul(nh_re, nh_im, dinv_re, dinv_im)
    parts = []
    for field_re, field_im in ((zr, zi), (dr, di), (hr, hi)):
        out_re, out_im = cmul(weight_re, weight_im, field_re, field_im)
        parts.append(jnp.sum(out_re, axis=0))
        parts.append(jnp.sum(out_im, axis=0))
    return jnp.stack(parts, axis=0)


def lookup(pole_table, chosen):
    columns = jnp.arange(pole_table.shape[1], dtype=jnp.int32)
    onehot = (chosen[:, None] == columns[None, :]).astype(jnp.float32)
    return jnp.dot(onehot, jnp.transpose(pole_table), precision=lax.Precision.HIGHEST)


def shards(grid, legendre, wave_table, pole_table, pole_index):
    slots = legendre.shape[0]
    local_k = legendre.shape[3]
    lat_rows = grid.shape[2]
    wave_count = lax.axis_size("wave")
    half_count = wave_count // 2
    waves = grid.shape[1]
    comps = grid.shape[0]
    group = slots // GROUPS
    pole_count = lax.axis_size("pole")
    pole_pos = lax.axis_index("pole")
    rightward = [(i, i + 1) for i in range(pole_count - 1)]
    leftward = [(i + 1, i) for i in range(pole_count - 1)]
    own_waves = lax.dynamic_slice_in_dim(wave_table, lax.axis_index("wave") * slots, slots).astype(
        jnp.float32
    )
    coef_all = coefficients(own_waves, pole_pos * local_k, local_k, local_k * pole_count)
    coef_all = jnp.concatenate([coriolis_step * coef_all[:2], coef_all[2:]], axis=0)
    poles = jnp.take(pole_table, pole_index, axis=1)
    onehot = (wave_table[:, None] == jnp.arange(waves, dtype=jnp.int32)[None, :]).astype(jnp.float32)
    onehot = onehot.reshape(wave_count, GROUPS, group, waves)
    leg_blocks = legendre.reshape(slots, 2, half_count, lat_rows, local_k)
    outs = []
    for g in range(GROUPS):
        pick = onehot[:, g].reshape(wave_count * group, waves)
        columns = jnp.einsum("sm,cml->scl", pick, grid, precision=lax.Precision.HIGHEST)
        columns = columns.reshape(wave_count * group, comps * lat_rows)
        regrouped = lax.all_to_all(columns, "wave", split_axis=0, concat_axis=0, tiled=True)
        regrouped = regrouped.reshape(wave_count, group, comps, lat_rows)
        north = regrouped[:half_count]
        south = regrouped[half_count:]
        parts = jnp.stack([north + south, north - south], axis=0)
        high, low = split_high(parts)
        both = jnp.concatenate([high, low], axis=3)
        leg = leg_blocks[g * group : (g + 1) * group]
        products = jnp.einsum("mpwlk,pwmcl->cpmk", leg, both, preferred_element_type=jnp.float32)
        spectra = products[:comps] + products[comps:]
        left_halo = lax.ppermute(spectra[..., local_k - HALO :], "pole", rightward)
        right_halo = lax.ppermute(spectra[..., :HALO], "pole", leftward)
        gap = jnp.zeros(spectra.shape[:3] + (RING - local_k - 2 * HALO,), jnp.float32)
        wide = jnp.concatenate([spectra, right_halo, gap, left_halo], axis=3)
        coef = coef_all[:, :, g * group : (g + 1) * group]
        wide = jnp.concatenate([wide, coef[3][None] * wide[4:6]], axis=0)
        outs.append(solve_poles(poles, wide, coef, local_k))
    return jnp.concatenate(outs, axis=2)


def solution(mesh):
    in_specs = (P(None, None, "wave"), P("wave", None, None, "pole"), P(), P(), P())
    out_specs = P(None, None, "wave", "pole")
    return jax.shard_map(shards, mesh=mesh, in_specs=in_specs, out_specs=out_specs, check_vma=False)
```

```python
import jax
import jax.numpy as jnp
from jax import lax
from jax.experimental import pallas as pl
from jax.experimental.pallas import tpu as pltpu
from jax.sharding import PartitionSpec as P

SWEEPS = 8
HALO = 8
RING = 256
CHUNK = 8
GROUPS = 1
INTERLEAVE = 4


coriolis_step = 1.2
gravity_step = 0.0008


def split_high(values):
    upper_part = values.astype(jnp.bfloat16)
    kept = lax.optimization_barrier(upper_part)
    lower_part = (values - kept.astype(jnp.float32)).astype(jnp.bfloat16)
    return (upper_part, lower_part)


def coefficients(wavenum, base, width, total):
    lane = jnp.arange(RING, dtype=jnp.int32)
    index = jnp.where(lane >= RING - HALO, base + lane - RING, base + lane)
    inside = ((lane < width + HALO) | (lane >= RING - HALO)) & (index >= 0) & (index < total)
    index = jnp.clip(index, 0, total - 1).astype(jnp.float32)
    parity = jnp.arange(2, dtype=jnp.int32).astype(jnp.float32)
    order = (2.0 * index[None, :] + parity[:, None])[:, None, :]
    upper_inside = inside[None, None, :] & (order + 1.0 < 2.0 * total)
    wave = wavenum[None, :, None]
    degree = wave + order
    product = degree * (degree + 1.0)
    rossby = coriolis_step * wave / jnp.maximum(product, 2.0)
    gravity = gravity_step * jnp.sqrt(product)
    e_lo = jnp.sqrt(order * (2.0 * wave + order) / jnp.maximum(4.0 * degree * degree - 1.0, 1.0))
    after = order + 1.0
    upper_deg = degree + 1.0
    e_hi = jnp.sqrt(
        after * (2.0 * wave + after) / jnp.maximum(4.0 * upper_deg * upper_deg - 1.0, 1.0)
    )
    e_lo = jnp.where(inside[None, None, :], e_lo, 0.0)
    e_hi = jnp.where(upper_inside, e_hi, 0.0)
    return jnp.stack([e_lo, e_hi, rossby, gravity], axis=0)


def pole_kernel(poles_ref, spec_ref, coef_ref, out_ref):
    npoles = poles_ref.shape[1]
    rows = spec_ref.shape[2]
    lanes = spec_ref.shape[3]
    width = out_ref.shape[3]
    out_ref[...] = jnp.zeros(out_ref.shape, jnp.float32)

    def pole_step(step, carry):
        lanes_work = []
        for u in range(INTERLEAVE):
            q = step * INTERLEAVE + u
            scal = [poles_ref[i, q] for i in range(4)]
            for r0 in range(0, rows, CHUNK):
                lanes_work.append((scal, pl.ds(r0, CHUNK)))

        def ld(ref, i, p, sl):
            return ref[i, p, sl, :]

        def near(x, sl):
            n0 = ld(coef_ref, 0, 0, sl) * pltpu.roll(x[1], 1, 1) + ld(coef_ref, 1, 0, sl) * x[1]
            n1 = ld(coef_ref, 0, 1, sl) * x[0] + ld(coef_ref, 1, 1, sl) * pltpu.roll(
                x[0], lanes - 1, 1
            )
            return (n0, n1)

        prep = []
        for (a_re, a_im, _, _), sl in lanes_work:
            inv, dinv, lift, base = [], [], [], []
            for p in range(2):
                grav = ld(coef_ref, 3, p, sl)
                b_im = a_im + ld(coef_ref, 2, p, sl)
                b_rec = 1.0 / (a_re * a_re + b_im * b_im)
                inv.append((a_re * b_rec, -b_im * b_rec))
                det_re = a_re * a_re - b_im * a_im + grav * grav
                det_im = a_re * a_im + b_im * a_re
                det_rec = 1.0 / (det_re * det_re + det_im * det_im)
                dv = (det_re * det_rec, -det_im * det_rec)
                dinv.append(dv)
                lift.append(cmul(a_re, a_im, dv[0], dv[1]))
                base.append(cmul(ld(spec_ref, 6, p, sl), ld(spec_ref, 7, p, sl), dv[0], dv[1]))
            prep.append((inv, dinv, lift, base))
        state = [None] * len(lanes_work)
        for sweep in range(SWEEPS):
            for n, ((a_re, a_im, _, _), sl) in enumerate(lanes_work):
                inv, dinv, lift, base = prep[n]
                if sweep > 0:
                    zr, zi, dr, di, _, _ = state[n]
                    nzr, nzi, ndr, ndi = near(zr, sl), near(zi, sl), near(dr, sl), near(di, sl)
                zr, zi, dr, di, hr, hi = [], [], [], [], [], []
                for p in range(2):
                    if sweep == 0:
                        rzr, rzi = ld(spec_ref, 0, p, sl), ld(spec_ref, 1, p, sl)
                        rdr, rdi = ld(spec_ref, 2, p, sl), ld(spec_ref, 3, p, sl)
                    else:
                        rzr = ld(spec_ref, 0, p, sl) - ndr[p]
                        rzi = ld(spec_ref, 1, p, sl) - ndi[p]
                        rdr = ld(spec_ref, 2, p, sl) + nzr[p]
                        rdi = ld(spec_ref, 3, p, sl) + nzi[p]
                    z_re, z_im = cmul(rzr, rzi, inv[p][0], inv[p][1])
                    zr.append(z_re)
                    zi.append(z_im)
                    d_re, d_im = cmul(lift[p][0], lift[p][1], rdr, rdi)
                    dr.append(d_re + base[p][0])
                    di.append(d_im + base[p][1])
                    if sweep == SWEEPS - 1:
                        grav = ld(coef_ref, 3, p, sl)
                        b_im = a_im + ld(coef_ref, 2, p, sl)
                        h0r = ld(spec_ref, 4, p, sl)
                        h0i = ld(spec_ref, 5, p, sl)
                        nh_re = a_re * h0r - b_im * h0i - grav * rdr
                        nh_im = a_re * h0i + b_im * h0r - grav * rdi
                        h_re, h_im = cmul(nh_re, nh_im, dinv[p][0], dinv[p][1])
                        hr.append(h_re)
                        hi.append(h_im)
                state[n] = (zr, zi, dr, di, hr, hi)
        for n, ((_, _, w_re, w_im), sl) in enumerate(lanes_work):
            zr, zi, dr, di, hr, hi = state[n]
            for field, (f_re, f_im) in enumerate(((zr, zi), (dr, di), (hr, hi))):
                for p in range(2):
                    o_re, o_im = cmul(w_re, w_im, f_re[p], f_im[p])
                    out_ref[2 * field, p, sl, :] += o_re[:, :width]
                    out_ref[2 * field + 1, p, sl, :] += o_im[:, :width]
        return carry

    lax.fori_loop(0, npoles // INTERLEAVE, pole_step, 0)


def solve_poles(poles, wide, coef, width):
    _, parities, rows, _ = wide.shape
    return pl.pallas_call(
        pole_kernel,
        out_shape=jax.ShapeDtypeStruct((6, parities, rows, width), jnp.float32),
        in_specs=[
            pl.BlockSpec(memory_space=pltpu.SMEM),
            pl.BlockSpec(memory_space=pltpu.VMEM),
            pl.BlockSpec(memory_space=pltpu.VMEM),
        ],
        out_specs=pl.BlockSpec(memory_space=pltpu.VMEM),
    )(poles, wide, coef)


def cmul(are, aim, bre, bim):
    return (are * bre - aim * bim, are * bim + aim * bre)


def zero_extend(field):
    return jnp.pad(field, ((0, 0), (0, 0), (0, 0), (0, 0), (1, 1)))


def solve(spectra, coef, shifts, extend):
    e_lo, e_hi, rossby, gravity = coef
    count = spectra.shape[3]
    shift_re = shifts[:, 0][:, None, None, None]
    shift_im = shifts[:, 1][:, None, None, None]
    weight_re = shifts[:, 2][:, None, None, None]
    weight_im = shifts[:, 3][:, None, None, None]
    z0r, z0i = (spectra[0][None], spectra[1][None])
    d0r, d0i = (spectra[2][None], spectra[3][None])
    h0r, h0i = (spectra[4][None], spectra[5][None])
    b_re = shift_re + 0.0 * rossby[None]
    b_im = shift_im + rossby[None]
    b_mag = b_re * b_re + b_im * b_im
    inv_re, inv_im = (b_re / b_mag, -b_im / b_mag)
    det_re, det_im = cmul(b_re, b_im, shift_re, shift_im)
    det_re = det_re + gravity[None] * gravity[None]
    det_mag = det_re * det_re + det_im * det_im
    dinv_re, dinv_im = (det_re / det_mag, -det_im / det_mag)
    grav = gravity[None]
    hb_re, hb_im = cmul(b_re, b_im, h0r, h0i)
    zr, zi, dr, di, hr, hi = (z0r, z0i, d0r, d0i, h0r, h0i)
    for sweep in range(SWEEPS):
        if sweep == 0:
            rzr, rzi, rdr, rdi = (z0r, z0i, d0r, d0i)
        else:
            both = jnp.stack([zr, zi, dr, di], axis=0)
            ext = extend(both)
            lower = jnp.stack([ext[:, :, 1, :, 0:count], ext[:, :, 0, :, 1 : count + 1]], axis=2)
            upper = jnp.stack(
                [ext[:, :, 1, :, 1 : count + 1], ext[:, :, 0, :, 2 : count + 2]], axis=2
            )
            near = e_lo * lower + e_hi * upper
            rzr = z0r - coriolis_step * near[2]
            rzi = z0i - coriolis_step * near[3]
            rdr = d0r + coriolis_step * near[0]
            rdi = d0i + coriolis_step * near[1]
        zr, zi = cmul(rzr, rzi, inv_re, inv_im)
        nd_re, nd_im = cmul(shift_re, shift_im, rdr, rdi)
        nd_re = nd_re + grav * h0r
        nd_im = nd_im + grav * h0i
        nh_re = hb_re - grav * rdr
        nh_im = hb_im - grav * rdi
        dr, di = cmul(nd_re, nd_im, dinv_re, dinv_im)
        hr, hi = cmul(nh_re, nh_im, dinv_re, dinv_im)
    parts = []
    for field_re, field_im in ((zr, zi), (dr, di), (hr, hi)):
        out_re, out_im = cmul(weight_re, weight_im, field_re, field_im)
        parts.append(jnp.sum(out_re, axis=0))
        parts.append(jnp.sum(out_im, axis=0))
    return jnp.stack(parts, axis=0)


def lookup(pole_table, chosen):
    columns = jnp.arange(pole_table.shape[1], dtype=jnp.int32)
    onehot = (chosen[:, None] == columns[None, :]).astype(jnp.float32)
    return jnp.dot(onehot, jnp.transpose(pole_table), precision=lax.Precision.HIGHEST)


def shards(grid, legendre, wave_table, pole_table, pole_index):
    slots = legendre.shape[0]
    local_k = legendre.shape[3]
    lat_rows = grid.shape[2]
    wave_count = lax.axis_size("wave")
    half_count = wave_count // 2
    waves = grid.shape[1]
    comps = grid.shape[0]
    group = slots // GROUPS
    pole_count = lax.axis_size("pole")
    pole_pos = lax.axis_index("pole")
    rightward = [(i, i + 1) for i in range(pole_count - 1)]
    leftward = [(i + 1, i) for i in range(pole_count - 1)]
    own_waves = lax.dynamic_slice_in_dim(wave_table, lax.axis_index("wave") * slots, slots).astype(
        jnp.float32
    )
    coef_all = coefficients(own_waves, pole_pos * local_k, local_k, local_k * pole_count)
    coef_all = jnp.concatenate([coriolis_step * coef_all[:2], coef_all[2:]], axis=0)
    poles = jnp.take(pole_table, pole_index, axis=1)
    onehot = (wave_table[:, None] == jnp.arange(waves, dtype=jnp.int32)[None, :]).astype(jnp.float32)
    onehot = onehot.reshape(wave_count, GROUPS, group, waves)
    leg_blocks = legendre.reshape(slots, 2, half_count, lat_rows, local_k)
    outs = []
    for g in range(GROUPS):
        pick = onehot[:, g].reshape(wave_count * group, waves)
        columns = jnp.einsum("sm,cml->scl", pick, grid, precision=lax.Precision.HIGHEST)
        columns = columns.reshape(wave_count * group, comps * lat_rows)
        regrouped = lax.all_to_all(columns, "wave", split_axis=0, concat_axis=0, tiled=True)
        regrouped = regrouped.reshape(wave_count, group, comps, lat_rows)
        north = regrouped[:half_count]
        south = regrouped[half_count:]
        parts = jnp.stack([north + south, north - south], axis=0)
        high, low = split_high(parts)
        both = jnp.concatenate([high, low], axis=3)
        leg = leg_blocks[g * group : (g + 1) * group]
        products = jnp.einsum("mpwlk,pwmcl->cpmk", leg, both, preferred_element_type=jnp.float32)
        spectra = products[:comps] + products[comps:]
        left_halo = lax.ppermute(spectra[..., local_k - HALO :], "pole", rightward)
        right_halo = lax.ppermute(spectra[..., :HALO], "pole", leftward)
        gap = jnp.zeros(spectra.shape[:3] + (RING - local_k - 2 * HALO,), jnp.float32)
        wide = jnp.concatenate([spectra, right_halo, gap, left_halo], axis=3)
        coef = coef_all[:, :, g * group : (g + 1) * group]
        wide = jnp.concatenate([wide, coef[3][None] * wide[4:6]], axis=0)
        outs.append(solve_poles(poles, wide, coef, local_k))
    return jnp.concatenate(outs, axis=2)


def solution(mesh):
    in_specs = (P(None, None, "wave"), P("wave", None, None, "pole"), P(), P(), P())
    out_specs = P(None, None, "wave", "pole")
    return jax.shard_map(shards, mesh=mesh, in_specs=in_specs, out_specs=out_specs, check_vma=False)
```

```python
import functools

import jax
import jax.numpy as jnp
from jax import lax
from jax.experimental import pallas as pl
from jax.experimental.pallas import tpu as pltpu
from jax.sharding import PartitionSpec as P

SWEEPS = 8
HALO = 8
RING = 256
CHUNK = 8
GROUPS = 1
INTERLEAVE = 4
EDGE_INTERLEAVE = 16
WINDOW = 32


coriolis_step = 1.2
gravity_step = 0.0008


def split_high(values):
    upper_part = values.astype(jnp.bfloat16)
    kept = lax.optimization_barrier(upper_part)
    lower_part = (values - kept.astype(jnp.float32)).astype(jnp.bfloat16)
    return (upper_part, lower_part)


def coefficients(wavenum, base, width, total):
    lane = jnp.arange(RING, dtype=jnp.int32)
    index = jnp.where(lane >= RING - HALO, base + lane - RING, base + lane)
    inside = ((lane < width + HALO) | (lane >= RING - HALO)) & (index >= 0) & (index < total)
    index = jnp.clip(index, 0, total - 1).astype(jnp.float32)
    parity = jnp.arange(2, dtype=jnp.int32).astype(jnp.float32)
    order = (2.0 * index[None, :] + parity[:, None])[:, None, :]
    upper_inside = inside[None, None, :] & (order + 1.0 < 2.0 * total)
    wave = wavenum[None, :, None]
    degree = wave + order
    product = degree * (degree + 1.0)
    rossby = coriolis_step * wave / jnp.maximum(product, 2.0)
    gravity = gravity_step * jnp.sqrt(product)
    e_lo = jnp.sqrt(order * (2.0 * wave + order) / jnp.maximum(4.0 * degree * degree - 1.0, 1.0))
    after = order + 1.0
    upper_deg = degree + 1.0
    e_hi = jnp.sqrt(
        after * (2.0 * wave + after) / jnp.maximum(4.0 * upper_deg * upper_deg - 1.0, 1.0)
    )
    e_lo = jnp.where(inside[None, None, :], e_lo, 0.0)
    e_hi = jnp.where(upper_inside, e_hi, 0.0)
    return jnp.stack([e_lo, e_hi, rossby, gravity], axis=0)


def pole_kernel(poles_ref, spec_ref, coef_ref, out_ref, *, interleave):
    npoles = poles_ref.shape[1]
    rows = spec_ref.shape[2]
    chunk = min(CHUNK, rows)
    lanes = spec_ref.shape[3]
    width = out_ref.shape[3]
    out_ref[...] = jnp.zeros(out_ref.shape, jnp.float32)

    def pole_step(step, carry):
        lanes_work = []
        for u in range(interleave):
            q = step * interleave + u
            scal = [poles_ref[i, q] for i in range(4)]
            for r0 in range(0, rows, chunk):
                lanes_work.append((scal, pl.ds(r0, chunk)))

        def ld(ref, i, p, sl):
            return ref[i, p, sl, :]

        def near(x, sl):
            n0 = ld(coef_ref, 0, 0, sl) * pltpu.roll(x[1], 1, 1) + ld(coef_ref, 1, 0, sl) * x[1]
            n1 = ld(coef_ref, 0, 1, sl) * x[0] + ld(coef_ref, 1, 1, sl) * pltpu.roll(
                x[0], lanes - 1, 1
            )
            return (n0, n1)

        prep = []
        for (a_re, a_im, _, _), sl in lanes_work:
            inv, dinv, lift, base = [], [], [], []
            for p in range(2):
                grav = ld(coef_ref, 3, p, sl)
                b_im = a_im + ld(coef_ref, 2, p, sl)
                b_rec = 1.0 / (a_re * a_re + b_im * b_im)
                inv.append((a_re * b_rec, -b_im * b_rec))
                det_re = a_re * a_re - b_im * a_im + grav * grav
                det_im = a_re * a_im + b_im * a_re
                det_rec = 1.0 / (det_re * det_re + det_im * det_im)
                dv = (det_re * det_rec, -det_im * det_rec)
                dinv.append(dv)
                lift.append(cmul(a_re, a_im, dv[0], dv[1]))
                base.append(cmul(ld(spec_ref, 6, p, sl), ld(spec_ref, 7, p, sl), dv[0], dv[1]))
            prep.append((inv, dinv, lift, base))
        state = [None] * len(lanes_work)
        for sweep in range(SWEEPS):
            for n, ((a_re, a_im, _, _), sl) in enumerate(lanes_work):
                inv, dinv, lift, base = prep[n]
                if sweep > 0:
                    zr, zi, dr, di, _, _ = state[n]
                    nzr, nzi, ndr, ndi = near(zr, sl), near(zi, sl), near(dr, sl), near(di, sl)
                zr, zi, dr, di, hr, hi = [], [], [], [], [], []
                for p in range(2):
                    if sweep == 0:
                        rzr, rzi = ld(spec_ref, 0, p, sl), ld(spec_ref, 1, p, sl)
                        rdr, rdi = ld(spec_ref, 2, p, sl), ld(spec_ref, 3, p, sl)
                    else:
                        rzr = ld(spec_ref, 0, p, sl) - ndr[p]
                        rzi = ld(spec_ref, 1, p, sl) - ndi[p]
                        rdr = ld(spec_ref, 2, p, sl) + nzr[p]
                        rdi = ld(spec_ref, 3, p, sl) + nzi[p]
                    z_re, z_im = cmul(rzr, rzi, inv[p][0], inv[p][1])
                    zr.append(z_re)
                    zi.append(z_im)
                    d_re, d_im = cmul(lift[p][0], lift[p][1], rdr, rdi)
                    dr.append(d_re + base[p][0])
                    di.append(d_im + base[p][1])
                    if sweep == SWEEPS - 1:
                        grav = ld(coef_ref, 3, p, sl)
                        b_im = a_im + ld(coef_ref, 2, p, sl)
                        h0r = ld(spec_ref, 4, p, sl)
                        h0i = ld(spec_ref, 5, p, sl)
                        nh_re = a_re * h0r - b_im * h0i - grav * rdr
                        nh_im = a_re * h0i + b_im * h0r - grav * rdi
                        h_re, h_im = cmul(nh_re, nh_im, dinv[p][0], dinv[p][1])
                        hr.append(h_re)
                        hi.append(h_im)
                state[n] = (zr, zi, dr, di, hr, hi)
        for n, ((_, _, w_re, w_im), sl) in enumerate(lanes_work):
            zr, zi, dr, di, hr, hi = state[n]
            for field, (f_re, f_im) in enumerate(((zr, zi), (dr, di), (hr, hi))):
                for p in range(2):
                    o_re, o_im = cmul(w_re, w_im, f_re[p], f_im[p])
                    out_ref[2 * field, p, sl, :] += o_re[:, :width]
                    out_ref[2 * field + 1, p, sl, :] += o_im[:, :width]
        return carry

    lax.fori_loop(0, npoles // interleave, pole_step, 0)


def solve_poles(poles, wide, coef, width, interleave):
    _, parities, rows, _ = wide.shape
    return pl.pallas_call(
        functools.partial(pole_kernel, interleave=interleave),
        out_shape=jax.ShapeDtypeStruct((6, parities, rows, width), jnp.float32),
        in_specs=[
            pl.BlockSpec(memory_space=pltpu.SMEM),
            pl.BlockSpec(memory_space=pltpu.VMEM),
            pl.BlockSpec(memory_space=pltpu.VMEM),
        ],
        out_specs=pl.BlockSpec(memory_space=pltpu.VMEM),
    )(poles, wide, coef)


def cmul(are, aim, bre, bim):
    return (are * bre - aim * bim, are * bim + aim * bre)


def zero_extend(field):
    return jnp.pad(field, ((0, 0), (0, 0), (0, 0), (0, 0), (1, 1)))


def solve(spectra, coef, shifts, extend):
    e_lo, e_hi, rossby, gravity = coef
    count = spectra.shape[3]
    shift_re = shifts[:, 0][:, None, None, None]
    shift_im = shifts[:, 1][:, None, None, None]
    weight_re = shifts[:, 2][:, None, None, None]
    weight_im = shifts[:, 3][:, None, None, None]
    z0r, z0i = (spectra[0][None], spectra[1][None])
    d0r, d0i = (spectra[2][None], spectra[3][None])
    h0r, h0i = (spectra[4][None], spectra[5][None])
    b_re = shift_re + 0.0 * rossby[None]
    b_im = shift_im + rossby[None]
    b_mag = b_re * b_re + b_im * b_im
    inv_re, inv_im = (b_re / b_mag, -b_im / b_mag)
    det_re, det_im = cmul(b_re, b_im, shift_re, shift_im)
    det_re = det_re + gravity[None] * gravity[None]
    det_mag = det_re * det_re + det_im * det_im
    dinv_re, dinv_im = (det_re / det_mag, -det_im / det_mag)
    grav = gravity[None]
    hb_re, hb_im = cmul(b_re, b_im, h0r, h0i)
    zr, zi, dr, di, hr, hi = (z0r, z0i, d0r, d0i, h0r, h0i)
    for sweep in range(SWEEPS):
        if sweep == 0:
            rzr, rzi, rdr, rdi = (z0r, z0i, d0r, d0i)
        else:
            both = jnp.stack([zr, zi, dr, di], axis=0)
            ext = extend(both)
            lower = jnp.stack([ext[:, :, 1, :, 0:count], ext[:, :, 0, :, 1 : count + 1]], axis=2)
            upper = jnp.stack(
                [ext[:, :, 1, :, 1 : count + 1], ext[:, :, 0, :, 2 : count + 2]], axis=2
            )
            near = e_lo * lower + e_hi * upper
            rzr = z0r - coriolis_step * near[2]
            rzi = z0i - coriolis_step * near[3]
            rdr = d0r + coriolis_step * near[0]
            rdi = d0i + coriolis_step * near[1]
        zr, zi = cmul(rzr, rzi, inv_re, inv_im)
        nd_re, nd_im = cmul(shift_re, shift_im, rdr, rdi)
        nd_re = nd_re + grav * h0r
        nd_im = nd_im + grav * h0i
        nh_re = hb_re - grav * rdr
        nh_im = hb_im - grav * rdi
        dr, di = cmul(nd_re, nd_im, dinv_re, dinv_im)
        hr, hi = cmul(nh_re, nh_im, dinv_re, dinv_im)
    parts = []
    for field_re, field_im in ((zr, zi), (dr, di), (hr, hi)):
        out_re, out_im = cmul(weight_re, weight_im, field_re, field_im)
        parts.append(jnp.sum(out_re, axis=0))
        parts.append(jnp.sum(out_im, axis=0))
    return jnp.stack(parts, axis=0)


def lookup(pole_table, chosen):
    columns = jnp.arange(pole_table.shape[1], dtype=jnp.int32)
    onehot = (chosen[:, None] == columns[None, :]).astype(jnp.float32)
    return jnp.dot(onehot, jnp.transpose(pole_table), precision=lax.Precision.HIGHEST)


def shards(grid, legendre, wave_table, pole_table, pole_index):
    slots = legendre.shape[0]
    local_k = legendre.shape[3]
    lat_rows = grid.shape[2]
    wave_count = lax.axis_size("wave")
    half_count = wave_count // 2
    waves = grid.shape[1]
    comps = grid.shape[0]
    group = slots // GROUPS
    pole_count = lax.axis_size("pole")
    pole_pos = lax.axis_index("pole")
    rightward = [(i, i + 1) for i in range(pole_count - 1)]
    leftward = [(i + 1, i) for i in range(pole_count - 1)]
    own_waves = lax.dynamic_slice_in_dim(wave_table, lax.axis_index("wave") * slots, slots).astype(
        jnp.float32
    )
    coef_all = coefficients(own_waves, pole_pos * local_k, local_k, local_k * pole_count)
    coef_all = jnp.concatenate([coriolis_step * coef_all[:2], coef_all[2:]], axis=0)
    poles = jnp.take(pole_table, pole_index, axis=1)
    onehot = (wave_table[:, None] == jnp.arange(waves, dtype=jnp.int32)[None, :]).astype(jnp.float32)
    onehot = onehot.reshape(wave_count, GROUPS, group, waves)
    leg_blocks = legendre.reshape(slots, 2, half_count, lat_rows, local_k)
    outs = []
    for g in range(GROUPS):
        pick = onehot[:, g].reshape(wave_count * group, waves)
        columns = jnp.einsum("sm,cml->scl", pick, grid, precision=lax.Precision.HIGHEST)
        columns = columns.reshape(wave_count * group, comps * lat_rows)
        regrouped = lax.all_to_all(columns, "wave", split_axis=0, concat_axis=0, tiled=True)
        regrouped = regrouped.reshape(wave_count, group, comps, lat_rows)
        north = regrouped[:half_count]
        south = regrouped[half_count:]
        parts = jnp.stack([north + south, north - south], axis=0)
        high, low = split_high(parts)
        both = jnp.concatenate([high, low], axis=3)
        leg = leg_blocks[g * group : (g + 1) * group]
        products = jnp.einsum("mpwlk,pwmcl->cpmk", leg, both, preferred_element_type=jnp.float32)
        spectra = products[:comps] + products[comps:]
        coef = coef_all[:, :, g * group : (g + 1) * group]
        gap = jnp.zeros(spectra.shape[:3] + (RING - local_k,), jnp.float32)
        wide = jnp.concatenate([spectra, gap], axis=3)
        wide = jnp.concatenate([wide, coef[3][None] * wide[4:6]], axis=0)
        main = solve_poles(poles, wide, coef, local_k, INTERLEAVE)
        left_halo = lax.ppermute(spectra[..., local_k - HALO :], "pole", rightward)
        right_halo = lax.ppermute(spectra[..., :HALO], "pole", leftward)
        edge = HALO // 2
        pad = jnp.zeros(spectra.shape[:3] + (edge,), jnp.float32)
        tail = jnp.zeros(spectra.shape[:3] + (WINDOW - 2 * HALO - 2 * edge,), jnp.float32)
        win = jnp.concatenate([pad, right_halo, left_halo, pad, tail], axis=3)
        win_coef = jnp.concatenate(
            [
                coef[..., local_k - edge : local_k + HALO],
                coef[..., RING - HALO :],
                coef[..., :edge],
                jnp.zeros(coef.shape[:3] + (WINDOW - 2 * HALO - 2 * edge,), jnp.float32),
            ],
            axis=3,
        )
        win = jnp.concatenate([win, win_coef[3][None] * win[4:6]], axis=0)
        packed = 128 // WINDOW
        win = win.reshape(win.shape[0], 2, group // packed, 128)
        win_coef = win_coef.reshape(win_coef.shape[0], 2, group // packed, 128)
        fix = solve_poles(poles, win, win_coef, 128, EDGE_INTERLEAVE)
        fix = fix.reshape(fix.shape[0], 2, group, WINDOW)
        main = main.at[..., local_k - edge :].add(fix[..., :edge])
        main = main.at[..., :edge].add(fix[..., 2 * HALO + edge : 2 * HALO + 2 * edge])
        outs.append(main)
    return jnp.concatenate(outs, axis=2)


def solution(mesh):
    in_specs = (P(None, None, "wave"), P("wave", None, None, "pole"), P(), P(), P())
    out_specs = P(None, None, "wave", "pole")
    return jax.shard_map(shards, mesh=mesh, in_specs=in_specs, out_specs=out_specs, check_vma=False)
```

```python
import jax
import jax.numpy as jnp
from jax import lax
from jax.experimental import pallas as pl
from jax.experimental.pallas import tpu as pltpu
from jax.sharding import PartitionSpec as P

SWEEPS = 8
HALO = 4
RING = 256
CHUNK = 8
GROUPS = 1
INTERLEAVE = 4


coriolis_step = 1.2
gravity_step = 0.0008


def split_high(values):
    upper_part = values.astype(jnp.bfloat16)
    kept = lax.optimization_barrier(upper_part)
    lower_part = (values - kept.astype(jnp.float32)).astype(jnp.bfloat16)
    return (upper_part, lower_part)


def coefficients(wavenum, base, width, total):
    lane = jnp.arange(RING, dtype=jnp.int32)
    index = jnp.where(lane >= RING - HALO, base + lane - RING, base + lane)
    inside = ((lane < width + HALO) | (lane >= RING - HALO)) & (index >= 0) & (index < total)
    index = jnp.clip(index, 0, total - 1).astype(jnp.float32)
    parity = jnp.arange(2, dtype=jnp.int32).astype(jnp.float32)
    order = (2.0 * index[None, :] + parity[:, None])[:, None, :]
    upper_inside = inside[None, None, :] & (order + 1.0 < 2.0 * total)
    wave = wavenum[None, :, None]
    degree = wave + order
    product = degree * (degree + 1.0)
    rossby = coriolis_step * wave / jnp.maximum(product, 2.0)
    gravity = gravity_step * jnp.sqrt(product)
    e_lo = jnp.sqrt(order * (2.0 * wave + order) / jnp.maximum(4.0 * degree * degree - 1.0, 1.0))
    after = order + 1.0
    upper_deg = degree + 1.0
    e_hi = jnp.sqrt(
        after * (2.0 * wave + after) / jnp.maximum(4.0 * upper_deg * upper_deg - 1.0, 1.0)
    )
    e_lo = jnp.where(inside[None, None, :], e_lo, 0.0)
    e_hi = jnp.where(upper_inside, e_hi, 0.0)
    return jnp.stack([e_lo, e_hi, rossby, gravity], axis=0)


def pole_kernel(poles_ref, spec_ref, coef_ref, out_ref):
    npoles = poles_ref.shape[1]
    rows = spec_ref.shape[2]
    lanes = spec_ref.shape[3]
    width = out_ref.shape[3]
    out_ref[...] = jnp.zeros(out_ref.shape, jnp.float32)

    def pole_step(step, carry):
        lanes_work = []
        for u in range(INTERLEAVE):
            q = step * INTERLEAVE + u
            scal = [poles_ref[i, q] for i in range(4)]
            for r0 in range(0, rows, CHUNK):
                lanes_work.append((scal, pl.ds(r0, CHUNK)))

        def ld(ref, i, p, sl):
            return ref[i, p, sl, :]

        def near(x, sl):
            n0 = ld(coef_ref, 0, 0, sl) * pltpu.roll(x[1], 1, 1) + ld(coef_ref, 1, 0, sl) * x[1]
            n1 = ld(coef_ref, 0, 1, sl) * x[0] + ld(coef_ref, 1, 1, sl) * pltpu.roll(
                x[0], lanes - 1, 1
            )
            return (n0, n1)

        prep = []
        for (a_re, a_im, _, _), sl in lanes_work:
            inv, dinv, lift, base = [], [], [], []
            for p in range(2):
                grav = ld(coef_ref, 3, p, sl)
                b_im = a_im + ld(coef_ref, 2, p, sl)
                b_rec = 1.0 / (a_re * a_re + b_im * b_im)
                inv.append((a_re * b_rec, -b_im * b_rec))
                det_re = a_re * a_re - b_im * a_im + grav * grav
                det_im = a_re * a_im + b_im * a_re
                det_rec = 1.0 / (det_re * det_re + det_im * det_im)
                dv = (det_re * det_rec, -det_im * det_rec)
                dinv.append(dv)
                lift.append(cmul(a_re, a_im, dv[0], dv[1]))
                base.append(cmul(ld(spec_ref, 6, p, sl), ld(spec_ref, 7, p, sl), dv[0], dv[1]))
            prep.append((inv, dinv, lift, base))
        state = [None] * len(lanes_work)
        for sweep in range(SWEEPS):
            for n, ((a_re, a_im, _, _), sl) in enumerate(lanes_work):
                inv, dinv, lift, base = prep[n]
                if sweep > 0:
                    zr, zi, dr, di, _, _ = state[n]
                    nzr, nzi, ndr, ndi = near(zr, sl), near(zi, sl), near(dr, sl), near(di, sl)
                zr, zi, dr, di, hr, hi = [], [], [], [], [], []
                for p in range(2):
                    if sweep == 0:
                        rzr, rzi = ld(spec_ref, 0, p, sl), ld(spec_ref, 1, p, sl)
                        rdr, rdi = ld(spec_ref, 2, p, sl), ld(spec_ref, 3, p, sl)
                    else:
                        rzr = ld(spec_ref, 0, p, sl) - ndr[p]
                        rzi = ld(spec_ref, 1, p, sl) - ndi[p]
                        rdr = ld(spec_ref, 2, p, sl) + nzr[p]
                        rdi = ld(spec_ref, 3, p, sl) + nzi[p]
                    z_re, z_im = cmul(rzr, rzi, inv[p][0], inv[p][1])
                    zr.append(z_re)
                    zi.append(z_im)
                    d_re, d_im = cmul(lift[p][0], lift[p][1], rdr, rdi)
                    dr.append(d_re + base[p][0])
                    di.append(d_im + base[p][1])
                    if sweep == SWEEPS - 1:
                        grav = ld(coef_ref, 3, p, sl)
                        b_im = a_im + ld(coef_ref, 2, p, sl)
                        h0r = ld(spec_ref, 4, p, sl)
                        h0i = ld(spec_ref, 5, p, sl)
                        nh_re = a_re * h0r - b_im * h0i - grav * rdr
                        nh_im = a_re * h0i + b_im * h0r - grav * rdi
                        h_re, h_im = cmul(nh_re, nh_im, dinv[p][0], dinv[p][1])
                        hr.append(h_re)
                        hi.append(h_im)
                state[n] = (zr, zi, dr, di, hr, hi)
        for n, ((_, _, w_re, w_im), sl) in enumerate(lanes_work):
            zr, zi, dr, di, hr, hi = state[n]
            for field, (f_re, f_im) in enumerate(((zr, zi), (dr, di), (hr, hi))):
                for p in range(2):
                    o_re, o_im = cmul(w_re, w_im, f_re[p], f_im[p])
                    out_ref[2 * field, p, sl, :] += o_re[:, :width]
                    out_ref[2 * field + 1, p, sl, :] += o_im[:, :width]
        return carry

    lax.fori_loop(0, npoles // INTERLEAVE, pole_step, 0)


def solve_poles(poles, wide, coef, width):
    _, parities, rows, _ = wide.shape
    return pl.pallas_call(
        pole_kernel,
        out_shape=jax.ShapeDtypeStruct((6, parities, rows, width), jnp.float32),
        in_specs=[
            pl.BlockSpec(memory_space=pltpu.SMEM),
            pl.BlockSpec(memory_space=pltpu.VMEM),
            pl.BlockSpec(memory_space=pltpu.VMEM),
        ],
        out_specs=pl.BlockSpec(memory_space=pltpu.VMEM),
    )(poles, wide, coef)


def cmul(are, aim, bre, bim):
    return (are * bre - aim * bim, are * bim + aim * bre)


def zero_extend(field):
    return jnp.pad(field, ((0, 0), (0, 0), (0, 0), (0, 0), (1, 1)))


def solve(spectra, coef, shifts, extend):
    e_lo, e_hi, rossby, gravity = coef
    count = spectra.shape[3]
    shift_re = shifts[:, 0][:, None, None, None]
    shift_im = shifts[:, 1][:, None, None, None]
    weight_re = shifts[:, 2][:, None, None, None]
    weight_im = shifts[:, 3][:, None, None, None]
    z0r, z0i = (spectra[0][None], spectra[1][None])
    d0r, d0i = (spectra[2][None], spectra[3][None])
    h0r, h0i = (spectra[4][None], spectra[5][None])
    b_re = shift_re + 0.0 * rossby[None]
    b_im = shift_im + rossby[None]
    b_mag = b_re * b_re + b_im * b_im
    inv_re, inv_im = (b_re / b_mag, -b_im / b_mag)
    det_re, det_im = cmul(b_re, b_im, shift_re, shift_im)
    det_re = det_re + gravity[None] * gravity[None]
    det_mag = det_re * det_re + det_im * det_im
    dinv_re, dinv_im = (det_re / det_mag, -det_im / det_mag)
    grav = gravity[None]
    hb_re, hb_im = cmul(b_re, b_im, h0r, h0i)
    zr, zi, dr, di, hr, hi = (z0r, z0i, d0r, d0i, h0r, h0i)
    for sweep in range(SWEEPS):
        if sweep == 0:
            rzr, rzi, rdr, rdi = (z0r, z0i, d0r, d0i)
        else:
            both = jnp.stack([zr, zi, dr, di], axis=0)
            ext = extend(both)
            lower = jnp.stack([ext[:, :, 1, :, 0:count], ext[:, :, 0, :, 1 : count + 1]], axis=2)
            upper = jnp.stack(
                [ext[:, :, 1, :, 1 : count + 1], ext[:, :, 0, :, 2 : count + 2]], axis=2
            )
            near = e_lo * lower + e_hi * upper
            rzr = z0r - coriolis_step * near[2]
            rzi = z0i - coriolis_step * near[3]
            rdr = d0r + coriolis_step * near[0]
            rdi = d0i + coriolis_step * near[1]
        zr, zi = cmul(rzr, rzi, inv_re, inv_im)
        nd_re, nd_im = cmul(shift_re, shift_im, rdr, rdi)
        nd_re = nd_re + grav * h0r
        nd_im = nd_im + grav * h0i
        nh_re = hb_re - grav * rdr
        nh_im = hb_im - grav * rdi
        dr, di = cmul(nd_re, nd_im, dinv_re, dinv_im)
        hr, hi = cmul(nh_re, nh_im, dinv_re, dinv_im)
    parts = []
    for field_re, field_im in ((zr, zi), (dr, di), (hr, hi)):
        out_re, out_im = cmul(weight_re, weight_im, field_re, field_im)
        parts.append(jnp.sum(out_re, axis=0))
        parts.append(jnp.sum(out_im, axis=0))
    return jnp.stack(parts, axis=0)


def lookup(pole_table, chosen):
    columns = jnp.arange(pole_table.shape[1], dtype=jnp.int32)
    onehot = (chosen[:, None] == columns[None, :]).astype(jnp.float32)
    return jnp.dot(onehot, jnp.transpose(pole_table), precision=lax.Precision.HIGHEST)


def shards(grid, legendre, wave_table, pole_table, pole_index):
    slots = legendre.shape[0]
    local_k = legendre.shape[3]
    lat_rows = grid.shape[2]
    wave_count = lax.axis_size("wave")
    half_count = wave_count // 2
    waves = grid.shape[1]
    comps = grid.shape[0]
    group = slots // GROUPS
    pole_count = lax.axis_size("pole")
    pole_pos = lax.axis_index("pole")
    rightward = [(i, i + 1) for i in range(pole_count - 1)]
    leftward = [(i + 1, i) for i in range(pole_count - 1)]
    own_waves = lax.dynamic_slice_in_dim(wave_table, lax.axis_index("wave") * slots, slots).astype(
        jnp.float32
    )
    coef_all = coefficients(own_waves, pole_pos * local_k, local_k, local_k * pole_count)
    coef_all = jnp.concatenate([coriolis_step * coef_all[:2], coef_all[2:]], axis=0)
    poles = jnp.take(pole_table, pole_index, axis=1)
    send_left, send_right = lax.optimization_barrier(
        (legendre[..., local_k - HALO :].astype(jnp.float32), legendre[..., :HALO].astype(jnp.float32))
    )
    edge_left = lax.ppermute(send_left, "pole", rightward)
    edge_right = lax.ppermute(send_right, "pole", leftward)
    edges = jnp.concatenate([edge_right, edge_left], axis=3)
    edges = edges.reshape(slots, 2, half_count, lat_rows, 2 * HALO)
    onehot = (wave_table[:, None] == jnp.arange(waves, dtype=jnp.int32)[None, :]).astype(jnp.float32)
    onehot = onehot.reshape(wave_count, GROUPS, group, waves)
    leg_blocks = legendre.reshape(slots, 2, half_count, lat_rows, local_k)
    outs = []
    for g in range(GROUPS):
        pick = onehot[:, g].reshape(wave_count * group, waves)
        columns = jnp.einsum("sm,cml->scl", pick, grid, precision=lax.Precision.HIGHEST)
        columns = columns.reshape(wave_count * group, comps * lat_rows)
        regrouped = lax.all_to_all(columns, "wave", split_axis=0, concat_axis=0, tiled=True)
        regrouped = regrouped.reshape(wave_count, group, comps, lat_rows)
        north = regrouped[:half_count]
        south = regrouped[half_count:]
        parts = jnp.stack([north + south, north - south], axis=0)
        high, low = split_high(parts)
        both = jnp.concatenate([high, low], axis=3)
        leg = leg_blocks[g * group : (g + 1) * group]
        products = jnp.einsum("mpwlk,pwmcl->cpmk", leg, both, preferred_element_type=jnp.float32)
        spectra = products[:comps] + products[comps:]
        halo_products = jnp.einsum(
            "mpwlk,pwmcl->cpmk", edges[g * group : (g + 1) * group], both.astype(jnp.float32),
            precision=lax.Precision.HIGHEST, preferred_element_type=jnp.float32,
        )
        halos = halo_products[:comps] + halo_products[comps:]
        right_halo = halos[..., :HALO]
        left_halo = halos[..., HALO:]
        gap = jnp.zeros(spectra.shape[:3] + (RING - local_k - 2 * HALO,), jnp.float32)
        wide = jnp.concatenate([spectra, right_halo, gap, left_halo], axis=3)
        coef = coef_all[:, :, g * group : (g + 1) * group]
        wide = jnp.concatenate([wide, coef[3][None] * wide[4:6]], axis=0)
        outs.append(solve_poles(poles, wide, coef, local_k))
    return jnp.concatenate(outs, axis=2)


def solution(mesh):
    in_specs = (P(None, None, "wave"), P("wave", None, None, "pole"), P(), P(), P())
    out_specs = P(None, None, "wave", "pole")
    return jax.shard_map(shards, mesh=mesh, in_specs=in_specs, out_specs=out_specs, check_vma=False)
```

```python
import jax
import jax.numpy as jnp
from jax import lax
from jax.experimental import pallas as pl
from jax.experimental.pallas import tpu as pltpu
from jax.sharding import PartitionSpec as P

SWEEPS = 8
HALO = 4
RING = 256
CHUNK = 8
GROUPS = 1
INTERLEAVE = 4


coriolis_step = 1.2
gravity_step = 0.0008


def split_high(values):
    upper_part = values.astype(jnp.bfloat16)
    kept = lax.optimization_barrier(upper_part)
    lower_part = (values - kept.astype(jnp.float32)).astype(jnp.bfloat16)
    return (upper_part, lower_part)


def coefficients(wavenum, base, width, total):
    lane = jnp.arange(RING, dtype=jnp.int32)
    index = jnp.where(lane >= RING - HALO, base + lane - RING, base + lane)
    inside = ((lane < width + HALO) | (lane >= RING - HALO)) & (index >= 0) & (index < total)
    index = jnp.clip(index, 0, total - 1).astype(jnp.float32)
    parity = jnp.arange(2, dtype=jnp.int32).astype(jnp.float32)
    order = (2.0 * index[None, :] + parity[:, None])[:, None, :]
    upper_inside = inside[None, None, :] & (order + 1.0 < 2.0 * total)
    wave = wavenum[None, :, None]
    degree = wave + order
    product = degree * (degree + 1.0)
    rossby = coriolis_step * wave / jnp.maximum(product, 2.0)
    gravity = gravity_step * jnp.sqrt(product)
    e_lo = jnp.sqrt(order * (2.0 * wave + order) / jnp.maximum(4.0 * degree * degree - 1.0, 1.0))
    after = order + 1.0
    upper_deg = degree + 1.0
    e_hi = jnp.sqrt(
        after * (2.0 * wave + after) / jnp.maximum(4.0 * upper_deg * upper_deg - 1.0, 1.0)
    )
    e_lo = jnp.where(inside[None, None, :], e_lo, 0.0)
    e_hi = jnp.where(upper_inside, e_hi, 0.0)
    return jnp.stack([e_lo, e_hi, rossby, gravity], axis=0)


def pole_kernel(poles_ref, spec_ref, coef_ref, out_ref):
    npoles = poles_ref.shape[1]
    rows = spec_ref.shape[2]
    lanes = spec_ref.shape[3]
    width = out_ref.shape[3]
    out_ref[...] = jnp.zeros(out_ref.shape, jnp.float32)

    def pole_step(step, carry):
        lanes_work = []
        for u in range(INTERLEAVE):
            q = step * INTERLEAVE + u
            scal = [poles_ref[i, q] for i in range(4)]
            for r0 in range(0, rows, CHUNK):
                lanes_work.append((scal, pl.ds(r0, CHUNK)))

        def ld(ref, i, p, sl):
            return ref[i, p, sl, :]

        def near(x, sl):
            n0 = ld(coef_ref, 0, 0, sl) * pltpu.roll(x[1], 1, 1) + ld(coef_ref, 1, 0, sl) * x[1]
            n1 = ld(coef_ref, 0, 1, sl) * x[0] + ld(coef_ref, 1, 1, sl) * pltpu.roll(
                x[0], lanes - 1, 1
            )
            return (n0, n1)

        prep = []
        for (a_re, a_im, _, _), sl in lanes_work:
            inv, dinv, lift, base = [], [], [], []
            for p in range(2):
                grav = ld(coef_ref, 3, p, sl)
                b_im = a_im + ld(coef_ref, 2, p, sl)
                b_rec = 1.0 / (a_re * a_re + b_im * b_im)
                inv.append((a_re * b_rec, -b_im * b_rec))
                det_re = a_re * a_re - b_im * a_im + grav * grav
                det_im = a_re * a_im + b_im * a_re
                det_rec = 1.0 / (det_re * det_re + det_im * det_im)
                dv = (det_re * det_rec, -det_im * det_rec)
                dinv.append(dv)
                lift.append(cmul(a_re, a_im, dv[0], dv[1]))
                base.append(cmul(ld(spec_ref, 6, p, sl), ld(spec_ref, 7, p, sl), dv[0], dv[1]))
            prep.append((inv, dinv, lift, base))
        state = [None] * len(lanes_work)
        for sweep in range(SWEEPS):
            for n, ((a_re, a_im, _, _), sl) in enumerate(lanes_work):
                inv, dinv, lift, base = prep[n]
                if sweep > 0:
                    zr, zi, dr, di, _, _ = state[n]
                    nzr, nzi, ndr, ndi = near(zr, sl), near(zi, sl), near(dr, sl), near(di, sl)
                zr, zi, dr, di, hr, hi = [], [], [], [], [], []
                for p in range(2):
                    if sweep == 0:
                        rzr, rzi = ld(spec_ref, 0, p, sl), ld(spec_ref, 1, p, sl)
                        rdr, rdi = ld(spec_ref, 2, p, sl), ld(spec_ref, 3, p, sl)
                    else:
                        rzr = ld(spec_ref, 0, p, sl) - ndr[p]
                        rzi = ld(spec_ref, 1, p, sl) - ndi[p]
                        rdr = ld(spec_ref, 2, p, sl) + nzr[p]
                        rdi = ld(spec_ref, 3, p, sl) + nzi[p]
                    z_re, z_im = cmul(rzr, rzi, inv[p][0], inv[p][1])
                    zr.append(z_re)
                    zi.append(z_im)
                    d_re, d_im = cmul(lift[p][0], lift[p][1], rdr, rdi)
                    dr.append(d_re + base[p][0])
                    di.append(d_im + base[p][1])
                    if sweep == SWEEPS - 1:
                        grav = ld(coef_ref, 3, p, sl)
                        b_im = a_im + ld(coef_ref, 2, p, sl)
                        h0r = ld(spec_ref, 4, p, sl)
                        h0i = ld(spec_ref, 5, p, sl)
                        nh_re = a_re * h0r - b_im * h0i - grav * rdr
                        nh_im = a_re * h0i + b_im * h0r - grav * rdi
                        h_re, h_im = cmul(nh_re, nh_im, dinv[p][0], dinv[p][1])
                        hr.append(h_re)
                        hi.append(h_im)
                state[n] = (zr, zi, dr, di, hr, hi)
        for n, ((_, _, w_re, w_im), sl) in enumerate(lanes_work):
            zr, zi, dr, di, hr, hi = state[n]
            for field, (f_re, f_im) in enumerate(((zr, zi), (dr, di), (hr, hi))):
                for p in range(2):
                    o_re, o_im = cmul(w_re, w_im, f_re[p], f_im[p])
                    out_ref[2 * field, p, sl, :] += o_re[:, :width]
                    out_ref[2 * field + 1, p, sl, :] += o_im[:, :width]
        return carry

    lax.fori_loop(0, npoles // INTERLEAVE, pole_step, 0)


def solve_poles(poles, wide, coef, width):
    _, parities, rows, _ = wide.shape
    return pl.pallas_call(
        pole_kernel,
        out_shape=jax.ShapeDtypeStruct((6, parities, rows, width), jnp.float32),
        in_specs=[
            pl.BlockSpec(memory_space=pltpu.SMEM),
            pl.BlockSpec(memory_space=pltpu.VMEM),
            pl.BlockSpec(memory_space=pltpu.VMEM),
        ],
        out_specs=pl.BlockSpec(memory_space=pltpu.VMEM),
    )(poles, wide, coef)


def cmul(are, aim, bre, bim):
    return (are * bre - aim * bim, are * bim + aim * bre)


def zero_extend(field):
    return jnp.pad(field, ((0, 0), (0, 0), (0, 0), (0, 0), (1, 1)))


def solve(spectra, coef, shifts, extend):
    e_lo, e_hi, rossby, gravity = coef
    count = spectra.shape[3]
    shift_re = shifts[:, 0][:, None, None, None]
    shift_im = shifts[:, 1][:, None, None, None]
    weight_re = shifts[:, 2][:, None, None, None]
    weight_im = shifts[:, 3][:, None, None, None]
    z0r, z0i = (spectra[0][None], spectra[1][None])
    d0r, d0i = (spectra[2][None], spectra[3][None])
    h0r, h0i = (spectra[4][None], spectra[5][None])
    b_re = shift_re + 0.0 * rossby[None]
    b_im = shift_im + rossby[None]
    b_mag = b_re * b_re + b_im * b_im
    inv_re, inv_im = (b_re / b_mag, -b_im / b_mag)
    det_re, det_im = cmul(b_re, b_im, shift_re, shift_im)
    det_re = det_re + gravity[None] * gravity[None]
    det_mag = det_re * det_re + det_im * det_im
    dinv_re, dinv_im = (det_re / det_mag, -det_im / det_mag)
    grav = gravity[None]
    hb_re, hb_im = cmul(b_re, b_im, h0r, h0i)
    zr, zi, dr, di, hr, hi = (z0r, z0i, d0r, d0i, h0r, h0i)
    for sweep in range(SWEEPS):
        if sweep == 0:
            rzr, rzi, rdr, rdi = (z0r, z0i, d0r, d0i)
        else:
            both = jnp.stack([zr, zi, dr, di], axis=0)
            ext = extend(both)
            lower = jnp.stack([ext[:, :, 1, :, 0:count], ext[:, :, 0, :, 1 : count + 1]], axis=2)
            upper = jnp.stack(
                [ext[:, :, 1, :, 1 : count + 1], ext[:, :, 0, :, 2 : count + 2]], axis=2
            )
            near = e_lo * lower + e_hi * upper
            rzr = z0r - coriolis_step * near[2]
            rzi = z0i - coriolis_step * near[3]
            rdr = d0r + coriolis_step * near[0]
            rdi = d0i + coriolis_step * near[1]
        zr, zi = cmul(rzr, rzi, inv_re, inv_im)
        nd_re, nd_im = cmul(shift_re, shift_im, rdr, rdi)
        nd_re = nd_re + grav * h0r
        nd_im = nd_im + grav * h0i
        nh_re = hb_re - grav * rdr
        nh_im = hb_im - grav * rdi
        dr, di = cmul(nd_re, nd_im, dinv_re, dinv_im)
        hr, hi = cmul(nh_re, nh_im, dinv_re, dinv_im)
    parts = []
    for field_re, field_im in ((zr, zi), (dr, di), (hr, hi)):
        out_re, out_im = cmul(weight_re, weight_im, field_re, field_im)
        parts.append(jnp.sum(out_re, axis=0))
        parts.append(jnp.sum(out_im, axis=0))
    return jnp.stack(parts, axis=0)


def lookup(pole_table, chosen):
    columns = jnp.arange(pole_table.shape[1], dtype=jnp.int32)
    onehot = (chosen[:, None] == columns[None, :]).astype(jnp.float32)
    return jnp.dot(onehot, jnp.transpose(pole_table), precision=lax.Precision.HIGHEST)


def shards(grid, legendre, wave_table, pole_table, pole_index):
    slots = legendre.shape[0]
    local_k = legendre.shape[3]
    lat_rows = grid.shape[2]
    wave_count = lax.axis_size("wave")
    half_count = wave_count // 2
    waves = grid.shape[1]
    comps = grid.shape[0]
    group = slots // GROUPS
    pole_count = lax.axis_size("pole")
    pole_pos = lax.axis_index("pole")
    rightward = [(i, i + 1) for i in range(pole_count - 1)]
    leftward = [(i + 1, i) for i in range(pole_count - 1)]
    own_waves = lax.dynamic_slice_in_dim(wave_table, lax.axis_index("wave") * slots, slots).astype(
        jnp.float32
    )
    coef_all = coefficients(own_waves, pole_pos * local_k, local_k, local_k * pole_count)
    coef_all = jnp.concatenate([coriolis_step * coef_all[:2], coef_all[2:]], axis=0)
    poles = jnp.take(pole_table, pole_index, axis=1)
    send_left = jnp.swapaxes(legendre[..., local_k - HALO :], 2, 3).astype(jnp.float32)
    send_right = jnp.swapaxes(legendre[..., :HALO], 2, 3).astype(jnp.float32)
    edge_left = lax.ppermute(send_left, "pole", rightward)
    edge_right = lax.ppermute(send_right, "pole", leftward)
    edges = jnp.concatenate([edge_right, edge_left], axis=2)
    edges = edges.reshape(slots, 2, 2 * HALO, half_count, lat_rows)
    onehot = (wave_table[:, None] == jnp.arange(waves, dtype=jnp.int32)[None, :]).astype(jnp.float32)
    onehot = onehot.reshape(wave_count, GROUPS, group, waves)
    leg_blocks = legendre.reshape(slots, 2, half_count, lat_rows, local_k)
    outs = []
    for g in range(GROUPS):
        pick = onehot[:, g].reshape(wave_count * group, waves)
        columns = jnp.einsum("sm,cml->scl", pick, grid, precision=lax.Precision.HIGHEST)
        columns = columns.reshape(wave_count * group, comps * lat_rows)
        regrouped = lax.all_to_all(columns, "wave", split_axis=0, concat_axis=0, tiled=True)
        regrouped = regrouped.reshape(wave_count, group, comps, lat_rows)
        north = regrouped[:half_count]
        south = regrouped[half_count:]
        parts = jnp.stack([north + south, north - south], axis=0)
        high, low = split_high(parts)
        both = jnp.concatenate([high, low], axis=3)
        leg = leg_blocks[g * group : (g + 1) * group]
        products = jnp.einsum("mpwlk,pwmcl->cpmk", leg, both, preferred_element_type=jnp.float32)
        spectra = products[:comps] + products[comps:]
        halo_products = jnp.einsum(
            "mpkwl,pwmcl->cpmk",
            edges[g * group : (g + 1) * group],
            both.astype(jnp.float32),
            precision=lax.Precision.HIGHEST,
            preferred_element_type=jnp.float32,
        )
        halos = halo_products[:comps] + halo_products[comps:]
        right_halo = halos[..., :HALO]
        left_halo = halos[..., HALO:]
        gap = jnp.zeros(spectra.shape[:3] + (RING - local_k - 2 * HALO,), jnp.float32)
        wide = jnp.concatenate([spectra, right_halo, gap, left_halo], axis=3)
        coef = coef_all[:, :, g * group : (g + 1) * group]
        wide = jnp.concatenate([wide, coef[3][None] * wide[4:6]], axis=0)
        outs.append(solve_poles(poles, wide, coef, local_k))
    return jnp.concatenate(outs, axis=2)


def solution(mesh):
    in_specs = (P(None, None, "wave"), P("wave", None, None, "pole"), P(), P(), P())
    out_specs = P(None, None, "wave", "pole")
    return jax.shard_map(shards, mesh=mesh, in_specs=in_specs, out_specs=out_specs, check_vma=False)
```

```python
import jax
import jax.numpy as jnp
from jax import lax
from jax.experimental import pallas as pl
from jax.experimental.pallas import tpu as pltpu
from jax.sharding import PartitionSpec as P

SWEEPS = 8
HALO_K = 4
HALO = 2 * HALO_K
RING = 384
CHUNK = 8
GROUPS = 1
INTERLEAVE = 4


coriolis_step = 1.2
gravity_step = 0.0008


def split_high(values):
    upper_part = values.astype(jnp.bfloat16)
    kept = lax.optimization_barrier(upper_part)
    lower_part = (values - kept.astype(jnp.float32)).astype(jnp.bfloat16)
    return (upper_part, lower_part)


def coefficients(wavenum, base, width, total):
    lane = jnp.arange(RING, dtype=jnp.int32)
    index = jnp.where(lane >= RING - HALO, base + lane - RING, base + lane)
    inside = ((lane < width + HALO) | (lane >= RING - HALO)) & (index >= 0) & (index < total)
    order = jnp.clip(index, 0, total - 1).astype(jnp.float32)[None, :]
    upper_inside = inside & (index + 1 < total)
    lower_inside = inside & (index - 1 >= 0)
    wave = wavenum[:, None]
    degree = wave + order
    product = degree * (degree + 1.0)
    rossby = coriolis_step * wave / jnp.maximum(product, 2.0)
    gravity = gravity_step * jnp.sqrt(product)
    e_lo = jnp.sqrt(order * (2.0 * wave + order) / jnp.maximum(4.0 * degree * degree - 1.0, 1.0))
    after = order + 1.0
    upper_deg = degree + 1.0
    e_hi = jnp.sqrt(
        after * (2.0 * wave + after) / jnp.maximum(4.0 * upper_deg * upper_deg - 1.0, 1.0)
    )
    e_lo = jnp.where(lower_inside[None, :], e_lo, 0.0)
    e_hi = jnp.where(upper_inside[None, :], e_hi, 0.0)
    return jnp.stack([e_lo, e_hi, rossby, gravity], axis=0)


def pole_kernel(poles_ref, spec_ref, coef_ref, out_ref):
    npoles = poles_ref.shape[1]
    rows = spec_ref.shape[1]
    lanes = spec_ref.shape[2]
    width = out_ref.shape[2]
    out_ref[...] = jnp.zeros(out_ref.shape, jnp.float32)

    def pole_step(step, carry):
        work = []
        for u in range(INTERLEAVE):
            q = step * INTERLEAVE + u
            scal = [poles_ref[i, q] for i in range(4)]
            for r0 in range(0, rows, CHUNK):
                work.append((scal, pl.ds(r0, CHUNK)))

        def ld(ref, i, sl):
            return ref[i, sl, :]

        def near(x, sl):
            return ld(coef_ref, 0, sl) * pltpu.roll(x, 1, 1) + ld(coef_ref, 1, sl) * pltpu.roll(
                x, lanes - 1, 1
            )

        prep = []
        for (a_re, a_im, _, _), sl in work:
            grav = ld(coef_ref, 3, sl)
            b_im = a_im + ld(coef_ref, 2, sl)
            b_rec = 1.0 / (a_re * a_re + b_im * b_im)
            inv = (a_re * b_rec, -b_im * b_rec)
            det_re = a_re * a_re - b_im * a_im + grav * grav
            det_im = a_re * a_im + b_im * a_re
            det_rec = 1.0 / (det_re * det_re + det_im * det_im)
            dinv = (det_re * det_rec, -det_im * det_rec)
            lift = cmul(a_re, a_im, dinv[0], dinv[1])
            base = cmul(ld(spec_ref, 6, sl), ld(spec_ref, 7, sl), dinv[0], dinv[1])
            prep.append((inv, dinv, lift, base))
        state = [None] * len(work)
        for sweep in range(SWEEPS):
            for n, ((a_re, a_im, _, _), sl) in enumerate(work):
                inv, dinv, lift, base = prep[n]
                if sweep == 0:
                    rzr, rzi = ld(spec_ref, 0, sl), ld(spec_ref, 1, sl)
                    rdr, rdi = ld(spec_ref, 2, sl), ld(spec_ref, 3, sl)
                else:
                    zr, zi, dr, di, _, _ = state[n]
                    rzr = ld(spec_ref, 0, sl) - near(dr, sl)
                    rzi = ld(spec_ref, 1, sl) - near(di, sl)
                    rdr = ld(spec_ref, 2, sl) + near(zr, sl)
                    rdi = ld(spec_ref, 3, sl) + near(zi, sl)
                zr, zi = cmul(rzr, rzi, inv[0], inv[1])
                d_re, d_im = cmul(lift[0], lift[1], rdr, rdi)
                dr, di = d_re + base[0], d_im + base[1]
                hr = hi = None
                if sweep == SWEEPS - 1:
                    grav = ld(coef_ref, 3, sl)
                    b_im = a_im + ld(coef_ref, 2, sl)
                    h0r = ld(spec_ref, 4, sl)
                    h0i = ld(spec_ref, 5, sl)
                    nh_re = a_re * h0r - b_im * h0i - grav * rdr
                    nh_im = a_re * h0i + b_im * h0r - grav * rdi
                    hr, hi = cmul(nh_re, nh_im, dinv[0], dinv[1])
                state[n] = (zr, zi, dr, di, hr, hi)
        for n, ((_, _, w_re, w_im), sl) in enumerate(work):
            zr, zi, dr, di, hr, hi = state[n]
            for field, (f_re, f_im) in enumerate(((zr, zi), (dr, di), (hr, hi))):
                o_re, o_im = cmul(w_re, w_im, f_re, f_im)
                out_ref[2 * field, sl, :] += o_re[:, :width]
                out_ref[2 * field + 1, sl, :] += o_im[:, :width]
        return carry

    lax.fori_loop(0, npoles // INTERLEAVE, pole_step, 0)


def solve_poles(poles, wide, coef, width):
    _, rows, _ = wide.shape
    return pl.pallas_call(
        pole_kernel,
        out_shape=jax.ShapeDtypeStruct((6, rows, width), jnp.float32),
        in_specs=[
            pl.BlockSpec(memory_space=pltpu.SMEM),
            pl.BlockSpec(memory_space=pltpu.VMEM),
            pl.BlockSpec(memory_space=pltpu.VMEM),
        ],
        out_specs=pl.BlockSpec(memory_space=pltpu.VMEM),
    )(poles, wide, coef)


def cmul(are, aim, bre, bim):
    return (are * bre - aim * bim, are * bim + aim * bre)


def zero_extend(field):
    return jnp.pad(field, ((0, 0), (0, 0), (0, 0), (0, 0), (1, 1)))


def solve(spectra, coef, shifts, extend):
    e_lo, e_hi, rossby, gravity = coef
    count = spectra.shape[3]
    shift_re = shifts[:, 0][:, None, None, None]
    shift_im = shifts[:, 1][:, None, None, None]
    weight_re = shifts[:, 2][:, None, None, None]
    weight_im = shifts[:, 3][:, None, None, None]
    z0r, z0i = (spectra[0][None], spectra[1][None])
    d0r, d0i = (spectra[2][None], spectra[3][None])
    h0r, h0i = (spectra[4][None], spectra[5][None])
    b_re = shift_re + 0.0 * rossby[None]
    b_im = shift_im + rossby[None]
    b_mag = b_re * b_re + b_im * b_im
    inv_re, inv_im = (b_re / b_mag, -b_im / b_mag)
    det_re, det_im = cmul(b_re, b_im, shift_re, shift_im)
    det_re = det_re + gravity[None] * gravity[None]
    det_mag = det_re * det_re + det_im * det_im
    dinv_re, dinv_im = (det_re / det_mag, -det_im / det_mag)
    grav = gravity[None]
    hb_re, hb_im = cmul(b_re, b_im, h0r, h0i)
    zr, zi, dr, di, hr, hi = (z0r, z0i, d0r, d0i, h0r, h0i)
    for sweep in range(SWEEPS):
        if sweep == 0:
            rzr, rzi, rdr, rdi = (z0r, z0i, d0r, d0i)
        else:
            both = jnp.stack([zr, zi, dr, di], axis=0)
            ext = extend(both)
            lower = jnp.stack([ext[:, :, 1, :, 0:count], ext[:, :, 0, :, 1 : count + 1]], axis=2)
            upper = jnp.stack(
                [ext[:, :, 1, :, 1 : count + 1], ext[:, :, 0, :, 2 : count + 2]], axis=2
            )
            near = e_lo * lower + e_hi * upper
            rzr = z0r - coriolis_step * near[2]
            rzi = z0i - coriolis_step * near[3]
            rdr = d0r + coriolis_step * near[0]
            rdi = d0i + coriolis_step * near[1]
        zr, zi = cmul(rzr, rzi, inv_re, inv_im)
        nd_re, nd_im = cmul(shift_re, shift_im, rdr, rdi)
        nd_re = nd_re + grav * h0r
        nd_im = nd_im + grav * h0i
        nh_re = hb_re - grav * rdr
        nh_im = hb_im - grav * rdi
        dr, di = cmul(nd_re, nd_im, dinv_re, dinv_im)
        hr, hi = cmul(nh_re, nh_im, dinv_re, dinv_im)
    parts = []
    for field_re, field_im in ((zr, zi), (dr, di), (hr, hi)):
        out_re, out_im = cmul(weight_re, weight_im, field_re, field_im)
        parts.append(jnp.sum(out_re, axis=0))
        parts.append(jnp.sum(out_im, axis=0))
    return jnp.stack(parts, axis=0)


def lookup(pole_table, chosen):
    columns = jnp.arange(pole_table.shape[1], dtype=jnp.int32)
    onehot = (chosen[:, None] == columns[None, :]).astype(jnp.float32)
    return jnp.dot(onehot, jnp.transpose(pole_table), precision=lax.Precision.HIGHEST)


def shards(grid, legendre, wave_table, pole_table, pole_index):
    slots = legendre.shape[0]
    local_k = legendre.shape[3]
    lat_rows = grid.shape[2]
    wave_count = lax.axis_size("wave")
    half_count = wave_count // 2
    waves = grid.shape[1]
    comps = grid.shape[0]
    group = slots // GROUPS
    pole_count = lax.axis_size("pole")
    pole_pos = lax.axis_index("pole")
    rightward = [(i, i + 1) for i in range(pole_count - 1)]
    leftward = [(i + 1, i) for i in range(pole_count - 1)]
    own_waves = lax.dynamic_slice_in_dim(wave_table, lax.axis_index("wave") * slots, slots).astype(
        jnp.float32
    )
    coef_all = coefficients(own_waves, pole_pos * 2 * local_k, 2 * local_k, 2 * local_k * pole_count)
    coef_all = jnp.concatenate([coriolis_step * coef_all[:2], coef_all[2:]], axis=0)
    poles = jnp.take(pole_table, pole_index, axis=1)
    onehot = (wave_table[:, None] == jnp.arange(waves, dtype=jnp.int32)[None, :]).astype(jnp.float32)
    onehot = onehot.reshape(wave_count, GROUPS, group, waves)
    leg_blocks = legendre.reshape(slots, 2, half_count, lat_rows, local_k)
    outs = []
    for g in range(GROUPS):
        pick = onehot[:, g].reshape(wave_count * group, waves)
        columns = jnp.einsum("sm,cml->scl", pick, grid, precision=lax.Precision.HIGHEST)
        columns = columns.reshape(wave_count * group, comps * lat_rows)
        regrouped = lax.all_to_all(columns, "wave", split_axis=0, concat_axis=0, tiled=True)
        regrouped = regrouped.reshape(wave_count, group, comps, lat_rows)
        north = regrouped[:half_count]
        south = regrouped[half_count:]
        parts = jnp.stack([north + south, north - south], axis=0)
        high, low = split_high(parts)
        both = jnp.concatenate([high, low], axis=3)
        leg = leg_blocks[g * group : (g + 1) * group]
        products = jnp.einsum("mpwlk,pwmcl->cpmk", leg, both, preferred_element_type=jnp.float32)
        spectra = products[:comps] + products[comps:]
        left_halo = lax.ppermute(spectra[..., local_k - HALO_K :], "pole", rightward)
        right_halo = lax.ppermute(spectra[..., :HALO_K], "pole", leftward)

        def interleave(x):
            return jnp.moveaxis(x, 1, -1).reshape(x.shape[0], x.shape[2], -1)

        gap = jnp.zeros((comps, group, RING - 2 * local_k - 2 * HALO), jnp.float32)
        wide = jnp.concatenate(
            [interleave(spectra), interleave(right_halo), gap, interleave(left_halo)], axis=2
        )
        coef = coef_all[:, g * group : (g + 1) * group]
        wide = jnp.concatenate([wide, coef[3][None] * wide[4:6]], axis=0)
        flat = solve_poles(poles, wide, coef, 2 * local_k)
        outs.append(jnp.moveaxis(flat.reshape(comps, group, local_k, 2), 3, 1))
    return jnp.concatenate(outs, axis=2)


def solution(mesh):
    in_specs = (P(None, None, "wave"), P("wave", None, None, "pole"), P(), P(), P())
    out_specs = P(None, None, "wave", "pole")
    return jax.shard_map(shards, mesh=mesh, in_specs=in_specs, out_specs=out_specs, check_vma=False)
```

```python
import jax
import jax.numpy as jnp
from jax import lax
from jax.experimental import pallas as pl
from jax.experimental.pallas import tpu as pltpu
from jax.sharding import PartitionSpec as P

SWEEPS = 8
HALO = 8
RING = 256
CHUNK = 8
GROUPS = 1
INTERLEAVE = 4


coriolis_step = 1.2
gravity_step = 0.0008


def split_high(values):
    upper_part = values.astype(jnp.bfloat16)
    kept = lax.optimization_barrier(upper_part)
    lower_part = (values - kept.astype(jnp.float32)).astype(jnp.bfloat16)
    return (upper_part, lower_part)


def coefficients(wavenum, base, width, total):
    lane = jnp.arange(RING, dtype=jnp.int32)
    index = jnp.where(lane >= RING - HALO, base + lane - RING, base + lane)
    inside = ((lane < width + HALO) | (lane >= RING - HALO)) & (index >= 0) & (index < total)
    index = jnp.clip(index, 0, total - 1).astype(jnp.float32)
    parity = jnp.arange(2, dtype=jnp.int32).astype(jnp.float32)
    order = (2.0 * index[None, :] + parity[:, None])[:, None, :]
    upper_inside = inside[None, None, :] & (order + 1.0 < 2.0 * total)
    wave = wavenum[None, :, None]
    degree = wave + order
    product = degree * (degree + 1.0)
    rossby = coriolis_step * wave / jnp.maximum(product, 2.0)
    gravity = gravity_step * jnp.sqrt(product)
    e_lo = jnp.sqrt(order * (2.0 * wave + order) / jnp.maximum(4.0 * degree * degree - 1.0, 1.0))
    after = order + 1.0
    upper_deg = degree + 1.0
    e_hi = jnp.sqrt(
        after * (2.0 * wave + after) / jnp.maximum(4.0 * upper_deg * upper_deg - 1.0, 1.0)
    )
    e_lo = jnp.where(inside[None, None, :], e_lo, 0.0)
    e_hi = jnp.where(upper_inside, e_hi, 0.0)
    return jnp.stack([e_lo, e_hi, rossby, gravity], axis=0)


def pole_kernel(poles_ref, spec_ref, coef_ref, out_ref):
    npoles = poles_ref.shape[1]
    rows = spec_ref.shape[2]
    lanes = spec_ref.shape[3]
    width = out_ref.shape[3]
    out_ref[...] = jnp.zeros(out_ref.shape, jnp.float32)

    def pole_step(step, carry):
        lanes_work = []
        for u in range(INTERLEAVE):
            q = step * INTERLEAVE + u
            scal = [poles_ref[i, q] for i in range(4)]
            for r0 in range(0, rows, CHUNK):
                lanes_work.append((scal, pl.ds(r0, CHUNK)))

        def ld(ref, i, p, sl):
            return ref[i, p, sl, :]

        def near(x, sl):
            n0 = ld(coef_ref, 0, 0, sl) * pltpu.roll(x[1], 1, 1) + ld(coef_ref, 1, 0, sl) * x[1]
            n1 = ld(coef_ref, 0, 1, sl) * x[0] + ld(coef_ref, 1, 1, sl) * pltpu.roll(
                x[0], lanes - 1, 1
            )
            return (n0, n1)

        prep = []
        for (a_re, a_im, _, _), sl in lanes_work:
            inv, dinv, lift, base = [], [], [], []
            for p in range(2):
                grav = ld(coef_ref, 3, p, sl)
                b_im = a_im + ld(coef_ref, 2, p, sl)
                b_rec = 1.0 / (a_re * a_re + b_im * b_im)
                inv.append((a_re * b_rec, -b_im * b_rec))
                det_re = a_re * a_re - b_im * a_im + grav * grav
                det_im = a_re * a_im + b_im * a_re
                det_rec = 1.0 / (det_re * det_re + det_im * det_im)
                dv = (det_re * det_rec, -det_im * det_rec)
                dinv.append(dv)
                lift.append(cmul(a_re, a_im, dv[0], dv[1]))
                base.append(cmul(ld(spec_ref, 6, p, sl), ld(spec_ref, 7, p, sl), dv[0], dv[1]))
            prep.append((inv, dinv, lift, base))
        state = [None] * len(lanes_work)
        for sweep in range(SWEEPS):
            for n, ((a_re, a_im, _, _), sl) in enumerate(lanes_work):
                inv, dinv, lift, base = prep[n]
                if sweep > 0:
                    zr, zi, dr, di, _, _ = state[n]
                    nzr, nzi, ndr, ndi = near(zr, sl), near(zi, sl), near(dr, sl), near(di, sl)
                zr, zi, dr, di, hr, hi = [], [], [], [], [], []
                for p in range(2):
                    if sweep == 0:
                        rzr, rzi = ld(spec_ref, 0, p, sl), ld(spec_ref, 1, p, sl)
                        rdr, rdi = ld(spec_ref, 2, p, sl), ld(spec_ref, 3, p, sl)
                    else:
                        rzr = ld(spec_ref, 0, p, sl) - ndr[p]
                        rzi = ld(spec_ref, 1, p, sl) - ndi[p]
                        rdr = ld(spec_ref, 2, p, sl) + nzr[p]
                        rdi = ld(spec_ref, 3, p, sl) + nzi[p]
                    z_re, z_im = cmul(rzr, rzi, inv[p][0], inv[p][1])
                    zr.append(z_re)
                    zi.append(z_im)
                    d_re, d_im = cmul(lift[p][0], lift[p][1], rdr, rdi)
                    dr.append(d_re + base[p][0])
                    di.append(d_im + base[p][1])
                    if sweep == SWEEPS - 1:
                        grav = ld(coef_ref, 3, p, sl)
                        b_im = a_im + ld(coef_ref, 2, p, sl)
                        h0r = ld(spec_ref, 4, p, sl)
                        h0i = ld(spec_ref, 5, p, sl)
                        nh_re = a_re * h0r - b_im * h0i - grav * rdr
                        nh_im = a_re * h0i + b_im * h0r - grav * rdi
                        h_re, h_im = cmul(nh_re, nh_im, dinv[p][0], dinv[p][1])
                        hr.append(h_re)
                        hi.append(h_im)
                state[n] = (zr, zi, dr, di, hr, hi)
        for n, ((_, _, w_re, w_im), sl) in enumerate(lanes_work):
            zr, zi, dr, di, hr, hi = state[n]
            for field, (f_re, f_im) in enumerate(((zr, zi), (dr, di), (hr, hi))):
                for p in range(2):
                    o_re, o_im = cmul(w_re, w_im, f_re[p], f_im[p])
                    out_ref[2 * field, p, sl, :] += o_re[:, :width]
                    out_ref[2 * field + 1, p, sl, :] += o_im[:, :width]
        return carry

    lax.fori_loop(0, npoles // INTERLEAVE, pole_step, 0)


def solve_poles(poles, wide, coef, width):
    _, parities, rows, _ = wide.shape
    return pl.pallas_call(
        pole_kernel,
        out_shape=jax.ShapeDtypeStruct((6, parities, rows, width), jnp.float32),
        in_specs=[
            pl.BlockSpec(memory_space=pltpu.SMEM),
            pl.BlockSpec(memory_space=pltpu.VMEM),
            pl.BlockSpec(memory_space=pltpu.VMEM),
        ],
        out_specs=pl.BlockSpec(memory_space=pltpu.VMEM),
    )(poles, wide, coef)


def cmul(are, aim, bre, bim):
    return (are * bre - aim * bim, are * bim + aim * bre)


def zero_extend(field):
    return jnp.pad(field, ((0, 0), (0, 0), (0, 0), (0, 0), (1, 1)))


def solve(spectra, coef, shifts, extend):
    e_lo, e_hi, rossby, gravity = coef
    count = spectra.shape[3]
    shift_re = shifts[:, 0][:, None, None, None]
    shift_im = shifts[:, 1][:, None, None, None]
    weight_re = shifts[:, 2][:, None, None, None]
    weight_im = shifts[:, 3][:, None, None, None]
    z0r, z0i = (spectra[0][None], spectra[1][None])
    d0r, d0i = (spectra[2][None], spectra[3][None])
    h0r, h0i = (spectra[4][None], spectra[5][None])
    b_re = shift_re + 0.0 * rossby[None]
    b_im = shift_im + rossby[None]
    b_mag = b_re * b_re + b_im * b_im
    inv_re, inv_im = (b_re / b_mag, -b_im / b_mag)
    det_re, det_im = cmul(b_re, b_im, shift_re, shift_im)
    det_re = det_re + gravity[None] * gravity[None]
    det_mag = det_re * det_re + det_im * det_im
    dinv_re, dinv_im = (det_re / det_mag, -det_im / det_mag)
    grav = gravity[None]
    hb_re, hb_im = cmul(b_re, b_im, h0r, h0i)
    zr, zi, dr, di, hr, hi = (z0r, z0i, d0r, d0i, h0r, h0i)
    for sweep in range(SWEEPS):
        if sweep == 0:
            rzr, rzi, rdr, rdi = (z0r, z0i, d0r, d0i)
        else:
            both = jnp.stack([zr, zi, dr, di], axis=0)
            ext = extend(both)
            lower = jnp.stack([ext[:, :, 1, :, 0:count], ext[:, :, 0, :, 1 : count + 1]], axis=2)
            upper = jnp.stack(
                [ext[:, :, 1, :, 1 : count + 1], ext[:, :, 0, :, 2 : count + 2]], axis=2
            )
            near = e_lo * lower + e_hi * upper
            rzr = z0r - coriolis_step * near[2]
            rzi = z0i - coriolis_step * near[3]
            rdr = d0r + coriolis_step * near[0]
            rdi = d0i + coriolis_step * near[1]
        zr, zi = cmul(rzr, rzi, inv_re, inv_im)
        nd_re, nd_im = cmul(shift_re, shift_im, rdr, rdi)
        nd_re = nd_re + grav * h0r
        nd_im = nd_im + grav * h0i
        nh_re = hb_re - grav * rdr
        nh_im = hb_im - grav * rdi
        dr, di = cmul(nd_re, nd_im, dinv_re, dinv_im)
        hr, hi = cmul(nh_re, nh_im, dinv_re, dinv_im)
    parts = []
    for field_re, field_im in ((zr, zi), (dr, di), (hr, hi)):
        out_re, out_im = cmul(weight_re, weight_im, field_re, field_im)
        parts.append(jnp.sum(out_re, axis=0))
        parts.append(jnp.sum(out_im, axis=0))
    return jnp.stack(parts, axis=0)


def lookup(pole_table, chosen):
    columns = jnp.arange(pole_table.shape[1], dtype=jnp.int32)
    onehot = (chosen[:, None] == columns[None, :]).astype(jnp.float32)
    return jnp.dot(onehot, jnp.transpose(pole_table), precision=lax.Precision.HIGHEST)


def shards(grid, legendre, wave_table, pole_table, pole_index):
    slots = legendre.shape[0]
    local_k = legendre.shape[3]
    lat_rows = grid.shape[2]
    wave_count = lax.axis_size("wave")
    half_count = wave_count // 2
    waves = grid.shape[1]
    comps = grid.shape[0]
    group = slots // GROUPS
    pole_count = lax.axis_size("pole")
    pole_pos = lax.axis_index("pole")
    rightward = [(i, i + 1) for i in range(pole_count - 1)]
    leftward = [(i + 1, i) for i in range(pole_count - 1)]
    own_waves = lax.dynamic_slice_in_dim(wave_table, lax.axis_index("wave") * slots, slots).astype(
        jnp.float32
    )
    coef_all = coefficients(own_waves, pole_pos * local_k, local_k, local_k * pole_count)
    coef_all = jnp.concatenate([coriolis_step * coef_all[:2], coef_all[2:]], axis=0)
    poles = jnp.take(pole_table, pole_index, axis=1)
    onehot = (wave_table[:, None] == jnp.arange(waves, dtype=jnp.int32)[None, :]).astype(jnp.float32)
    onehot = onehot.reshape(wave_count, GROUPS, group, waves)
    leg_blocks = legendre.reshape(slots, 2, half_count, lat_rows, local_k)
    outs = []
    for g in range(GROUPS):
        pick = onehot[:, g].reshape(wave_count * group, waves)
        columns = jnp.einsum("sm,cml->scl", pick, grid, precision=lax.Precision.HIGHEST)
        columns = columns.reshape(wave_count * group, comps * lat_rows)
        regrouped = lax.all_to_all(columns, "wave", split_axis=0, concat_axis=0, tiled=True)
        regrouped = regrouped.reshape(wave_count, group, comps, lat_rows)
        north = regrouped[:half_count]
        south = regrouped[half_count:]
        parts = jnp.stack([north + south, north - south], axis=0)
        high, low = split_high(parts)
        both = jnp.concatenate([high, low], axis=3)
        leg = leg_blocks[g * group : (g + 1) * group]
        products = jnp.einsum("mpwlk,pwmcl->mpkc", leg, both, preferred_element_type=jnp.float32)
        spectra = jnp.transpose(products[..., :comps] + products[..., comps:], (3, 1, 0, 2))
        left_halo = lax.ppermute(spectra[..., local_k - HALO :], "pole", rightward)
        right_halo = lax.ppermute(spectra[..., :HALO], "pole", leftward)
        gap = jnp.zeros(spectra.shape[:3] + (RING - local_k - 2 * HALO,), jnp.float32)
        wide = jnp.concatenate([spectra, right_halo, gap, left_halo], axis=3)
        coef = coef_all[:, :, g * group : (g + 1) * group]
        wide = jnp.concatenate([wide, coef[3][None] * wide[4:6]], axis=0)
        outs.append(solve_poles(poles, wide, coef, local_k))
    return jnp.concatenate(outs, axis=2)


def solution(mesh):
    in_specs = (P(None, None, "wave"), P("wave", None, None, "pole"), P(), P(), P())
    out_specs = P(None, None, "wave", "pole")
    return jax.shard_map(shards, mesh=mesh, in_specs=in_specs, out_specs=out_specs, check_vma=False)
```

```python
import jax
import jax.numpy as jnp
from jax import lax
from jax.experimental import pallas as pl
from jax.experimental.pallas import tpu as pltpu
from jax.sharding import PartitionSpec as P

SWEEPS = 8
HALO = 8
RING = 256
CHUNK = 8
GROUPS = 1
INTERLEAVE = 4


coriolis_step = 1.2
gravity_step = 0.0008


def split_high(values):
    upper_part = values.astype(jnp.bfloat16)
    kept = lax.optimization_barrier(upper_part)
    lower_part = (values - kept.astype(jnp.float32)).astype(jnp.bfloat16)
    return (upper_part, lower_part)


def coefficients(wavenum, base, width, total):
    lane = jnp.arange(RING, dtype=jnp.int32)
    index = jnp.where(lane >= RING - HALO, base + lane - RING, base + lane)
    inside = ((lane < width + HALO) | (lane >= RING - HALO)) & (index >= 0) & (index < total)
    index = jnp.clip(index, 0, total - 1).astype(jnp.float32)
    parity = jnp.arange(2, dtype=jnp.int32).astype(jnp.float32)
    order = (2.0 * index[None, :] + parity[:, None])[:, None, :]
    upper_inside = inside[None, None, :] & (order + 1.0 < 2.0 * total)
    wave = wavenum[None, :, None]
    degree = wave + order
    product = degree * (degree + 1.0)
    rossby = coriolis_step * wave / jnp.maximum(product, 2.0)
    gravity = gravity_step * jnp.sqrt(product)
    e_lo = jnp.sqrt(order * (2.0 * wave + order) / jnp.maximum(4.0 * degree * degree - 1.0, 1.0))
    after = order + 1.0
    upper_deg = degree + 1.0
    e_hi = jnp.sqrt(
        after * (2.0 * wave + after) / jnp.maximum(4.0 * upper_deg * upper_deg - 1.0, 1.0)
    )
    e_lo = jnp.where(inside[None, None, :], e_lo, 0.0)
    e_hi = jnp.where(upper_inside, e_hi, 0.0)
    return jnp.stack([e_lo, e_hi, rossby, gravity], axis=0)


def pole_kernel(poles_ref, spec_ref, coef_ref, out_ref):
    npoles = poles_ref.shape[1]
    rows = spec_ref.shape[2]
    lanes = spec_ref.shape[3]
    width = out_ref.shape[3]
    out_ref[...] = jnp.zeros(out_ref.shape, jnp.float32)

    def pole_step(step, carry):
        lanes_work = []
        for u in range(INTERLEAVE):
            q = step * INTERLEAVE + u
            scal = [poles_ref[i, q] for i in range(4)]
            for r0 in range(0, rows, CHUNK):
                lanes_work.append((scal, pl.ds(r0, CHUNK)))

        def ld(ref, i, p, sl):
            return ref[i, p, sl, :]

        def near(x, sl):
            n0 = ld(coef_ref, 0, 0, sl) * pltpu.roll(x[1], 1, 1) + ld(coef_ref, 1, 0, sl) * x[1]
            n1 = ld(coef_ref, 0, 1, sl) * x[0] + ld(coef_ref, 1, 1, sl) * pltpu.roll(
                x[0], lanes - 1, 1
            )
            return (n0, n1)

        prep = []
        for (a_re, a_im, _, _), sl in lanes_work:
            inv, dinv, lift, base = [], [], [], []
            for p in range(2):
                grav = ld(coef_ref, 3, p, sl)
                b_im = a_im + ld(coef_ref, 2, p, sl)
                b_rec = 1.0 / (a_re * a_re + b_im * b_im)
                inv.append((a_re * b_rec, -b_im * b_rec))
                det_re = a_re * a_re - b_im * a_im + grav * grav
                det_im = a_re * a_im + b_im * a_re
                det_rec = 1.0 / (det_re * det_re + det_im * det_im)
                dv = (det_re * det_rec, -det_im * det_rec)
                dinv.append(dv)
                lift.append(cmul(a_re, a_im, dv[0], dv[1]))
                base.append(cmul(ld(spec_ref, 6, p, sl), ld(spec_ref, 7, p, sl), dv[0], dv[1]))
            prep.append((inv, dinv, lift, base))
        state = [None] * len(lanes_work)
        for sweep in range(SWEEPS):
            for n, ((a_re, a_im, _, _), sl) in enumerate(lanes_work):
                inv, dinv, lift, base = prep[n]
                if sweep > 0:
                    zr, zi, dr, di, _, _ = state[n]
                    nzr, nzi, ndr, ndi = near(zr, sl), near(zi, sl), near(dr, sl), near(di, sl)
                zr, zi, dr, di, hr, hi = [], [], [], [], [], []
                for p in range(2):
                    if sweep == 0:
                        rzr, rzi = ld(spec_ref, 0, p, sl), ld(spec_ref, 1, p, sl)
                        rdr, rdi = ld(spec_ref, 2, p, sl), ld(spec_ref, 3, p, sl)
                    else:
                        rzr = ld(spec_ref, 0, p, sl) - ndr[p]
                        rzi = ld(spec_ref, 1, p, sl) - ndi[p]
                        rdr = ld(spec_ref, 2, p, sl) + nzr[p]
                        rdi = ld(spec_ref, 3, p, sl) + nzi[p]
                    z_re, z_im = cmul(rzr, rzi, inv[p][0], inv[p][1])
                    zr.append(z_re)
                    zi.append(z_im)
                    d_re, d_im = cmul(lift[p][0], lift[p][1], rdr, rdi)
                    dr.append(d_re + base[p][0])
                    di.append(d_im + base[p][1])
                    if sweep == SWEEPS - 1:
                        grav = ld(coef_ref, 3, p, sl)
                        b_im = a_im + ld(coef_ref, 2, p, sl)
                        h0r = ld(spec_ref, 4, p, sl)
                        h0i = ld(spec_ref, 5, p, sl)
                        nh_re = a_re * h0r - b_im * h0i - grav * rdr
                        nh_im = a_re * h0i + b_im * h0r - grav * rdi
                        h_re, h_im = cmul(nh_re, nh_im, dinv[p][0], dinv[p][1])
                        hr.append(h_re)
                        hi.append(h_im)
                state[n] = (zr, zi, dr, di, hr, hi)
        for n, ((_, _, w_re, w_im), sl) in enumerate(lanes_work):
            zr, zi, dr, di, hr, hi = state[n]
            for field, (f_re, f_im) in enumerate(((zr, zi), (dr, di), (hr, hi))):
                for p in range(2):
                    o_re, o_im = cmul(w_re, w_im, f_re[p], f_im[p])
                    out_ref[2 * field, p, sl, :] += o_re[:, :width]
                    out_ref[2 * field + 1, p, sl, :] += o_im[:, :width]
        return carry

    lax.fori_loop(0, npoles // INTERLEAVE, pole_step, 0)


def solve_poles(poles, wide, coef, width):
    _, parities, rows, _ = wide.shape
    return pl.pallas_call(
        pole_kernel,
        out_shape=jax.ShapeDtypeStruct((6, parities, rows, width), jnp.float32),
        in_specs=[
            pl.BlockSpec(memory_space=pltpu.SMEM),
            pl.BlockSpec(memory_space=pltpu.VMEM),
            pl.BlockSpec(memory_space=pltpu.VMEM),
        ],
        out_specs=pl.BlockSpec(memory_space=pltpu.VMEM),
    )(poles, wide, coef)


def cmul(are, aim, bre, bim):
    return (are * bre - aim * bim, are * bim + aim * bre)


def zero_extend(field):
    return jnp.pad(field, ((0, 0), (0, 0), (0, 0), (0, 0), (1, 1)))


def solve(spectra, coef, shifts, extend):
    e_lo, e_hi, rossby, gravity = coef
    count = spectra.shape[3]
    shift_re = shifts[:, 0][:, None, None, None]
    shift_im = shifts[:, 1][:, None, None, None]
    weight_re = shifts[:, 2][:, None, None, None]
    weight_im = shifts[:, 3][:, None, None, None]
    z0r, z0i = (spectra[0][None], spectra[1][None])
    d0r, d0i = (spectra[2][None], spectra[3][None])
    h0r, h0i = (spectra[4][None], spectra[5][None])
    b_re = shift_re + 0.0 * rossby[None]
    b_im = shift_im + rossby[None]
    b_mag = b_re * b_re + b_im * b_im
    inv_re, inv_im = (b_re / b_mag, -b_im / b_mag)
    det_re, det_im = cmul(b_re, b_im, shift_re, shift_im)
    det_re = det_re + gravity[None] * gravity[None]
    det_mag = det_re * det_re + det_im * det_im
    dinv_re, dinv_im = (det_re / det_mag, -det_im / det_mag)
    grav = gravity[None]
    hb_re, hb_im = cmul(b_re, b_im, h0r, h0i)
    zr, zi, dr, di, hr, hi = (z0r, z0i, d0r, d0i, h0r, h0i)
    for sweep in range(SWEEPS):
        if sweep == 0:
            rzr, rzi, rdr, rdi = (z0r, z0i, d0r, d0i)
        else:
            both = jnp.stack([zr, zi, dr, di], axis=0)
            ext = extend(both)
            lower = jnp.stack([ext[:, :, 1, :, 0:count], ext[:, :, 0, :, 1 : count + 1]], axis=2)
            upper = jnp.stack(
                [ext[:, :, 1, :, 1 : count + 1], ext[:, :, 0, :, 2 : count + 2]], axis=2
            )
            near = e_lo * lower + e_hi * upper
            rzr = z0r - coriolis_step * near[2]
            rzi = z0i - coriolis_step * near[3]
            rdr = d0r + coriolis_step * near[0]
            rdi = d0i + coriolis_step * near[1]
        zr, zi = cmul(rzr, rzi, inv_re, inv_im)
        nd_re, nd_im = cmul(shift_re, shift_im, rdr, rdi)
        nd_re = nd_re + grav * h0r
        nd_im = nd_im + grav * h0i
        nh_re = hb_re - grav * rdr
        nh_im = hb_im - grav * rdi
        dr, di = cmul(nd_re, nd_im, dinv_re, dinv_im)
        hr, hi = cmul(nh_re, nh_im, dinv_re, dinv_im)
    parts = []
    for field_re, field_im in ((zr, zi), (dr, di), (hr, hi)):
        out_re, out_im = cmul(weight_re, weight_im, field_re, field_im)
        parts.append(jnp.sum(out_re, axis=0))
        parts.append(jnp.sum(out_im, axis=0))
    return jnp.stack(parts, axis=0)


def lookup(pole_table, chosen):
    columns = jnp.arange(pole_table.shape[1], dtype=jnp.int32)
    onehot = (chosen[:, None] == columns[None, :]).astype(jnp.float32)
    return jnp.dot(onehot, jnp.transpose(pole_table), precision=lax.Precision.HIGHEST)


def shards(grid, legendre, wave_table, pole_table, pole_index):
    slots = legendre.shape[0]
    local_k = legendre.shape[3]
    lat_rows = grid.shape[2]
    wave_count = lax.axis_size("wave")
    half_count = wave_count // 2
    waves = grid.shape[1]
    comps = grid.shape[0]
    group = slots // GROUPS
    pole_count = lax.axis_size("pole")
    pole_pos = lax.axis_index("pole")
    rightward = [(i, i + 1) for i in range(pole_count - 1)]
    leftward = [(i + 1, i) for i in range(pole_count - 1)]
    own_waves = lax.dynamic_slice_in_dim(wave_table, lax.axis_index("wave") * slots, slots).astype(
        jnp.float32
    )
    coef_all = coefficients(own_waves, pole_pos * local_k, local_k, local_k * pole_count)
    coef_all = jnp.concatenate([coriolis_step * coef_all[:2], coef_all[2:]], axis=0)
    poles = jnp.take(pole_table, pole_index, axis=1)
    onehot = (wave_table[:, None] == jnp.arange(waves, dtype=jnp.int32)[None, :]).astype(jnp.float32)
    onehot = onehot.reshape(wave_count, GROUPS, group, waves)
    leg_blocks = legendre.reshape(slots, 2, half_count, lat_rows, local_k)
    outs = []
    for g in range(GROUPS):
        pick = onehot[:, g].reshape(wave_count * group, waves)
        columns = jnp.einsum("sm,cml->scl", pick, grid, precision=lax.Precision.HIGH)
        columns = columns.reshape(wave_count * group, comps * lat_rows)
        regrouped = lax.all_to_all(columns, "wave", split_axis=0, concat_axis=0, tiled=True)
        regrouped = regrouped.reshape(wave_count, group, comps, lat_rows)
        north = regrouped[:half_count]
        south = regrouped[half_count:]
        parts = jnp.stack([north + south, north - south], axis=0)
        high, low = split_high(parts)
        both = jnp.concatenate([high, low], axis=3)
        leg = leg_blocks[g * group : (g + 1) * group]
        products = jnp.einsum("mpwlk,pwmcl->cpmk", leg, both, preferred_element_type=jnp.float32)
        spectra = products[:comps] + products[comps:]
        left_halo = lax.ppermute(spectra[..., local_k - HALO :], "pole", rightward)
        right_halo = lax.ppermute(spectra[..., :HALO], "pole", leftward)
        gap = jnp.zeros(spectra.shape[:3] + (RING - local_k - 2 * HALO,), jnp.float32)
        wide = jnp.concatenate([spectra, right_halo, gap, left_halo], axis=3)
        coef = coef_all[:, :, g * group : (g + 1) * group]
        wide = jnp.concatenate([wide, coef[3][None] * wide[4:6]], axis=0)
        outs.append(solve_poles(poles, wide, coef, local_k))
    return jnp.concatenate(outs, axis=2)


def solution(mesh):
    in_specs = (P(None, None, "wave"), P("wave", None, None, "pole"), P(), P(), P())
    out_specs = P(None, None, "wave", "pole")
    return jax.shard_map(shards, mesh=mesh, in_specs=in_specs, out_specs=out_specs, check_vma=False)
```

```python
import jax
import jax.numpy as jnp
from jax import lax
from jax.experimental import pallas as pl
from jax.experimental.pallas import tpu as pltpu
from jax.sharding import PartitionSpec as P

SWEEPS = 8
HALO = 4
RING = 256
CHUNK = 8
GROUPS = 1
INTERLEAVE = 4


coriolis_step = 1.2
gravity_step = 0.0008


def split_high(values):
    upper_part = values.astype(jnp.bfloat16)
    kept = lax.optimization_barrier(upper_part)
    lower_part = (values - kept.astype(jnp.float32)).astype(jnp.bfloat16)
    return (upper_part, lower_part)


def coefficients(wavenum, base, width, total):
    lane = jnp.arange(RING, dtype=jnp.int32)
    index = jnp.where(lane >= RING - HALO, base + lane - RING, base + lane)
    inside = ((lane < width + HALO) | (lane >= RING - HALO)) & (index >= 0) & (index < total)
    index = jnp.clip(index, 0, total - 1).astype(jnp.float32)
    parity = jnp.arange(2, dtype=jnp.int32).astype(jnp.float32)
    order = (2.0 * index[None, :] + parity[:, None])[:, None, :]
    upper_inside = inside[None, None, :] & (order + 1.0 < 2.0 * total)
    wave = wavenum[None, :, None]
    degree = wave + order
    product = degree * (degree + 1.0)
    rossby = coriolis_step * wave / jnp.maximum(product, 2.0)
    gravity = gravity_step * jnp.sqrt(product)
    e_lo = jnp.sqrt(order * (2.0 * wave + order) / jnp.maximum(4.0 * degree * degree - 1.0, 1.0))
    after = order + 1.0
    upper_deg = degree + 1.0
    e_hi = jnp.sqrt(
        after * (2.0 * wave + after) / jnp.maximum(4.0 * upper_deg * upper_deg - 1.0, 1.0)
    )
    e_lo = jnp.where(inside[None, None, :], e_lo, 0.0)
    e_hi = jnp.where(upper_inside, e_hi, 0.0)
    return jnp.stack([e_lo, e_hi, rossby, gravity], axis=0)


def pole_kernel(poles_ref, spec_ref, coef_ref, out_ref):
    npoles = poles_ref.shape[1]
    rows = spec_ref.shape[2]
    lanes = spec_ref.shape[3]
    width = out_ref.shape[3]
    out_ref[...] = jnp.zeros(out_ref.shape, jnp.float32)

    def pole_step(step, carry):
        lanes_work = []
        for u in range(INTERLEAVE):
            q = step * INTERLEAVE + u
            scal = [poles_ref[i, q] for i in range(4)]
            for r0 in range(0, rows, CHUNK):
                lanes_work.append((scal, pl.ds(r0, CHUNK)))

        def ld(ref, i, p, sl):
            return ref[i, p, sl, :]

        def near(x, sl):
            n0 = ld(coef_ref, 0, 0, sl) * pltpu.roll(x[1], 1, 1) + ld(coef_ref, 1, 0, sl) * x[1]
            n1 = ld(coef_ref, 0, 1, sl) * x[0] + ld(coef_ref, 1, 1, sl) * pltpu.roll(
                x[0], lanes - 1, 1
            )
            return (n0, n1)

        prep = []
        for (a_re, a_im, _, _), sl in lanes_work:
            inv, dinv, lift, base = [], [], [], []
            for p in range(2):
                grav = ld(coef_ref, 3, p, sl)
                b_im = a_im + ld(coef_ref, 2, p, sl)
                b_rec = 1.0 / (a_re * a_re + b_im * b_im)
                inv.append((a_re * b_rec, -b_im * b_rec))
                det_re = a_re * a_re - b_im * a_im + grav * grav
                det_im = a_re * a_im + b_im * a_re
                det_rec = 1.0 / (det_re * det_re + det_im * det_im)
                dv = (det_re * det_rec, -det_im * det_rec)
                dinv.append(dv)
                lift.append(cmul(a_re, a_im, dv[0], dv[1]))
                base.append(cmul(ld(spec_ref, 6, p, sl), ld(spec_ref, 7, p, sl), dv[0], dv[1]))
            prep.append((inv, dinv, lift, base))
        state = [None] * len(lanes_work)
        for sweep in range(SWEEPS):
            for n, ((a_re, a_im, _, _), sl) in enumerate(lanes_work):
                inv, dinv, lift, base = prep[n]
                if sweep > 0:
                    zr, zi, dr, di, _, _ = state[n]
                    nzr, nzi, ndr, ndi = near(zr, sl), near(zi, sl), near(dr, sl), near(di, sl)
                zr, zi, dr, di, hr, hi = [], [], [], [], [], []
                for p in range(2):
                    if sweep == 0:
                        rzr, rzi = ld(spec_ref, 0, p, sl), ld(spec_ref, 1, p, sl)
                        rdr, rdi = ld(spec_ref, 2, p, sl), ld(spec_ref, 3, p, sl)
                    else:
                        rzr = ld(spec_ref, 0, p, sl) - ndr[p]
                        rzi = ld(spec_ref, 1, p, sl) - ndi[p]
                        rdr = ld(spec_ref, 2, p, sl) + nzr[p]
                        rdi = ld(spec_ref, 3, p, sl) + nzi[p]
                    z_re, z_im = cmul(rzr, rzi, inv[p][0], inv[p][1])
                    zr.append(z_re)
                    zi.append(z_im)
                    d_re, d_im = cmul(lift[p][0], lift[p][1], rdr, rdi)
                    dr.append(d_re + base[p][0])
                    di.append(d_im + base[p][1])
                    if sweep == SWEEPS - 1:
                        grav = ld(coef_ref, 3, p, sl)
                        b_im = a_im + ld(coef_ref, 2, p, sl)
                        h0r = ld(spec_ref, 4, p, sl)
                        h0i = ld(spec_ref, 5, p, sl)
                        nh_re = a_re * h0r - b_im * h0i - grav * rdr
                        nh_im = a_re * h0i + b_im * h0r - grav * rdi
                        h_re, h_im = cmul(nh_re, nh_im, dinv[p][0], dinv[p][1])
                        hr.append(h_re)
                        hi.append(h_im)
                state[n] = (zr, zi, dr, di, hr, hi)
        for n, ((_, _, w_re, w_im), sl) in enumerate(lanes_work):
            zr, zi, dr, di, hr, hi = state[n]
            for field, (f_re, f_im) in enumerate(((zr, zi), (dr, di), (hr, hi))):
                for p in range(2):
                    o_re, o_im = cmul(w_re, w_im, f_re[p], f_im[p])
                    out_ref[2 * field, p, sl, :] += o_re[:, :width]
                    out_ref[2 * field + 1, p, sl, :] += o_im[:, :width]
        return carry

    lax.fori_loop(0, npoles // INTERLEAVE, pole_step, 0)


def solve_poles(poles, wide, coef, width):
    _, parities, rows, _ = wide.shape
    return pl.pallas_call(
        pole_kernel,
        out_shape=jax.ShapeDtypeStruct((6, parities, rows, width), jnp.float32),
        in_specs=[
            pl.BlockSpec(memory_space=pltpu.SMEM),
            pl.BlockSpec(memory_space=pltpu.VMEM),
            pl.BlockSpec(memory_space=pltpu.VMEM),
        ],
        out_specs=pl.BlockSpec(memory_space=pltpu.VMEM),
    )(poles, wide, coef)


def cmul(are, aim, bre, bim):
    return (are * bre - aim * bim, are * bim + aim * bre)


def zero_extend(field):
    return jnp.pad(field, ((0, 0), (0, 0), (0, 0), (0, 0), (1, 1)))


def solve(spectra, coef, shifts, extend):
    e_lo, e_hi, rossby, gravity = coef
    count = spectra.shape[3]
    shift_re = shifts[:, 0][:, None, None, None]
    shift_im = shifts[:, 1][:, None, None, None]
    weight_re = shifts[:, 2][:, None, None, None]
    weight_im = shifts[:, 3][:, None, None, None]
    z0r, z0i = (spectra[0][None], spectra[1][None])
    d0r, d0i = (spectra[2][None], spectra[3][None])
    h0r, h0i = (spectra[4][None], spectra[5][None])
    b_re = shift_re + 0.0 * rossby[None]
    b_im = shift_im + rossby[None]
    b_mag = b_re * b_re + b_im * b_im
    inv_re, inv_im = (b_re / b_mag, -b_im / b_mag)
    det_re, det_im = cmul(b_re, b_im, shift_re, shift_im)
    det_re = det_re + gravity[None] * gravity[None]
    det_mag = det_re * det_re + det_im * det_im
    dinv_re, dinv_im = (det_re / det_mag, -det_im / det_mag)
    grav = gravity[None]
    hb_re, hb_im = cmul(b_re, b_im, h0r, h0i)
    zr, zi, dr, di, hr, hi = (z0r, z0i, d0r, d0i, h0r, h0i)
    for sweep in range(SWEEPS):
        if sweep == 0:
            rzr, rzi, rdr, rdi = (z0r, z0i, d0r, d0i)
        else:
            both = jnp.stack([zr, zi, dr, di], axis=0)
            ext = extend(both)
            lower = jnp.stack([ext[:, :, 1, :, 0:count], ext[:, :, 0, :, 1 : count + 1]], axis=2)
            upper = jnp.stack(
                [ext[:, :, 1, :, 1 : count + 1], ext[:, :, 0, :, 2 : count + 2]], axis=2
            )
            near = e_lo * lower + e_hi * upper
            rzr = z0r - coriolis_step * near[2]
            rzi = z0i - coriolis_step * near[3]
            rdr = d0r + coriolis_step * near[0]
            rdi = d0i + coriolis_step * near[1]
        zr, zi = cmul(rzr, rzi, inv_re, inv_im)
        nd_re, nd_im = cmul(shift_re, shift_im, rdr, rdi)
        nd_re = nd_re + grav * h0r
        nd_im = nd_im + grav * h0i
        nh_re = hb_re - grav * rdr
        nh_im = hb_im - grav * rdi
        dr, di = cmul(nd_re, nd_im, dinv_re, dinv_im)
        hr, hi = cmul(nh_re, nh_im, dinv_re, dinv_im)
    parts = []
    for field_re, field_im in ((zr, zi), (dr, di), (hr, hi)):
        out_re, out_im = cmul(weight_re, weight_im, field_re, field_im)
        parts.append(jnp.sum(out_re, axis=0))
        parts.append(jnp.sum(out_im, axis=0))
    return jnp.stack(parts, axis=0)


def lookup(pole_table, chosen):
    columns = jnp.arange(pole_table.shape[1], dtype=jnp.int32)
    onehot = (chosen[:, None] == columns[None, :]).astype(jnp.float32)
    return jnp.dot(onehot, jnp.transpose(pole_table), precision=lax.Precision.HIGHEST)


def shards(grid, legendre, wave_table, pole_table, pole_index):
    slots = legendre.shape[0]
    local_k = legendre.shape[3]
    lat_rows = grid.shape[2]
    wave_count = lax.axis_size("wave")
    half_count = wave_count // 2
    waves = grid.shape[1]
    comps = grid.shape[0]
    group = slots // GROUPS
    pole_count = lax.axis_size("pole")
    pole_pos = lax.axis_index("pole")
    rightward = [(i, (i + 1) % pole_count) for i in range(pole_count)]
    leftward = [((i + 1) % pole_count, i) for i in range(pole_count)]
    own_waves = lax.dynamic_slice_in_dim(wave_table, lax.axis_index("wave") * slots, slots).astype(
        jnp.float32
    )
    coef_all = coefficients(own_waves, pole_pos * local_k, local_k, local_k * pole_count)
    coef_all = jnp.concatenate([coriolis_step * coef_all[:2], coef_all[2:]], axis=0)
    poles = jnp.take(pole_table, pole_index, axis=1)
    onehot = (wave_table[:, None] == jnp.arange(waves, dtype=jnp.int32)[None, :]).astype(jnp.float32)
    onehot = onehot.reshape(wave_count, GROUPS, group, waves)
    leg_blocks = legendre.reshape(slots, 2, half_count, lat_rows, local_k)
    outs = []
    for g in range(GROUPS):
        pick = onehot[:, g].reshape(wave_count * group, waves)
        columns = jnp.einsum("sm,cml->scl", pick, grid, precision=lax.Precision.HIGHEST)
        columns = columns.reshape(wave_count * group, comps * lat_rows)
        regrouped = lax.all_to_all(columns, "wave", split_axis=0, concat_axis=0, tiled=True)
        regrouped = regrouped.reshape(wave_count, group, comps, lat_rows)
        north = regrouped[:half_count]
        south = regrouped[half_count:]
        parts = jnp.stack([north + south, north - south], axis=0)
        high, low = split_high(parts)
        both = jnp.concatenate([high, low], axis=3)
        leg = leg_blocks[g * group : (g + 1) * group]
        products = jnp.einsum("mpwlk,pwmcl->cpmk", leg, both, preferred_element_type=jnp.float32)
        spectra = products[:comps] + products[comps:]
        left_halo = lax.ppermute(spectra[..., local_k - HALO :], "pole", rightward)
        right_halo = lax.ppermute(spectra[..., :HALO], "pole", leftward)
        left_halo = jnp.where(pole_pos > 0, left_halo, 0.0)
        right_halo = jnp.where(pole_pos < pole_count - 1, right_halo, 0.0)
        gap = jnp.zeros(spectra.shape[:3] + (RING - local_k - 2 * HALO,), jnp.float32)
        wide = jnp.concatenate([spectra, right_halo, gap, left_halo], axis=3)
        coef = coef_all[:, :, g * group : (g + 1) * group]
        wide = jnp.concatenate([wide, coef[3][None] * wide[4:6]], axis=0)
        outs.append(solve_poles(poles, wide, coef, local_k))
    return jnp.concatenate(outs, axis=2)


def solution(mesh):
    in_specs = (P(None, None, "wave"), P("wave", None, None, "pole"), P(), P(), P())
    out_specs = P(None, None, "wave", "pole")
    return jax.shard_map(shards, mesh=mesh, in_specs=in_specs, out_specs=out_specs, check_vma=False)
```

```python
import jax
import jax.numpy as jnp
from jax import lax
from jax.experimental import pallas as pl
from jax.experimental.pallas import tpu as pltpu
from jax.sharding import PartitionSpec as P

SWEEPS = 8
HALO = 4
RING = 256
CHUNK = 8
GROUPS = 1
INTERLEAVE = 4


coriolis_step = 1.2
gravity_step = 0.0008


def split_high(values):
    upper_part = values.astype(jnp.bfloat16)
    kept = lax.optimization_barrier(upper_part)
    lower_part = (values - kept.astype(jnp.float32)).astype(jnp.bfloat16)
    return (upper_part, lower_part)


def coefficients(wavenum, base, width, total):
    lane = jnp.arange(RING, dtype=jnp.int32)
    index = jnp.where(lane >= RING - HALO, base + lane - RING, base + lane)
    inside = ((lane < width + HALO) | (lane >= RING - HALO)) & (index >= 0) & (index < total)
    index = jnp.clip(index, 0, total - 1).astype(jnp.float32)
    parity = jnp.arange(2, dtype=jnp.int32).astype(jnp.float32)
    order = (2.0 * index[None, :] + parity[:, None])[:, None, :]
    upper_inside = inside[None, None, :] & (order + 1.0 < 2.0 * total)
    wave = wavenum[None, :, None]
    degree = wave + order
    product = degree * (degree + 1.0)
    rossby = coriolis_step * wave / jnp.maximum(product, 2.0)
    gravity = gravity_step * jnp.sqrt(product)
    e_lo = jnp.sqrt(order * (2.0 * wave + order) / jnp.maximum(4.0 * degree * degree - 1.0, 1.0))
    after = order + 1.0
    upper_deg = degree + 1.0
    e_hi = jnp.sqrt(
        after * (2.0 * wave + after) / jnp.maximum(4.0 * upper_deg * upper_deg - 1.0, 1.0)
    )
    e_lo = jnp.where(inside[None, None, :], e_lo, 0.0)
    e_hi = jnp.where(upper_inside, e_hi, 0.0)
    return jnp.stack([e_lo, e_hi, rossby, gravity], axis=0)


def pole_kernel(poles_ref, spec_ref, coef_ref, out_ref):
    npoles = poles_ref.shape[1]
    rows = spec_ref.shape[2]
    lanes = spec_ref.shape[3]
    width = out_ref.shape[3]
    out_ref[...] = jnp.zeros(out_ref.shape, jnp.float32)

    def pole_step(step, carry):
        lanes_work = []
        for u in range(INTERLEAVE):
            q = step * INTERLEAVE + u
            scal = [poles_ref[i, q] for i in range(4)]
            for r0 in range(0, rows, CHUNK):
                lanes_work.append((scal, pl.ds(r0, CHUNK)))

        def ld(ref, i, p, sl):
            return ref[i, p, sl, :]

        def near(x, sl):
            n0 = ld(coef_ref, 0, 0, sl) * pltpu.roll(x[1], 1, 1) + ld(coef_ref, 1, 0, sl) * x[1]
            n1 = ld(coef_ref, 0, 1, sl) * x[0] + ld(coef_ref, 1, 1, sl) * pltpu.roll(
                x[0], lanes - 1, 1
            )
            return (n0, n1)

        prep = []
        for (a_re, a_im, _, _), sl in lanes_work:
            inv, dinv, lift, base = [], [], [], []
            for p in range(2):
                grav = ld(coef_ref, 3, p, sl)
                b_im = a_im + ld(coef_ref, 2, p, sl)
                b_rec = 1.0 / (a_re * a_re + b_im * b_im)
                inv.append((a_re * b_rec, -b_im * b_rec))
                det_re = a_re * a_re - b_im * a_im + grav * grav
                det_im = a_re * a_im + b_im * a_re
                det_rec = 1.0 / (det_re * det_re + det_im * det_im)
                dv = (det_re * det_rec, -det_im * det_rec)
                dinv.append(dv)
                lift.append(cmul(a_re, a_im, dv[0], dv[1]))
                base.append(cmul(ld(spec_ref, 6, p, sl), ld(spec_ref, 7, p, sl), dv[0], dv[1]))
            prep.append((inv, dinv, lift, base))
        state = [None] * len(lanes_work)
        for sweep in range(SWEEPS):
            for n, ((a_re, a_im, _, _), sl) in enumerate(lanes_work):
                inv, dinv, lift, base = prep[n]
                if sweep > 0:
                    zr, zi, dr, di, _, _ = state[n]
                    nzr, nzi, ndr, ndi = near(zr, sl), near(zi, sl), near(dr, sl), near(di, sl)
                zr, zi, dr, di, hr, hi = [], [], [], [], [], []
                for p in range(2):
                    if sweep == 0:
                        rzr, rzi = ld(spec_ref, 0, p, sl), ld(spec_ref, 1, p, sl)
                        rdr, rdi = ld(spec_ref, 2, p, sl), ld(spec_ref, 3, p, sl)
                    else:
                        rzr = ld(spec_ref, 0, p, sl) - ndr[p]
                        rzi = ld(spec_ref, 1, p, sl) - ndi[p]
                        rdr = ld(spec_ref, 2, p, sl) + nzr[p]
                        rdi = ld(spec_ref, 3, p, sl) + nzi[p]
                    z_re, z_im = cmul(rzr, rzi, inv[p][0], inv[p][1])
                    zr.append(z_re)
                    zi.append(z_im)
                    d_re, d_im = cmul(lift[p][0], lift[p][1], rdr, rdi)
                    dr.append(d_re + base[p][0])
                    di.append(d_im + base[p][1])
                    if sweep == SWEEPS - 1:
                        grav = ld(coef_ref, 3, p, sl)
                        b_im = a_im + ld(coef_ref, 2, p, sl)
                        h0r = ld(spec_ref, 4, p, sl)
                        h0i = ld(spec_ref, 5, p, sl)
                        nh_re = a_re * h0r - b_im * h0i - grav * rdr
                        nh_im = a_re * h0i + b_im * h0r - grav * rdi
                        h_re, h_im = cmul(nh_re, nh_im, dinv[p][0], dinv[p][1])
                        hr.append(h_re)
                        hi.append(h_im)
                state[n] = (zr, zi, dr, di, hr, hi)
        for n, ((_, _, w_re, w_im), sl) in enumerate(lanes_work):
            zr, zi, dr, di, hr, hi = state[n]
            for field, (f_re, f_im) in enumerate(((zr, zi), (dr, di), (hr, hi))):
                for p in range(2):
                    o_re, o_im = cmul(w_re, w_im, f_re[p], f_im[p])
                    out_ref[2 * field, p, sl, :] += o_re[:, :width]
                    out_ref[2 * field + 1, p, sl, :] += o_im[:, :width]
        return carry

    lax.fori_loop(0, npoles // INTERLEAVE, pole_step, 0)


def solve_poles(poles, wide, coef, width):
    _, parities, rows, _ = wide.shape
    return pl.pallas_call(
        pole_kernel,
        out_shape=jax.ShapeDtypeStruct((6, parities, rows, width), jnp.float32),
        in_specs=[
            pl.BlockSpec(memory_space=pltpu.SMEM),
            pl.BlockSpec(memory_space=pltpu.VMEM),
            pl.BlockSpec(memory_space=pltpu.VMEM),
        ],
        out_specs=pl.BlockSpec(memory_space=pltpu.VMEM),
    )(poles, wide, coef)


def cmul(are, aim, bre, bim):
    return (are * bre - aim * bim, are * bim + aim * bre)


def zero_extend(field):
    return jnp.pad(field, ((0, 0), (0, 0), (0, 0), (0, 0), (1, 1)))


def solve(spectra, coef, shifts, extend):
    e_lo, e_hi, rossby, gravity = coef
    count = spectra.shape[3]
    shift_re = shifts[:, 0][:, None, None, None]
    shift_im = shifts[:, 1][:, None, None, None]
    weight_re = shifts[:, 2][:, None, None, None]
    weight_im = shifts[:, 3][:, None, None, None]
    z0r, z0i = (spectra[0][None], spectra[1][None])
    d0r, d0i = (spectra[2][None], spectra[3][None])
    h0r, h0i = (spectra[4][None], spectra[5][None])
    b_re = shift_re + 0.0 * rossby[None]
    b_im = shift_im + rossby[None]
    b_mag = b_re * b_re + b_im * b_im
    inv_re, inv_im = (b_re / b_mag, -b_im / b_mag)
    det_re, det_im = cmul(b_re, b_im, shift_re, shift_im)
    det_re = det_re + gravity[None] * gravity[None]
    det_mag = det_re * det_re + det_im * det_im
    dinv_re, dinv_im = (det_re / det_mag, -det_im / det_mag)
    grav = gravity[None]
    hb_re, hb_im = cmul(b_re, b_im, h0r, h0i)
    zr, zi, dr, di, hr, hi = (z0r, z0i, d0r, d0i, h0r, h0i)
    for sweep in range(SWEEPS):
        if sweep == 0:
            rzr, rzi, rdr, rdi = (z0r, z0i, d0r, d0i)
        else:
            both = jnp.stack([zr, zi, dr, di], axis=0)
            ext = extend(both)
            lower = jnp.stack([ext[:, :, 1, :, 0:count], ext[:, :, 0, :, 1 : count + 1]], axis=2)
            upper = jnp.stack(
                [ext[:, :, 1, :, 1 : count + 1], ext[:, :, 0, :, 2 : count + 2]], axis=2
            )
            near = e_lo * lower + e_hi * upper
            rzr = z0r - coriolis_step * near[2]
            rzi = z0i - coriolis_step * near[3]
            rdr = d0r + coriolis_step * near[0]
            rdi = d0i + coriolis_step * near[1]
        zr, zi = cmul(rzr, rzi, inv_re, inv_im)
        nd_re, nd_im = cmul(shift_re, shift_im, rdr, rdi)
        nd_re = nd_re + grav * h0r
        nd_im = nd_im + grav * h0i
        nh_re = hb_re - grav * rdr
        nh_im = hb_im - grav * rdi
        dr, di = cmul(nd_re, nd_im, dinv_re, dinv_im)
        hr, hi = cmul(nh_re, nh_im, dinv_re, dinv_im)
    parts = []
    for field_re, field_im in ((zr, zi), (dr, di), (hr, hi)):
        out_re, out_im = cmul(weight_re, weight_im, field_re, field_im)
        parts.append(jnp.sum(out_re, axis=0))
        parts.append(jnp.sum(out_im, axis=0))
    return jnp.stack(parts, axis=0)


def lookup(pole_table, chosen):
    columns = jnp.arange(pole_table.shape[1], dtype=jnp.int32)
    onehot = (chosen[:, None] == columns[None, :]).astype(jnp.float32)
    return jnp.dot(onehot, jnp.transpose(pole_table), precision=lax.Precision.HIGHEST)


def shards(grid, legendre, wave_table, pole_table, pole_index):
    slots = legendre.shape[0]
    local_k = legendre.shape[3]
    lat_rows = grid.shape[2]
    wave_count = lax.axis_size("wave")
    half_count = wave_count // 2
    waves = grid.shape[1]
    comps = grid.shape[0]
    group = slots // GROUPS
    pole_count = lax.axis_size("pole")
    pole_pos = lax.axis_index("pole")
    rightward = [(i, (i + 1) % pole_count) for i in range(pole_count)]
    leftward = [((i + 1) % pole_count, i) for i in range(pole_count)]
    own_waves = lax.dynamic_slice_in_dim(wave_table, lax.axis_index("wave") * slots, slots).astype(
        jnp.float32
    )
    coef_all = coefficients(own_waves, pole_pos * local_k, local_k, local_k * pole_count)
    coef_all = jnp.concatenate([coriolis_step * coef_all[:2], coef_all[2:]], axis=0)
    poles = jnp.take(pole_table, pole_index, axis=1)
    onehot = (wave_table[:, None] == jnp.arange(waves, dtype=jnp.int32)[None, :]).astype(jnp.float32)
    onehot = onehot.reshape(wave_count, GROUPS, group, waves)
    leg_blocks = legendre.reshape(slots, 2, half_count, lat_rows, local_k)
    outs = []
    for g in range(GROUPS):
        pick = onehot[:, g].reshape(wave_count * group, waves)
        columns = jnp.einsum("sm,cml->scl", pick, grid, precision=lax.Precision.HIGHEST)
        columns = columns.reshape(wave_count * group, comps * lat_rows)
        regrouped = lax.all_to_all(columns, "wave", split_axis=0, concat_axis=0, tiled=True)
        regrouped = regrouped.reshape(wave_count, group, comps * lat_rows)
        north = regrouped[:half_count]
        south = regrouped[half_count:]
        parts = jnp.stack([north + south, north - south], axis=0)
        high, low = split_high(parts)
        both = jnp.concatenate([high, low], axis=3)
        both = both.reshape(2, half_count, group, 2 * comps, lat_rows)
        leg = leg_blocks[g * group : (g + 1) * group]
        products = jnp.einsum("mpwlk,pwmcl->cpmk", leg, both, preferred_element_type=jnp.float32)
        spectra = products[:comps] + products[comps:]
        left_halo = lax.ppermute(spectra[..., local_k - HALO :], "pole", rightward)
        right_halo = lax.ppermute(spectra[..., :HALO], "pole", leftward)
        left_halo = jnp.where(pole_pos > 0, left_halo, 0.0)
        right_halo = jnp.where(pole_pos < pole_count - 1, right_halo, 0.0)
        gap = jnp.zeros(spectra.shape[:3] + (RING - local_k - 2 * HALO,), jnp.float32)
        wide = jnp.concatenate([spectra, right_halo, gap, left_halo], axis=3)
        coef = coef_all[:, :, g * group : (g + 1) * group]
        wide = jnp.concatenate([wide, coef[3][None] * wide[4:6]], axis=0)
        outs.append(solve_poles(poles, wide, coef, local_k))
    return jnp.concatenate(outs, axis=2)


def solution(mesh):
    in_specs = (P(None, None, "wave"), P("wave", None, None, "pole"), P(), P(), P())
    out_specs = P(None, None, "wave", "pole")
    return jax.shard_map(shards, mesh=mesh, in_specs=in_specs, out_specs=out_specs, check_vma=False)
```

```python
import jax
import jax.numpy as jnp
from jax import lax
from jax.experimental import pallas as pl
from jax.experimental.pallas import tpu as pltpu
from jax.sharding import PartitionSpec as P

SWEEPS = 8
HALO = 4
RING = 256
CHUNK = 8
GROUPS = 1
INTERLEAVE = 4


coriolis_step = 1.2
gravity_step = 0.0008


def split_high(values):
    upper_part = values.astype(jnp.bfloat16)
    kept = lax.optimization_barrier(upper_part)
    lower_part = (values - kept.astype(jnp.float32)).astype(jnp.bfloat16)
    return (upper_part, lower_part)


def coefficients(wavenum, base, width, total):
    lane = jnp.arange(RING, dtype=jnp.int32)
    index = jnp.where(lane >= RING - HALO, base + lane - RING, base + lane)
    inside = ((lane < width + HALO) | (lane >= RING - HALO)) & (index >= 0) & (index < total)
    index = jnp.clip(index, 0, total - 1).astype(jnp.float32)
    parity = jnp.arange(2, dtype=jnp.int32).astype(jnp.float32)
    order = (2.0 * index[None, :] + parity[:, None])[:, None, :]
    upper_inside = inside[None, None, :] & (order + 1.0 < 2.0 * total)
    wave = wavenum[None, :, None]
    degree = wave + order
    product = degree * (degree + 1.0)
    rossby = coriolis_step * wave / jnp.maximum(product, 2.0)
    gravity = gravity_step * jnp.sqrt(product)
    e_lo = jnp.sqrt(order * (2.0 * wave + order) / jnp.maximum(4.0 * degree * degree - 1.0, 1.0))
    after = order + 1.0
    upper_deg = degree + 1.0
    e_hi = jnp.sqrt(
        after * (2.0 * wave + after) / jnp.maximum(4.0 * upper_deg * upper_deg - 1.0, 1.0)
    )
    e_lo = jnp.where(inside[None, None, :], e_lo, 0.0)
    e_hi = jnp.where(upper_inside, e_hi, 0.0)
    return jnp.stack([e_lo, e_hi, rossby, gravity], axis=0)


def pole_kernel(poles_ref, own_ref, right_ref, left_ref, coef_ref, out_ref, spec_ref):
    npoles = poles_ref.shape[1]
    rows = spec_ref.shape[2]
    lanes = spec_ref.shape[3]
    width = out_ref.shape[3]
    halo = right_ref.shape[3]
    comps = own_ref.shape[0]
    spec_ref[...] = jnp.zeros(spec_ref.shape, jnp.float32)
    spec_ref[:comps, :, :, :width] = own_ref[...]
    spec_ref[:comps, :, :, width : width + halo] = right_ref[...]
    spec_ref[:comps, :, :, lanes - halo :] = left_ref[...]
    for c in range(2):
        spec_ref[comps + c] = coef_ref[3] * spec_ref[comps - 2 + c]
    out_ref[...] = jnp.zeros(out_ref.shape, jnp.float32)

    def pole_step(step, carry):
        lanes_work = []
        for u in range(INTERLEAVE):
            q = step * INTERLEAVE + u
            scal = [poles_ref[i, q] for i in range(4)]
            for r0 in range(0, rows, CHUNK):
                lanes_work.append((scal, pl.ds(r0, CHUNK)))

        def ld(ref, i, p, sl):
            return ref[i, p, sl, :]

        def near(x, sl):
            n0 = ld(coef_ref, 0, 0, sl) * pltpu.roll(x[1], 1, 1) + ld(coef_ref, 1, 0, sl) * x[1]
            n1 = ld(coef_ref, 0, 1, sl) * x[0] + ld(coef_ref, 1, 1, sl) * pltpu.roll(
                x[0], lanes - 1, 1
            )
            return (n0, n1)

        prep = []
        for (a_re, a_im, _, _), sl in lanes_work:
            inv, dinv, lift, base = [], [], [], []
            for p in range(2):
                grav = ld(coef_ref, 3, p, sl)
                b_im = a_im + ld(coef_ref, 2, p, sl)
                b_rec = 1.0 / (a_re * a_re + b_im * b_im)
                inv.append((a_re * b_rec, -b_im * b_rec))
                det_re = a_re * a_re - b_im * a_im + grav * grav
                det_im = a_re * a_im + b_im * a_re
                det_rec = 1.0 / (det_re * det_re + det_im * det_im)
                dv = (det_re * det_rec, -det_im * det_rec)
                dinv.append(dv)
                lift.append(cmul(a_re, a_im, dv[0], dv[1]))
                base.append(cmul(ld(spec_ref, 6, p, sl), ld(spec_ref, 7, p, sl), dv[0], dv[1]))
            prep.append((inv, dinv, lift, base))
        state = [None] * len(lanes_work)
        for sweep in range(SWEEPS):
            for n, ((a_re, a_im, _, _), sl) in enumerate(lanes_work):
                inv, dinv, lift, base = prep[n]
                if sweep > 0:
                    zr, zi, dr, di, _, _ = state[n]
                    nzr, nzi, ndr, ndi = near(zr, sl), near(zi, sl), near(dr, sl), near(di, sl)
                zr, zi, dr, di, hr, hi = [], [], [], [], [], []
                for p in range(2):
                    if sweep == 0:
                        rzr, rzi = ld(spec_ref, 0, p, sl), ld(spec_ref, 1, p, sl)
                        rdr, rdi = ld(spec_ref, 2, p, sl), ld(spec_ref, 3, p, sl)
                    else:
                        rzr = ld(spec_ref, 0, p, sl) - ndr[p]
                        rzi = ld(spec_ref, 1, p, sl) - ndi[p]
                        rdr = ld(spec_ref, 2, p, sl) + nzr[p]
                        rdi = ld(spec_ref, 3, p, sl) + nzi[p]
                    z_re, z_im = cmul(rzr, rzi, inv[p][0], inv[p][1])
                    zr.append(z_re)
                    zi.append(z_im)
                    d_re, d_im = cmul(lift[p][0], lift[p][1], rdr, rdi)
                    dr.append(d_re + base[p][0])
                    di.append(d_im + base[p][1])
                    if sweep == SWEEPS - 1:
                        grav = ld(coef_ref, 3, p, sl)
                        b_im = a_im + ld(coef_ref, 2, p, sl)
                        h0r = ld(spec_ref, 4, p, sl)
                        h0i = ld(spec_ref, 5, p, sl)
                        nh_re = a_re * h0r - b_im * h0i - grav * rdr
                        nh_im = a_re * h0i + b_im * h0r - grav * rdi
                        h_re, h_im = cmul(nh_re, nh_im, dinv[p][0], dinv[p][1])
                        hr.append(h_re)
                        hi.append(h_im)
                state[n] = (zr, zi, dr, di, hr, hi)
        for n, ((_, _, w_re, w_im), sl) in enumerate(lanes_work):
            zr, zi, dr, di, hr, hi = state[n]
            for field, (f_re, f_im) in enumerate(((zr, zi), (dr, di), (hr, hi))):
                for p in range(2):
                    o_re, o_im = cmul(w_re, w_im, f_re[p], f_im[p])
                    out_ref[2 * field, p, sl, :] += o_re[:, :width]
                    out_ref[2 * field + 1, p, sl, :] += o_im[:, :width]
        return carry

    lax.fori_loop(0, npoles // INTERLEAVE, pole_step, 0)


def solve_poles(poles, own, right, left, coef):
    comps, parities, rows, width = own.shape
    lanes = coef.shape[3]
    return pl.pallas_call(
        pole_kernel,
        out_shape=jax.ShapeDtypeStruct((comps, parities, rows, width), jnp.float32),
        in_specs=[pl.BlockSpec(memory_space=pltpu.SMEM)]
        + [pl.BlockSpec(memory_space=pltpu.VMEM)] * 4,
        out_specs=pl.BlockSpec(memory_space=pltpu.VMEM),
        scratch_shapes=[pltpu.VMEM((comps + 2, parities, rows, lanes), jnp.float32)],
    )(poles, own, right, left, coef)


def cmul(are, aim, bre, bim):
    return (are * bre - aim * bim, are * bim + aim * bre)


def zero_extend(field):
    return jnp.pad(field, ((0, 0), (0, 0), (0, 0), (0, 0), (1, 1)))


def solve(spectra, coef, shifts, extend):
    e_lo, e_hi, rossby, gravity = coef
    count = spectra.shape[3]
    shift_re = shifts[:, 0][:, None, None, None]
    shift_im = shifts[:, 1][:, None, None, None]
    weight_re = shifts[:, 2][:, None, None, None]
    weight_im = shifts[:, 3][:, None, None, None]
    z0r, z0i = (spectra[0][None], spectra[1][None])
    d0r, d0i = (spectra[2][None], spectra[3][None])
    h0r, h0i = (spectra[4][None], spectra[5][None])
    b_re = shift_re + 0.0 * rossby[None]
    b_im = shift_im + rossby[None]
    b_mag = b_re * b_re + b_im * b_im
    inv_re, inv_im = (b_re / b_mag, -b_im / b_mag)
    det_re, det_im = cmul(b_re, b_im, shift_re, shift_im)
    det_re = det_re + gravity[None] * gravity[None]
    det_mag = det_re * det_re + det_im * det_im
    dinv_re, dinv_im = (det_re / det_mag, -det_im / det_mag)
    grav = gravity[None]
    hb_re, hb_im = cmul(b_re, b_im, h0r, h0i)
    zr, zi, dr, di, hr, hi = (z0r, z0i, d0r, d0i, h0r, h0i)
    for sweep in range(SWEEPS):
        if sweep == 0:
            rzr, rzi, rdr, rdi = (z0r, z0i, d0r, d0i)
        else:
            both = jnp.stack([zr, zi, dr, di], axis=0)
            ext = extend(both)
            lower = jnp.stack([ext[:, :, 1, :, 0:count], ext[:, :, 0, :, 1 : count + 1]], axis=2)
            upper = jnp.stack(
                [ext[:, :, 1, :, 1 : count + 1], ext[:, :, 0, :, 2 : count + 2]], axis=2
            )
            near = e_lo * lower + e_hi * upper
            rzr = z0r - coriolis_step * near[2]
            rzi = z0i - coriolis_step * near[3]
            rdr = d0r + coriolis_step * near[0]
            rdi = d0i + coriolis_step * near[1]
        zr, zi = cmul(rzr, rzi, inv_re, inv_im)
        nd_re, nd_im = cmul(shift_re, shift_im, rdr, rdi)
        nd_re = nd_re + grav * h0r
        nd_im = nd_im + grav * h0i
        nh_re = hb_re - grav * rdr
        nh_im = hb_im - grav * rdi
        dr, di = cmul(nd_re, nd_im, dinv_re, dinv_im)
        hr, hi = cmul(nh_re, nh_im, dinv_re, dinv_im)
    parts = []
    for field_re, field_im in ((zr, zi), (dr, di), (hr, hi)):
        out_re, out_im = cmul(weight_re, weight_im, field_re, field_im)
        parts.append(jnp.sum(out_re, axis=0))
        parts.append(jnp.sum(out_im, axis=0))
    return jnp.stack(parts, axis=0)


def lookup(pole_table, chosen):
    columns = jnp.arange(pole_table.shape[1], dtype=jnp.int32)
    onehot = (chosen[:, None] == columns[None, :]).astype(jnp.float32)
    return jnp.dot(onehot, jnp.transpose(pole_table), precision=lax.Precision.HIGHEST)


def shards(grid, legendre, wave_table, pole_table, pole_index):
    slots = legendre.shape[0]
    local_k = legendre.shape[3]
    lat_rows = grid.shape[2]
    wave_count = lax.axis_size("wave")
    half_count = wave_count // 2
    waves = grid.shape[1]
    comps = grid.shape[0]
    group = slots // GROUPS
    pole_count = lax.axis_size("pole")
    pole_pos = lax.axis_index("pole")
    rightward = [(i, (i + 1) % pole_count) for i in range(pole_count)]
    leftward = [((i + 1) % pole_count, i) for i in range(pole_count)]
    own_waves = lax.dynamic_slice_in_dim(wave_table, lax.axis_index("wave") * slots, slots).astype(
        jnp.float32
    )
    coef_all = coefficients(own_waves, pole_pos * local_k, local_k, local_k * pole_count)
    coef_all = jnp.concatenate([coriolis_step * coef_all[:2], coef_all[2:]], axis=0)
    poles = jnp.take(pole_table, pole_index, axis=1)
    onehot = (wave_table[:, None] == jnp.arange(waves, dtype=jnp.int32)[None, :]).astype(jnp.float32)
    onehot = onehot.reshape(wave_count, GROUPS, group, waves)
    leg_blocks = legendre.reshape(slots, 2, half_count, lat_rows, local_k)
    outs = []
    for g in range(GROUPS):
        pick = onehot[:, g].reshape(wave_count * group, waves)
        columns = jnp.einsum("sm,cml->scl", pick, grid, precision=lax.Precision.HIGHEST)
        columns = columns.reshape(wave_count * group, comps * lat_rows)
        regrouped = lax.all_to_all(columns, "wave", split_axis=0, concat_axis=0, tiled=True)
        regrouped = regrouped.reshape(wave_count, group, comps, lat_rows)
        north = regrouped[:half_count]
        south = regrouped[half_count:]
        parts = jnp.stack([north + south, north - south], axis=0)
        high, low = split_high(parts)
        both = jnp.concatenate([high, low], axis=3)
        leg = leg_blocks[g * group : (g + 1) * group]
        products = jnp.einsum("mpwlk,pwmcl->cpmk", leg, both, preferred_element_type=jnp.float32)
        spectra = products[:comps] + products[comps:]
        left_halo = lax.ppermute(spectra[..., local_k - HALO :], "pole", rightward)
        right_halo = lax.ppermute(spectra[..., :HALO], "pole", leftward)
        left_halo = jnp.where(pole_pos > 0, left_halo, 0.0)
        right_halo = jnp.where(pole_pos < pole_count - 1, right_halo, 0.0)
        coef = coef_all[:, :, g * group : (g + 1) * group]
        outs.append(solve_poles(poles, spectra, right_halo, left_halo, coef))
    return jnp.concatenate(outs, axis=2)


def solution(mesh):
    in_specs = (P(None, None, "wave"), P("wave", None, None, "pole"), P(), P(), P())
    out_specs = P(None, None, "wave", "pole")
    return jax.shard_map(shards, mesh=mesh, in_specs=in_specs, out_specs=out_specs, check_vma=False)
```

```python
import jax
import jax.numpy as jnp
from jax import lax
from jax.experimental import pallas as pl
from jax.experimental.pallas import tpu as pltpu
from jax.sharding import PartitionSpec as P

SWEEPS = 8
HALO = 4
RING = 256
CHUNK = 8
GROUPS = 1
INTERLEAVE = 4


coriolis_step = 1.2
gravity_step = 0.0008


def split_high(values):
    upper_part = values.astype(jnp.bfloat16)
    kept = lax.optimization_barrier(upper_part)
    lower_part = (values - kept.astype(jnp.float32)).astype(jnp.bfloat16)
    return (upper_part, lower_part)


def coefficients(wavenum, base, width, total):
    lane = jnp.arange(RING, dtype=jnp.int32)
    index = jnp.where(lane >= RING - HALO, base + lane - RING, base + lane)
    inside = ((lane < width + HALO) | (lane >= RING - HALO)) & (index >= 0) & (index < total)
    index = jnp.clip(index, 0, total - 1).astype(jnp.float32)
    parity = jnp.arange(2, dtype=jnp.int32).astype(jnp.float32)
    order = (2.0 * index[None, :] + parity[:, None])[:, None, :]
    upper_inside = inside[None, None, :] & (order + 1.0 < 2.0 * total)
    wave = wavenum[None, :, None]
    degree = wave + order
    product = degree * (degree + 1.0)
    rossby = coriolis_step * wave / jnp.maximum(product, 2.0)
    gravity = gravity_step * jnp.sqrt(product)
    e_lo = jnp.sqrt(order * (2.0 * wave + order) / jnp.maximum(4.0 * degree * degree - 1.0, 1.0))
    after = order + 1.0
    upper_deg = degree + 1.0
    e_hi = jnp.sqrt(
        after * (2.0 * wave + after) / jnp.maximum(4.0 * upper_deg * upper_deg - 1.0, 1.0)
    )
    e_lo = jnp.where(inside[None, None, :], e_lo, 0.0)
    e_hi = jnp.where(upper_inside, e_hi, 0.0)
    return jnp.stack([e_lo, e_hi, rossby, gravity], axis=0)


def pole_kernel(poles_ref, own_ref, edge_ref, coef_ref, out_ref):
    npoles = poles_ref.shape[1]
    rows = own_ref.shape[2]
    lanes = coef_ref.shape[3]
    spec_ref = (own_ref, edge_ref)
    width = out_ref.shape[3]
    out_ref[...] = jnp.zeros(out_ref.shape, jnp.float32)

    def pole_step(step, carry):
        lanes_work = []
        for u in range(INTERLEAVE):
            q = step * INTERLEAVE + u
            scal = [poles_ref[i, q] for i in range(4)]
            for r0 in range(0, rows, CHUNK):
                lanes_work.append((scal, pl.ds(r0, CHUNK)))

        def ld(ref, i, p, sl):
            if isinstance(ref, tuple):
                return jnp.concatenate([part[i, p, sl, :] for part in ref], axis=-1)
            return ref[i, p, sl, :]

        def near(x, sl):
            n0 = ld(coef_ref, 0, 0, sl) * pltpu.roll(x[1], 1, 1) + ld(coef_ref, 1, 0, sl) * x[1]
            n1 = ld(coef_ref, 0, 1, sl) * x[0] + ld(coef_ref, 1, 1, sl) * pltpu.roll(
                x[0], lanes - 1, 1
            )
            return (n0, n1)

        prep = []
        for (a_re, a_im, _, _), sl in lanes_work:
            inv, dinv, lift, base = [], [], [], []
            for p in range(2):
                grav = ld(coef_ref, 3, p, sl)
                b_im = a_im + ld(coef_ref, 2, p, sl)
                b_rec = 1.0 / (a_re * a_re + b_im * b_im)
                inv.append((a_re * b_rec, -b_im * b_rec))
                det_re = a_re * a_re - b_im * a_im + grav * grav
                det_im = a_re * a_im + b_im * a_re
                det_rec = 1.0 / (det_re * det_re + det_im * det_im)
                dv = (det_re * det_rec, -det_im * det_rec)
                dinv.append(dv)
                lift.append(cmul(a_re, a_im, dv[0], dv[1]))
                base.append(cmul(ld(spec_ref, 6, p, sl), ld(spec_ref, 7, p, sl), dv[0], dv[1]))
            prep.append((inv, dinv, lift, base))
        state = [None] * len(lanes_work)
        for sweep in range(SWEEPS):
            for n, ((a_re, a_im, _, _), sl) in enumerate(lanes_work):
                inv, dinv, lift, base = prep[n]
                if sweep > 0:
                    zr, zi, dr, di, _, _ = state[n]
                    nzr, nzi, ndr, ndi = near(zr, sl), near(zi, sl), near(dr, sl), near(di, sl)
                zr, zi, dr, di, hr, hi = [], [], [], [], [], []
                for p in range(2):
                    if sweep == 0:
                        rzr, rzi = ld(spec_ref, 0, p, sl), ld(spec_ref, 1, p, sl)
                        rdr, rdi = ld(spec_ref, 2, p, sl), ld(spec_ref, 3, p, sl)
                    else:
                        rzr = ld(spec_ref, 0, p, sl) - ndr[p]
                        rzi = ld(spec_ref, 1, p, sl) - ndi[p]
                        rdr = ld(spec_ref, 2, p, sl) + nzr[p]
                        rdi = ld(spec_ref, 3, p, sl) + nzi[p]
                    z_re, z_im = cmul(rzr, rzi, inv[p][0], inv[p][1])
                    zr.append(z_re)
                    zi.append(z_im)
                    d_re, d_im = cmul(lift[p][0], lift[p][1], rdr, rdi)
                    dr.append(d_re + base[p][0])
                    di.append(d_im + base[p][1])
                    if sweep == SWEEPS - 1:
                        grav = ld(coef_ref, 3, p, sl)
                        b_im = a_im + ld(coef_ref, 2, p, sl)
                        h0r = ld(spec_ref, 4, p, sl)
                        h0i = ld(spec_ref, 5, p, sl)
                        nh_re = a_re * h0r - b_im * h0i - grav * rdr
                        nh_im = a_re * h0i + b_im * h0r - grav * rdi
                        h_re, h_im = cmul(nh_re, nh_im, dinv[p][0], dinv[p][1])
                        hr.append(h_re)
                        hi.append(h_im)
                state[n] = (zr, zi, dr, di, hr, hi)
        for n, ((_, _, w_re, w_im), sl) in enumerate(lanes_work):
            zr, zi, dr, di, hr, hi = state[n]
            for field, (f_re, f_im) in enumerate(((zr, zi), (dr, di), (hr, hi))):
                for p in range(2):
                    o_re, o_im = cmul(w_re, w_im, f_re[p], f_im[p])
                    out_ref[2 * field, p, sl, :] += o_re[:, :width]
                    out_ref[2 * field + 1, p, sl, :] += o_im[:, :width]
        return carry

    lax.fori_loop(0, npoles // INTERLEAVE, pole_step, 0)


def solve_poles(poles, own, edge, coef, width):
    _, parities, rows, _ = own.shape
    return pl.pallas_call(
        pole_kernel,
        out_shape=jax.ShapeDtypeStruct((6, parities, rows, width), jnp.float32),
        in_specs=[pl.BlockSpec(memory_space=pltpu.SMEM)]
        + [pl.BlockSpec(memory_space=pltpu.VMEM)] * 3,
        out_specs=pl.BlockSpec(memory_space=pltpu.VMEM),
    )(poles, own, edge, coef)


def cmul(are, aim, bre, bim):
    return (are * bre - aim * bim, are * bim + aim * bre)


def zero_extend(field):
    return jnp.pad(field, ((0, 0), (0, 0), (0, 0), (0, 0), (1, 1)))


def solve(spectra, coef, shifts, extend):
    e_lo, e_hi, rossby, gravity = coef
    count = spectra.shape[3]
    shift_re = shifts[:, 0][:, None, None, None]
    shift_im = shifts[:, 1][:, None, None, None]
    weight_re = shifts[:, 2][:, None, None, None]
    weight_im = shifts[:, 3][:, None, None, None]
    z0r, z0i = (spectra[0][None], spectra[1][None])
    d0r, d0i = (spectra[2][None], spectra[3][None])
    h0r, h0i = (spectra[4][None], spectra[5][None])
    b_re = shift_re + 0.0 * rossby[None]
    b_im = shift_im + rossby[None]
    b_mag = b_re * b_re + b_im * b_im
    inv_re, inv_im = (b_re / b_mag, -b_im / b_mag)
    det_re, det_im = cmul(b_re, b_im, shift_re, shift_im)
    det_re = det_re + gravity[None] * gravity[None]
    det_mag = det_re * det_re + det_im * det_im
    dinv_re, dinv_im = (det_re / det_mag, -det_im / det_mag)
    grav = gravity[None]
    hb_re, hb_im = cmul(b_re, b_im, h0r, h0i)
    zr, zi, dr, di, hr, hi = (z0r, z0i, d0r, d0i, h0r, h0i)
    for sweep in range(SWEEPS):
        if sweep == 0:
            rzr, rzi, rdr, rdi = (z0r, z0i, d0r, d0i)
        else:
            both = jnp.stack([zr, zi, dr, di], axis=0)
            ext = extend(both)
            lower = jnp.stack([ext[:, :, 1, :, 0:count], ext[:, :, 0, :, 1 : count + 1]], axis=2)
            upper = jnp.stack(
                [ext[:, :, 1, :, 1 : count + 1], ext[:, :, 0, :, 2 : count + 2]], axis=2
            )
            near = e_lo * lower + e_hi * upper
            rzr = z0r - coriolis_step * near[2]
            rzi = z0i - coriolis_step * near[3]
            rdr = d0r + coriolis_step * near[0]
            rdi = d0i + coriolis_step * near[1]
        zr, zi = cmul(rzr, rzi, inv_re, inv_im)
        nd_re, nd_im = cmul(shift_re, shift_im, rdr, rdi)
        nd_re = nd_re + grav * h0r
        nd_im = nd_im + grav * h0i
        nh_re = hb_re - grav * rdr
        nh_im = hb_im - grav * rdi
        dr, di = cmul(nd_re, nd_im, dinv_re, dinv_im)
        hr, hi = cmul(nh_re, nh_im, dinv_re, dinv_im)
    parts = []
    for field_re, field_im in ((zr, zi), (dr, di), (hr, hi)):
        out_re, out_im = cmul(weight_re, weight_im, field_re, field_im)
        parts.append(jnp.sum(out_re, axis=0))
        parts.append(jnp.sum(out_im, axis=0))
    return jnp.stack(parts, axis=0)


def lookup(pole_table, chosen):
    columns = jnp.arange(pole_table.shape[1], dtype=jnp.int32)
    onehot = (chosen[:, None] == columns[None, :]).astype(jnp.float32)
    return jnp.dot(onehot, jnp.transpose(pole_table), precision=lax.Precision.HIGHEST)


def shards(grid, legendre, wave_table, pole_table, pole_index):
    slots = legendre.shape[0]
    local_k = legendre.shape[3]
    lat_rows = grid.shape[2]
    wave_count = lax.axis_size("wave")
    half_count = wave_count // 2
    waves = grid.shape[1]
    comps = grid.shape[0]
    group = slots // GROUPS
    pole_count = lax.axis_size("pole")
    pole_pos = lax.axis_index("pole")
    rightward = [(i, (i + 1) % pole_count) for i in range(pole_count)]
    leftward = [((i + 1) % pole_count, i) for i in range(pole_count)]
    own_waves = lax.dynamic_slice_in_dim(wave_table, lax.axis_index("wave") * slots, slots).astype(
        jnp.float32
    )
    coef_all = coefficients(own_waves, pole_pos * local_k, local_k, local_k * pole_count)
    coef_all = jnp.concatenate([coriolis_step * coef_all[:2], coef_all[2:]], axis=0)
    poles = jnp.take(pole_table, pole_index, axis=1)
    onehot = (wave_table[:, None] == jnp.arange(waves, dtype=jnp.int32)[None, :]).astype(jnp.float32)
    onehot = onehot.reshape(wave_count, GROUPS, group, waves)
    leg_blocks = legendre.reshape(slots, 2, half_count, lat_rows, local_k)
    outs = []
    for g in range(GROUPS):
        pick = onehot[:, g].reshape(wave_count * group, waves)
        columns = jnp.einsum("sm,cml->scl", pick, grid, precision=lax.Precision.HIGHEST)
        columns = columns.reshape(wave_count * group, comps * lat_rows)
        regrouped = lax.all_to_all(columns, "wave", split_axis=0, concat_axis=0, tiled=True)
        regrouped = regrouped.reshape(wave_count, group, comps, lat_rows)
        north = regrouped[:half_count]
        south = regrouped[half_count:]
        parts = jnp.stack([north + south, north - south], axis=0)
        high, low = split_high(parts)
        both = jnp.concatenate([high, low], axis=3)
        leg = leg_blocks[g * group : (g + 1) * group]
        products = jnp.einsum("mpwlk,pwmcl->cpmk", leg, both, preferred_element_type=jnp.float32)
        spectra = products[:comps] + products[comps:]
        left_halo = lax.ppermute(spectra[..., local_k - HALO :], "pole", rightward)
        right_halo = lax.ppermute(spectra[..., :HALO], "pole", leftward)
        left_halo = jnp.where(pole_pos > 0, left_halo, 0.0)
        right_halo = jnp.where(pole_pos < pole_count - 1, right_halo, 0.0)
        coef = coef_all[:, :, g * group : (g + 1) * group]
        own = jnp.concatenate([spectra, coef[3][None, ..., :local_k] * spectra[4:6]], axis=0)
        gap = jnp.zeros(spectra.shape[:3] + (RING - local_k - 2 * HALO,), jnp.float32)
        edge = jnp.concatenate([right_halo, gap, left_halo], axis=3)
        edge = jnp.concatenate([edge, coef[3][None, ..., local_k:] * edge[4:6]], axis=0)
        outs.append(solve_poles(poles, own, edge, coef, local_k))
    return jnp.concatenate(outs, axis=2)


def solution(mesh):
    in_specs = (P(None, None, "wave"), P("wave", None, None, "pole"), P(), P(), P())
    out_specs = P(None, None, "wave", "pole")
    return jax.shard_map(shards, mesh=mesh, in_specs=in_specs, out_specs=out_specs, check_vma=False)
```

```python
import jax
import jax.numpy as jnp
from jax import lax
from jax.experimental import pallas as pl
from jax.experimental.pallas import tpu as pltpu
from jax.sharding import PartitionSpec as P

SWEEPS = 8
HALO = 4
RING = 256
CHUNK = 8
GROUPS = 1
INTERLEAVE = 4


coriolis_step = 1.2
gravity_step = 0.0008


def split_high(values):
    upper_part = values.astype(jnp.bfloat16)
    kept = lax.optimization_barrier(upper_part)
    lower_part = (values - kept.astype(jnp.float32)).astype(jnp.bfloat16)
    return (upper_part, lower_part)


def coefficients(wavenum, base, width, total):
    lane = jnp.arange(RING, dtype=jnp.int32)
    index = jnp.where(lane >= RING - HALO, base + lane - RING, base + lane)
    inside = ((lane < width + HALO) | (lane >= RING - HALO)) & (index >= 0) & (index < total)
    index = jnp.clip(index, 0, total - 1).astype(jnp.float32)
    parity = jnp.arange(2, dtype=jnp.int32).astype(jnp.float32)
    order = (2.0 * index[None, :] + parity[:, None])[:, None, :]
    upper_inside = inside[None, None, :] & (order + 1.0 < 2.0 * total)
    wave = wavenum[None, :, None]
    degree = wave + order
    product = degree * (degree + 1.0)
    rossby = coriolis_step * wave / jnp.maximum(product, 2.0)
    gravity = gravity_step * jnp.sqrt(product)
    e_lo = jnp.sqrt(order * (2.0 * wave + order) / jnp.maximum(4.0 * degree * degree - 1.0, 1.0))
    after = order + 1.0
    upper_deg = degree + 1.0
    e_hi = jnp.sqrt(
        after * (2.0 * wave + after) / jnp.maximum(4.0 * upper_deg * upper_deg - 1.0, 1.0)
    )
    e_lo = jnp.where(inside[None, None, :], e_lo, 0.0)
    e_hi = jnp.where(upper_inside, e_hi, 0.0)
    return jnp.stack([e_lo, e_hi, rossby, gravity], axis=0)


def pole_kernel(poles_ref, spec_ref, coef_ref, out_ref):
    npoles = poles_ref.shape[1]
    rows = spec_ref.shape[2]
    lanes = spec_ref.shape[3]
    width = out_ref.shape[3]
    out_ref[...] = jnp.zeros(out_ref.shape, jnp.float32)

    def pole_step(step, carry):
        lanes_work = []
        for u in range(INTERLEAVE):
            q = step * INTERLEAVE + u
            scal = [poles_ref[i, q] for i in range(4)]
            for r0 in range(0, rows, CHUNK):
                lanes_work.append((scal, pl.ds(r0, CHUNK)))

        def ld(ref, i, p, sl):
            return ref[i, p, sl, :]

        def near(x, sl):
            n0 = ld(coef_ref, 0, 0, sl) * pltpu.roll(x[1], 1, 1) + ld(coef_ref, 1, 0, sl) * x[1]
            n1 = ld(coef_ref, 0, 1, sl) * x[0] + ld(coef_ref, 1, 1, sl) * pltpu.roll(
                x[0], lanes - 1, 1
            )
            return (n0, n1)

        prep = []
        for (a_re, a_im, _, _), sl in lanes_work:
            inv, dinv, lift, base = [], [], [], []
            for p in range(2):
                grav = ld(coef_ref, 3, p, sl)
                b_im = a_im + ld(coef_ref, 2, p, sl)
                b_rec = 1.0 / (a_re * a_re + b_im * b_im)
                inv.append((a_re * b_rec, -b_im * b_rec))
                det_re = a_re * a_re - b_im * a_im + grav * grav
                det_im = a_re * a_im + b_im * a_re
                det_rec = 1.0 / (det_re * det_re + det_im * det_im)
                dv = (det_re * det_rec, -det_im * det_rec)
                dinv.append(dv)
                lift.append(cmul(a_re, a_im, dv[0], dv[1]))
                base.append(cmul(ld(spec_ref, 6, p, sl), ld(spec_ref, 7, p, sl), dv[0], dv[1]))
            prep.append((inv, dinv, lift, base))
        state = [None] * len(lanes_work)
        for sweep in range(SWEEPS):
            for n, ((a_re, a_im, _, _), sl) in enumerate(lanes_work):
                inv, dinv, lift, base = prep[n]
                if sweep > 0:
                    zr, zi, dr, di, _, _ = state[n]
                    nzr, nzi, ndr, ndi = near(zr, sl), near(zi, sl), near(dr, sl), near(di, sl)
                zr, zi, dr, di, hr, hi = [], [], [], [], [], []
                for p in range(2):
                    if sweep == 0:
                        rzr, rzi = ld(spec_ref, 0, p, sl), ld(spec_ref, 1, p, sl)
                        rdr, rdi = ld(spec_ref, 2, p, sl), ld(spec_ref, 3, p, sl)
                    else:
                        rzr = ld(spec_ref, 0, p, sl) - ndr[p]
                        rzi = ld(spec_ref, 1, p, sl) - ndi[p]
                        rdr = ld(spec_ref, 2, p, sl) + nzr[p]
                        rdi = ld(spec_ref, 3, p, sl) + nzi[p]
                    z_re, z_im = cmul(rzr, rzi, inv[p][0], inv[p][1])
                    zr.append(z_re)
                    zi.append(z_im)
                    d_re, d_im = cmul(lift[p][0], lift[p][1], rdr, rdi)
                    dr.append(d_re + base[p][0])
                    di.append(d_im + base[p][1])
                    if sweep == SWEEPS - 1:
                        grav = ld(coef_ref, 3, p, sl)
                        b_im = a_im + ld(coef_ref, 2, p, sl)
                        h0r = ld(spec_ref, 4, p, sl)
                        h0i = ld(spec_ref, 5, p, sl)
                        nh_re = a_re * h0r - b_im * h0i - grav * rdr
                        nh_im = a_re * h0i + b_im * h0r - grav * rdi
                        h_re, h_im = cmul(nh_re, nh_im, dinv[p][0], dinv[p][1])
                        hr.append(h_re)
                        hi.append(h_im)
                state[n] = (zr, zi, dr, di, hr, hi)
        for n, ((_, _, w_re, w_im), sl) in enumerate(lanes_work):
            zr, zi, dr, di, hr, hi = state[n]
            for field, (f_re, f_im) in enumerate(((zr, zi), (dr, di), (hr, hi))):
                for p in range(2):
                    o_re, o_im = cmul(w_re, w_im, f_re[p], f_im[p])
                    out_ref[2 * field, p, sl, :] += o_re[:, :width]
                    out_ref[2 * field + 1, p, sl, :] += o_im[:, :width]
        return carry

    lax.fori_loop(0, npoles // INTERLEAVE, pole_step, 0)


def solve_poles(poles, wide, coef, width):
    _, parities, rows, _ = wide.shape
    return pl.pallas_call(
        pole_kernel,
        out_shape=jax.ShapeDtypeStruct((6, parities, rows, width), jnp.float32),
        in_specs=[
            pl.BlockSpec(memory_space=pltpu.SMEM),
            pl.BlockSpec(memory_space=pltpu.VMEM),
            pl.BlockSpec(memory_space=pltpu.VMEM),
        ],
        out_specs=pl.BlockSpec(memory_space=pltpu.VMEM),
    )(poles, wide, coef)


def cmul(are, aim, bre, bim):
    return (are * bre - aim * bim, are * bim + aim * bre)


def zero_extend(field):
    return jnp.pad(field, ((0, 0), (0, 0), (0, 0), (0, 0), (1, 1)))


def solve(spectra, coef, shifts, extend):
    e_lo, e_hi, rossby, gravity = coef
    count = spectra.shape[3]
    shift_re = shifts[:, 0][:, None, None, None]
    shift_im = shifts[:, 1][:, None, None, None]
    weight_re = shifts[:, 2][:, None, None, None]
    weight_im = shifts[:, 3][:, None, None, None]
    z0r, z0i = (spectra[0][None], spectra[1][None])
    d0r, d0i = (spectra[2][None], spectra[3][None])
    h0r, h0i = (spectra[4][None], spectra[5][None])
    b_re = shift_re + 0.0 * rossby[None]
    b_im = shift_im + rossby[None]
    b_mag = b_re * b_re + b_im * b_im
    inv_re, inv_im = (b_re / b_mag, -b_im / b_mag)
    det_re, det_im = cmul(b_re, b_im, shift_re, shift_im)
    det_re = det_re + gravity[None] * gravity[None]
    det_mag = det_re * det_re + det_im * det_im
    dinv_re, dinv_im = (det_re / det_mag, -det_im / det_mag)
    grav = gravity[None]
    hb_re, hb_im = cmul(b_re, b_im, h0r, h0i)
    zr, zi, dr, di, hr, hi = (z0r, z0i, d0r, d0i, h0r, h0i)
    for sweep in range(SWEEPS):
        if sweep == 0:
            rzr, rzi, rdr, rdi = (z0r, z0i, d0r, d0i)
        else:
            both = jnp.stack([zr, zi, dr, di], axis=0)
            ext = extend(both)
            lower = jnp.stack([ext[:, :, 1, :, 0:count], ext[:, :, 0, :, 1 : count + 1]], axis=2)
            upper = jnp.stack(
                [ext[:, :, 1, :, 1 : count + 1], ext[:, :, 0, :, 2 : count + 2]], axis=2
            )
            near = e_lo * lower + e_hi * upper
            rzr = z0r - coriolis_step * near[2]
            rzi = z0i - coriolis_step * near[3]
            rdr = d0r + coriolis_step * near[0]
            rdi = d0i + coriolis_step * near[1]
        zr, zi = cmul(rzr, rzi, inv_re, inv_im)
        nd_re, nd_im = cmul(shift_re, shift_im, rdr, rdi)
        nd_re = nd_re + grav * h0r
        nd_im = nd_im + grav * h0i
        nh_re = hb_re - grav * rdr
        nh_im = hb_im - grav * rdi
        dr, di = cmul(nd_re, nd_im, dinv_re, dinv_im)
        hr, hi = cmul(nh_re, nh_im, dinv_re, dinv_im)
    parts = []
    for field_re, field_im in ((zr, zi), (dr, di), (hr, hi)):
        out_re, out_im = cmul(weight_re, weight_im, field_re, field_im)
        parts.append(jnp.sum(out_re, axis=0))
        parts.append(jnp.sum(out_im, axis=0))
    return jnp.stack(parts, axis=0)


def lookup(pole_table, chosen):
    columns = jnp.arange(pole_table.shape[1], dtype=jnp.int32)
    onehot = (chosen[:, None] == columns[None, :]).astype(jnp.float32)
    return jnp.dot(onehot, jnp.transpose(pole_table), precision=lax.Precision.HIGHEST)


def shards(grid, legendre, wave_table, pole_table, pole_index):
    slots = legendre.shape[0]
    local_k = legendre.shape[3]
    lat_rows = grid.shape[2]
    wave_count = lax.axis_size("wave")
    half_count = wave_count // 2
    waves = grid.shape[1]
    comps = grid.shape[0]
    group = slots // GROUPS
    pole_count = lax.axis_size("pole")
    pole_pos = lax.axis_index("pole")
    rightward = [(i, (i + 1) % pole_count) for i in range(pole_count)]
    leftward = [((i + 1) % pole_count, i) for i in range(pole_count)]
    own_waves = lax.dynamic_slice_in_dim(wave_table, lax.axis_index("wave") * slots, slots).astype(
        jnp.float32
    )
    coef_all = coefficients(own_waves, pole_pos * local_k, local_k, local_k * pole_count)
    coef_all = jnp.concatenate([coriolis_step * coef_all[:2], coef_all[2:]], axis=0)
    poles = jnp.take(pole_table, pole_index, axis=1)
    onehot = (wave_table[:, None] == jnp.arange(waves, dtype=jnp.int32)[None, :]).astype(jnp.float32)
    onehot = onehot.reshape(wave_count, GROUPS, group, waves)
    leg_blocks = legendre.reshape(slots, 2, half_count, lat_rows, local_k)
    outs = []
    for g in range(GROUPS):
        pick = onehot[:, g].reshape(wave_count * group, waves)
        columns = jnp.einsum("sm,cml->scl", pick, grid, precision=lax.Precision.HIGH)
        columns = columns.reshape(wave_count * group, comps * lat_rows)
        regrouped = lax.all_to_all(columns, "wave", split_axis=0, concat_axis=0, tiled=True)
        regrouped = regrouped.reshape(wave_count, group, comps, lat_rows)
        north = regrouped[:half_count]
        south = regrouped[half_count:]
        parts = jnp.stack([north + south, north - south], axis=0)
        high, low = split_high(parts)
        both = jnp.concatenate([high, low], axis=3)
        leg = leg_blocks[g * group : (g + 1) * group]
        products = jnp.einsum("mpwlk,pwmcl->cpmk", leg, both, preferred_element_type=jnp.float32)
        spectra = products[:comps] + products[comps:]
        left_halo = lax.ppermute(spectra[..., local_k - HALO :], "pole", rightward)
        right_halo = lax.ppermute(spectra[..., :HALO], "pole", leftward)
        left_halo = jnp.where(pole_pos > 0, left_halo, 0.0)
        right_halo = jnp.where(pole_pos < pole_count - 1, right_halo, 0.0)
        gap = jnp.zeros(spectra.shape[:3] + (RING - local_k - 2 * HALO,), jnp.float32)
        wide = jnp.concatenate([spectra, right_halo, gap, left_halo], axis=3)
        coef = coef_all[:, :, g * group : (g + 1) * group]
        wide = jnp.concatenate([wide, coef[3][None] * wide[4:6]], axis=0)
        outs.append(solve_poles(poles, wide, coef, local_k))
    return jnp.concatenate(outs, axis=2)


def solution(mesh):
    in_specs = (P(None, None, "wave"), P("wave", None, None, "pole"), P(), P(), P())
    out_specs = P(None, None, "wave", "pole")
    return jax.shard_map(shards, mesh=mesh, in_specs=in_specs, out_specs=out_specs, check_vma=False)
```

```python
import jax
import jax.numpy as jnp
from jax import lax
from jax.experimental import pallas as pl
from jax.experimental.pallas import tpu as pltpu
from jax.sharding import PartitionSpec as P

SWEEPS = 8
HALO = 4
RING = 256
CHUNK = 8
GROUPS = 1
INTERLEAVE = 4


coriolis_step = 1.2
gravity_step = 0.0008


def split_high(values):
    upper_part = values.astype(jnp.bfloat16)
    kept = lax.optimization_barrier(upper_part)
    lower_part = (values - kept.astype(jnp.float32)).astype(jnp.bfloat16)
    return (upper_part, lower_part)


def coefficients(wavenum, base, width, total):
    lane = jnp.arange(RING, dtype=jnp.int32)
    index = jnp.where(lane >= RING - HALO, base + lane - RING, base + lane)
    inside = ((lane < width + HALO) | (lane >= RING - HALO)) & (index >= 0) & (index < total)
    index = jnp.clip(index, 0, total - 1).astype(jnp.float32)
    parity = jnp.arange(2, dtype=jnp.int32).astype(jnp.float32)
    order = (2.0 * index[None, :] + parity[:, None])[:, None, :]
    upper_inside = inside[None, None, :] & (order + 1.0 < 2.0 * total)
    wave = wavenum[None, :, None]
    degree = wave + order
    product = degree * (degree + 1.0)
    rossby = coriolis_step * wave / jnp.maximum(product, 2.0)
    gravity = gravity_step * jnp.sqrt(product)
    e_lo = jnp.sqrt(order * (2.0 * wave + order) / jnp.maximum(4.0 * degree * degree - 1.0, 1.0))
    after = order + 1.0
    upper_deg = degree + 1.0
    e_hi = jnp.sqrt(
        after * (2.0 * wave + after) / jnp.maximum(4.0 * upper_deg * upper_deg - 1.0, 1.0)
    )
    e_lo = jnp.where(inside[None, None, :], e_lo, 0.0)
    e_hi = jnp.where(upper_inside, e_hi, 0.0)
    return jnp.stack([e_lo, e_hi, rossby, gravity], axis=0)


def pole_kernel(poles_ref, spec_ref, coef_ref, out_ref):
    npoles = poles_ref.shape[1]
    rows = spec_ref.shape[2]
    lanes = spec_ref.shape[3]
    width = out_ref.shape[3]
    out_ref[...] = jnp.zeros(out_ref.shape, jnp.float32)

    def pole_step(step, carry):
        lanes_work = []
        for u in range(INTERLEAVE):
            q = step * INTERLEAVE + u
            scal = [poles_ref[i, q] for i in range(4)]
            for r0 in range(0, rows, CHUNK):
                lanes_work.append((scal, pl.ds(r0, CHUNK)))

        def ld(ref, i, p, sl):
            return ref[i, p, sl, :]

        def near(x, sl):
            n0 = ld(coef_ref, 0, 0, sl) * pltpu.roll(x[1], 1, 1) + ld(coef_ref, 1, 0, sl) * x[1]
            n1 = ld(coef_ref, 0, 1, sl) * x[0] + ld(coef_ref, 1, 1, sl) * pltpu.roll(
                x[0], lanes - 1, 1
            )
            return (n0, n1)

        prep = []
        for (a_re, a_im, _, _), sl in lanes_work:
            inv, dinv, lift, base = [], [], [], []
            for p in range(2):
                grav = ld(coef_ref, 3, p, sl)
                b_im = a_im + ld(coef_ref, 2, p, sl)
                b_rec = 1.0 / (a_re * a_re + b_im * b_im)
                inv.append((a_re * b_rec, -b_im * b_rec))
                det_re = a_re * a_re - b_im * a_im + grav * grav
                det_im = a_re * a_im + b_im * a_re
                det_rec = 1.0 / (det_re * det_re + det_im * det_im)
                dv = (det_re * det_rec, -det_im * det_rec)
                dinv.append(dv)
                lift.append(cmul(a_re, a_im, dv[0], dv[1]))
                base.append(cmul(ld(spec_ref, 6, p, sl), ld(spec_ref, 7, p, sl), dv[0], dv[1]))
            prep.append((inv, dinv, lift, base))
        state = [None] * len(lanes_work)
        for sweep in range(SWEEPS):
            for n, ((a_re, a_im, _, _), sl) in enumerate(lanes_work):
                inv, dinv, lift, base = prep[n]
                if sweep > 0:
                    zr, zi, dr, di, _, _ = state[n]
                    nzr, nzi, ndr, ndi = near(zr, sl), near(zi, sl), near(dr, sl), near(di, sl)
                zr, zi, dr, di, hr, hi = [], [], [], [], [], []
                for p in range(2):
                    if sweep == 0:
                        rzr, rzi = ld(spec_ref, 0, p, sl), ld(spec_ref, 1, p, sl)
                        rdr, rdi = ld(spec_ref, 2, p, sl), ld(spec_ref, 3, p, sl)
                    else:
                        rzr = ld(spec_ref, 0, p, sl) - ndr[p]
                        rzi = ld(spec_ref, 1, p, sl) - ndi[p]
                        rdr = ld(spec_ref, 2, p, sl) + nzr[p]
                        rdi = ld(spec_ref, 3, p, sl) + nzi[p]
                    z_re, z_im = cmul(rzr, rzi, inv[p][0], inv[p][1])
                    zr.append(z_re)
                    zi.append(z_im)
                    d_re, d_im = cmul(lift[p][0], lift[p][1], rdr, rdi)
                    dr.append(d_re + base[p][0])
                    di.append(d_im + base[p][1])
                    if sweep == SWEEPS - 1:
                        grav = ld(coef_ref, 3, p, sl)
                        b_im = a_im + ld(coef_ref, 2, p, sl)
                        h0r = ld(spec_ref, 4, p, sl)
                        h0i = ld(spec_ref, 5, p, sl)
                        nh_re = a_re * h0r - b_im * h0i - grav * rdr
                        nh_im = a_re * h0i + b_im * h0r - grav * rdi
                        h_re, h_im = cmul(nh_re, nh_im, dinv[p][0], dinv[p][1])
                        hr.append(h_re)
                        hi.append(h_im)
                state[n] = (zr, zi, dr, di, hr, hi)
        for n, ((_, _, w_re, w_im), sl) in enumerate(lanes_work):
            zr, zi, dr, di, hr, hi = state[n]
            for field, (f_re, f_im) in enumerate(((zr, zi), (dr, di), (hr, hi))):
                for p in range(2):
                    o_re, o_im = cmul(w_re, w_im, f_re[p], f_im[p])
                    out_ref[2 * field, p, sl, :] += o_re[:, :width]
                    out_ref[2 * field + 1, p, sl, :] += o_im[:, :width]
        return carry

    lax.fori_loop(0, npoles // INTERLEAVE, pole_step, 0)


def solve_poles(poles, wide, coef, width):
    _, parities, rows, _ = wide.shape
    return pl.pallas_call(
        pole_kernel,
        out_shape=jax.ShapeDtypeStruct((6, parities, rows, width), jnp.float32),
        in_specs=[
            pl.BlockSpec(memory_space=pltpu.SMEM),
            pl.BlockSpec(memory_space=pltpu.VMEM),
            pl.BlockSpec(memory_space=pltpu.VMEM),
        ],
        out_specs=pl.BlockSpec(memory_space=pltpu.VMEM),
    )(poles, wide, coef)


def cmul(are, aim, bre, bim):
    return (are * bre - aim * bim, are * bim + aim * bre)


def zero_extend(field):
    return jnp.pad(field, ((0, 0), (0, 0), (0, 0), (0, 0), (1, 1)))


def solve(spectra, coef, shifts, extend):
    e_lo, e_hi, rossby, gravity = coef
    count = spectra.shape[3]
    shift_re = shifts[:, 0][:, None, None, None]
    shift_im = shifts[:, 1][:, None, None, None]
    weight_re = shifts[:, 2][:, None, None, None]
    weight_im = shifts[:, 3][:, None, None, None]
    z0r, z0i = (spectra[0][None], spectra[1][None])
    d0r, d0i = (spectra[2][None], spectra[3][None])
    h0r, h0i = (spectra[4][None], spectra[5][None])
    b_re = shift_re + 0.0 * rossby[None]
    b_im = shift_im + rossby[None]
    b_mag = b_re * b_re + b_im * b_im
    inv_re, inv_im = (b_re / b_mag, -b_im / b_mag)
    det_re, det_im = cmul(b_re, b_im, shift_re, shift_im)
    det_re = det_re + gravity[None] * gravity[None]
    det_mag = det_re * det_re + det_im * det_im
    dinv_re, dinv_im = (det_re / det_mag, -det_im / det_mag)
    grav = gravity[None]
    hb_re, hb_im = cmul(b_re, b_im, h0r, h0i)
    zr, zi, dr, di, hr, hi = (z0r, z0i, d0r, d0i, h0r, h0i)
    for sweep in range(SWEEPS):
        if sweep == 0:
            rzr, rzi, rdr, rdi = (z0r, z0i, d0r, d0i)
        else:
            both = jnp.stack([zr, zi, dr, di], axis=0)
            ext = extend(both)
            lower = jnp.stack([ext[:, :, 1, :, 0:count], ext[:, :, 0, :, 1 : count + 1]], axis=2)
            upper = jnp.stack(
                [ext[:, :, 1, :, 1 : count + 1], ext[:, :, 0, :, 2 : count + 2]], axis=2
            )
            near = e_lo * lower + e_hi * upper
            rzr = z0r - coriolis_step * near[2]
            rzi = z0i - coriolis_step * near[3]
            rdr = d0r + coriolis_step * near[0]
            rdi = d0i + coriolis_step * near[1]
        zr, zi = cmul(rzr, rzi, inv_re, inv_im)
        nd_re, nd_im = cmul(shift_re, shift_im, rdr, rdi)
        nd_re = nd_re + grav * h0r
        nd_im = nd_im + grav * h0i
        nh_re = hb_re - grav * rdr
        nh_im = hb_im - grav * rdi
        dr, di = cmul(nd_re, nd_im, dinv_re, dinv_im)
        hr, hi = cmul(nh_re, nh_im, dinv_re, dinv_im)
    parts = []
    for field_re, field_im in ((zr, zi), (dr, di), (hr, hi)):
        out_re, out_im = cmul(weight_re, weight_im, field_re, field_im)
        parts.append(jnp.sum(out_re, axis=0))
        parts.append(jnp.sum(out_im, axis=0))
    return jnp.stack(parts, axis=0)


def lookup(pole_table, chosen):
    columns = jnp.arange(pole_table.shape[1], dtype=jnp.int32)
    onehot = (chosen[:, None] == columns[None, :]).astype(jnp.float32)
    return jnp.dot(onehot, jnp.transpose(pole_table), precision=lax.Precision.HIGHEST)


def shards(grid, legendre, wave_table, pole_table, pole_index):
    slots = legendre.shape[0]
    local_k = legendre.shape[3]
    lat_rows = grid.shape[2]
    wave_count = lax.axis_size("wave")
    half_count = wave_count // 2
    waves = grid.shape[1]
    comps = grid.shape[0]
    group = slots // GROUPS
    pole_count = lax.axis_size("pole")
    pole_pos = lax.axis_index("pole")
    rightward = [(i, (i + 1) % pole_count) for i in range(pole_count)]
    leftward = [((i + 1) % pole_count, i) for i in range(pole_count)]
    own_waves = lax.dynamic_slice_in_dim(wave_table, lax.axis_index("wave") * slots, slots).astype(
        jnp.float32
    )
    coef_all = coefficients(own_waves, pole_pos * local_k, local_k, local_k * pole_count)
    coef_all = jnp.concatenate([coriolis_step * coef_all[:2], coef_all[2:]], axis=0)
    poles = jnp.take(pole_table, pole_index, axis=1)
    onehot = (wave_table[:, None] == jnp.arange(waves, dtype=jnp.int32)[None, :]).astype(jnp.float32)
    onehot = onehot.reshape(wave_count, GROUPS, group, waves)
    leg_blocks = legendre.reshape(slots, 2, half_count, lat_rows, local_k)
    outs = []
    for g in range(GROUPS):
        pick = onehot[:, g].reshape(wave_count * group, waves)
        columns = jnp.einsum("sm,cml->scl", pick, grid, precision=lax.Precision.HIGHEST)
        columns = columns.reshape(wave_count * group, comps * lat_rows)
        regrouped = lax.all_to_all(columns, "wave", split_axis=0, concat_axis=0, tiled=True)
        regrouped = regrouped.reshape(wave_count, group, comps, lat_rows)
        north = regrouped[:half_count]
        south = regrouped[half_count:]
        parts = jnp.stack([north + south, north - south], axis=0)
        high, low = split_high(parts)
        both = jnp.concatenate([high, low], axis=3)
        leg = leg_blocks[g * group : (g + 1) * group]
        products = jnp.einsum("mpwlk,pwmcl->cpmk", leg, both, preferred_element_type=jnp.float32)
        spectra = products[:comps] + products[comps:]
        edge_shape = spectra.shape[:3] + (HALO,)
        left_halo = lax.ppermute(
            spectra[..., local_k - HALO :].reshape(-1, 128), "pole", rightward
        ).reshape(edge_shape)
        right_halo = lax.ppermute(spectra[..., :HALO].reshape(-1, 128), "pole", leftward).reshape(
            edge_shape
        )
        left_halo = jnp.where(pole_pos > 0, left_halo, 0.0)
        right_halo = jnp.where(pole_pos < pole_count - 1, right_halo, 0.0)
        gap = jnp.zeros(spectra.shape[:3] + (RING - local_k - 2 * HALO,), jnp.float32)
        wide = jnp.concatenate([spectra, right_halo, gap, left_halo], axis=3)
        coef = coef_all[:, :, g * group : (g + 1) * group]
        wide = jnp.concatenate([wide, coef[3][None] * wide[4:6]], axis=0)
        outs.append(solve_poles(poles, wide, coef, local_k))
    return jnp.concatenate(outs, axis=2)


def solution(mesh):
    in_specs = (P(None, None, "wave"), P("wave", None, None, "pole"), P(), P(), P())
    out_specs = P(None, None, "wave", "pole")
    return jax.shard_map(shards, mesh=mesh, in_specs=in_specs, out_specs=out_specs, check_vma=False)
```
